32 devices in a mesh: az: 4 (over x, core), rad: 4 (over z), ax: 2 (over y).
Axes of the slice: x: 2, y: 2, z: 4, core: 2. Of those that a mesh axis runs over, the one named last changes fastest.
Arguments:
- flow_state: float32 [5, 2, 512, 1024], P(None, 'ax', 'az', 'rad'), may hold values from -6 to 6
- source: float32 [5, 2, 512, 1024], P(None, 'ax', 'az', 'rad'), may hold values from -6 to 6
- cell_az: float32 [2, 512, 1024], P('ax', 'az', 'rad'), may hold values from 0.5 to 2
- cell_rad: float32 [2, 512, 1024], P('ax', 'az', 'rad'), may hold values from 0.5 to 2
- visc_az: float32 [5, 1024], P(None, 'rad'), may hold values from 1 to 20000
- beta_az: float32 [5, 1024], P(None, 'rad'), may hold values from -0.6 to 0.6
- visc_rad: float32 [5, 1024], replicated, may hold values from 1 to 20000
- axial_diff: float32 [5, 1024], P(None, 'rad'), may hold values from 0.1 to 0.45
- mix_in: float32 [5, 5, 1024], P(None, None, 'rad'), may hold values from -1.2 to 1.2
- mix_mid: float32 [5, 5, 1024], P(None, None, 'rad'), may hold values from -1.2 to 1.2
- mix_out: float32 [5, 5, 1024], P(None, None, 'rad'), may hold values from -1.2 to 1.2
Outputs:
- update: float32 [5, 2, 512, 1024], P(None, 'ax', 'az', 'rad')
The draws below stay inside these ranges and needn't reach their ends.
All inputs are finite; a program needn't handle non-finite values.
Results may differ from the reference program's by a relative error of at most 0.00045.
Values sent between devices are 32-bit elements; how exact they have to be, the bound alone decides.
No kernel may reach another device: no remote copies, remote signals or barrier semaphores. Data moves between devices by JAX's collectives and lax.ppermute only.
A program may use at most 128 MiB of HBM per device.

```python
import math
import jax
import jax.numpy as jnp
from jax import lax

NVAR = 5
NAX = 2
NAZ = 512
NRAD = 1024


def draw_source(key, part):
    dims_all = (NVAR, NAX, NAZ, NRAD)
    return jnp.clip(jax.random.normal(key, dims_all, jnp.float32), -6.0, 6.0)


def draw_visc_rad(key, part):
    key_pick = jax.random.fold_in(key, 11)
    key_centre = jax.random.fold_in(key, 12)
    key_rough = jax.random.fold_in(key, 13)
    order = jax.random.permutation(key_pick, NVAR).astype(jnp.int32)
    centre_cell = jax.random.randint(key_centre, (NVAR, 1), 0, NRAD, dtype=jnp.int32)
    cells = jnp.arange(NRAD, dtype=jnp.int32)[None, :]
    offset = ((cells - centre_cell) % NRAD).astype(jnp.float32)
    smooth = 15000.0 + 5000.0 * jnp.cos(offset * (2.0 * math.pi / NRAD))
    slow = (order < 3)[:, None]
    rough = jnp.exp(jax.random.uniform(key_rough, (NVAR, NRAD), jnp.float32, 0.0, math.log(20000.0)))
    rough = jnp.clip(rough, 1.0, 20000.0)
    return jnp.where(slow, smooth, rough)


def block_scale(own_key, extent, pieces, low, top_value):
    loudness, own = 1.0, jax.random.fold_in(own_key, 6)
    for axis_at, shards_of in pieces:
        draws = jnp.exp(jax.random.uniform(jax.random.fold_in(own, axis_at), (shards_of,), jnp.float32, low / len(pieces), top_value / len(pieces)))
        loudness = loudness * jnp.repeat(draws, extent[axis_at] // shards_of).reshape([-1 if axis == axis_at else 1 for axis in range(len(extent))])
    return loudness


def bell_draw(stream_key, dims, spread, bound, pieces=(), kind=jnp.bfloat16):
    drawn = jax.random.normal(stream_key, dims, jnp.float32) * spread
    if len(pieces) > 0:
        drawn = block_scale(stream_key, dims, pieces, -0.22, 0.18) * drawn
    return jnp.clip(drawn, min=-bound, max=bound).astype(kind)


def setup_inputs(seed: int = 0) -> dict:
    keys = jax.random.split(jax.random.key(seed), 12)
    flow_state = bell_draw(keys[0], (NVAR, NAX, NAZ, NRAD), 1.0, 6.0, ((1, 2), (2, 4), (3, 4)), jnp.float32)
    source = draw_source(jax.random.fold_in(keys[11], 71), 0)
    cell_az = jnp.clip(jnp.exp(math.log(2.0) - 1.3862944 * jax.random.uniform(keys[2], (NAX, NAZ, NRAD), jnp.float32) ** block_scale(keys[2], (NAX, NAZ, NRAD), ((0, 2), (1, 4), (2, 4)), -0.2, 0.2)), 0.5, 2.0)
    cell_rad = jnp.clip(jnp.exp(math.log(2.0) - 1.3862944 * jax.random.uniform(keys[3], (NAX, NAZ, NRAD), jnp.float32) ** block_scale(keys[3], (NAX, NAZ, NRAD), ((0, 2), (1, 4), (2, 4)), -0.2, 0.2)), 0.5, 2.0)
    visc_az = jnp.clip(jnp.exp(math.log(20000.0) - 9.9034876 * jax.random.uniform(keys[4], (NVAR, NRAD), jnp.float32) ** block_scale(keys[4], (NVAR, NRAD), ((1, 4),), -0.2, 0.2)), 1.0, 20000.0)
    beta_az = jnp.clip(jax.random.uniform(keys[5], (NVAR, NRAD), jnp.float32, -0.6, 0.6) * block_scale(keys[5], (NVAR, NRAD), ((1, 4),), -0.4, 0.0), -0.6, 0.6)
    visc_rad = draw_visc_rad(jax.random.fold_in(keys[11], 71), 0)
    axial_diff = jnp.clip(jnp.exp(math.log(0.45) - 1.50407736 * jax.random.uniform(keys[7], (NVAR, NRAD), jnp.float32) ** block_scale(keys[7], (NVAR, NRAD), ((1, 4),), -0.2, 0.2)), 0.1, 0.45)
    mix_in = bell_draw(keys[8], (NVAR, NVAR, NRAD), 0.3, 1.2, ((2, 4),), jnp.float32)
    mix_mid = bell_draw(keys[9], (NVAR, NVAR, NRAD), 0.3, 1.2, ((2, 4),), jnp.float32)
    mix_out = bell_draw(keys[10], (NVAR, NVAR, NRAD), 0.3, 1.2, ((2, 4),), jnp.float32)
    return {"flow_state": flow_state, "source": source, "cell_az": cell_az, "cell_rad": cell_rad, "visc_az": visc_az, "beta_az": beta_az, "visc_rad": visc_rad, "axial_diff": axial_diff, "mix_in": mix_in, "mix_mid": mix_mid, "mix_out": mix_out}


def open_shift(values, offset, axis):
    length = values.shape[axis]
    if offset > 0:
        kept = lax.slice_in_dim(values, 0, length - offset, axis=axis)
        zero_shape = list(values.shape)
        zero_shape[axis] = offset
        return jnp.concatenate([jnp.zeros(zero_shape, values.dtype), kept], axis=axis)
    kept = lax.slice_in_dim(values, -offset, length, axis=axis)
    zero_shape = list(values.shape)
    zero_shape[axis] = -offset
    return jnp.concatenate([kept, jnp.zeros(zero_shape, values.dtype)], axis=axis)


def neighbour(values, offset, axis, periodic):
    if periodic:
        return jnp.roll(values, offset, axis)
    return open_shift(values, offset, axis)


def reduce_lines(lower, upper, target, axis, periodic):
    length = lower.shape[axis]
    stride = 1
    while stride < length:
        low_left = neighbour(lower, stride, axis, periodic)
        up_left = neighbour(upper, stride, axis, periodic)
        tar_left = neighbour(target, stride, axis, periodic)
        low_right = neighbour(lower, -stride, axis, periodic)
        up_right = neighbour(upper, -stride, axis, periodic)
        tar_right = neighbour(target, -stride, axis, periodic)
        pivots = 1.0 - lower * up_left - upper * low_right
        new_lower = -lower * low_left / pivots
        new_upper = -upper * up_right / pivots
        new_target = (target - lower * tar_left - upper * tar_right) / pivots
        lower, upper, target = new_lower, new_upper, new_target
        stride = stride * 2
    return target / (1.0 + lower + upper)


def mix(matrix, values):
    mixed_rows = []
    for out_var in range(values.shape[0]):
        summed = values[out_var]
        for in_var in range(values.shape[0]):
            summed = summed + matrix[out_var, in_var][None, None, :] * values[in_var]
        mixed_rows.append(summed)
    return jnp.stack(mixed_rows)


def reference(flow_state, source, cell_az, cell_rad, visc_az, beta_az, visc_rad, axial_diff, mix_in, mix_mid, mix_out):
    padded = jnp.pad(flow_state, ((0, 0), (1, 1), (0, 0), (0, 0)))
    explicit = source + axial_diff[:, None, None, :] * (padded[:, :-2] - 2.0 * flow_state + padded[:, 2:])
    section_one = mix(mix_in, explicit)
    coupling = visc_az[:, None, None, :] * cell_az[None]
    centre = 1.0 + 2.0 * coupling
    tilt = beta_az[:, None, None, :]
    lower = -coupling * (1.0 + tilt) / centre
    upper = -coupling * (1.0 - tilt) / centre
    section_two = reduce_lines(lower, upper, section_one / centre, 2, True)
    section_three = mix(mix_mid, section_two)
    coupling = visc_rad[:, None, None, :] * cell_rad[None]
    centre = 1.0 + 2.0 * coupling
    side = -coupling / centre
    section_four = reduce_lines(side, side, section_three / centre, 3, False)
    return mix(mix_out, section_four)
```

```python
import jax
import jax.numpy as jnp
from jax import lax
from jax.sharding import PartitionSpec as P


def with_halo(block, sides, width, periodic):
    for axis, dim in sides:
        count = lax.axis_size(axis)
        forward = [(i, i + 1) for i in range(count - 1)]
        if periodic:
            forward.append((count - 1, 0))
        backward = [(target, source) for source, target in forward]
        low = lax.ppermute(
            lax.slice_in_dim(block, block.shape[dim] - width, None, axis=dim), axis, forward
        )
        high = lax.ppermute(lax.slice_in_dim(block, 0, width, axis=dim), axis, backward)
        block = jnp.concatenate([low, block, high], axis=dim)
    return block


def shifted(values, offset, axis, periodic):
    if periodic:
        return jnp.roll(values, offset, axis)
    length = values.shape[axis]
    zero_shape = list(values.shape)
    zero_shape[axis] = abs(offset)
    zeros = jnp.zeros(zero_shape, values.dtype)
    if offset > 0:
        kept = lax.slice_in_dim(values, 0, length - offset, axis=axis)
        return jnp.concatenate([zeros, kept], axis=axis)
    kept = lax.slice_in_dim(values, -offset, length, axis=axis)
    return jnp.concatenate([kept, zeros], axis=axis)


def cyclic_reduce(lower, upper, rhs, axis, periodic, steps_below):
    stride = 1
    while stride < steps_below:
        ll, ul = shifted(lower, stride, axis, periodic), shifted(upper, stride, axis, periodic)
        lr, ur = shifted(lower, -stride, axis, periodic), shifted(upper, -stride, axis, periodic)
        inv = 1.0 / (1.0 - lower * ul - upper * lr)
        rhs = [
            (r - lower * shifted(r, stride, axis, periodic) - upper * shifted(r, -stride, axis, periodic)) * inv
            for r in rhs
        ]
        lower, upper = -lower * ll * inv, -upper * ur * inv
        stride = stride * 2
    return lower, upper, rhs


def row(values, index, axis):
    return lax.slice_in_dim(values, index, index + 1, axis=axis)


def solve_lines(lower, upper, target, axis, axis_name, periodic):
    length = lower.shape[axis]
    idx = lax.broadcasted_iota(jnp.int32, lower.shape, axis)
    edge = (idx == 0) | (idx == length - 1)
    second = idx == 1
    penult = idx == length - 2
    zero = jnp.zeros_like(lower)
    il = jnp.where(edge | second, zero, lower)
    iu = jnp.where(edge | penult, zero, upper)
    it = jnp.where(edge, zero, target)
    ia = jnp.where(second, lower, zero)
    ib = jnp.where(penult, upper, zero)
    _, _, (it, ia, ib) = cyclic_reduce(il, iu, [it, ia, ib], axis, False, length - 2)
    l0, u0, t0 = row(lower, 0, axis), row(upper, 0, axis), row(target, 0, axis)
    le, ue, te = (row(v, length - 1, axis) for v in (lower, upper, target))
    a1, b1, t1 = row(ia, 1, axis), row(ib, 1, axis), row(it, 1, axis)
    a2, b2, t2 = (row(v, length - 2, axis) for v in (ia, ib, it))
    inv_f = 1.0 / (1.0 - u0 * a1)
    inv_e = 1.0 / (1.0 - le * b2)
    red = jnp.stack(
        [
            jnp.concatenate([l0 * inv_f, -le * a2 * inv_e], axis=axis),
            jnp.concatenate([-u0 * b1 * inv_f, ue * inv_e], axis=axis),
            jnp.concatenate([(t0 - u0 * t1) * inv_f, (te - le * t2) * inv_e], axis=axis),
        ]
    )
    red = lax.all_gather(red, axis_name, axis=axis + 1, tiled=True)
    count = red.shape[axis + 1]
    rl, ru, (rt,) = cyclic_reduce(red[0], red[1], [red[2]], axis, periodic, count)
    ends = rt / (1.0 + rl + ru)
    mine = lax.dynamic_slice_in_dim(ends, 2 * lax.axis_index(axis_name), 2, axis)
    first, last = row(mine, 0, axis), row(mine, 1, axis)
    inner = it - ia * first - ib * last
    return jnp.where(idx == 0, first, jnp.where(idx == length - 1, last, inner))


def mix(matrix, values):
    mixed_rows = []
    for out_var in range(values.shape[0]):
        summed = values[out_var]
        for in_var in range(values.shape[0]):
            summed = summed + matrix[out_var, in_var][None, None, :] * values[in_var]
        mixed_rows.append(summed)
    return jnp.stack(mixed_rows)


def per_device(
    flow_state,
    source,
    cell_az,
    cell_rad,
    visc_az,
    beta_az,
    visc_rad,
    axial_diff,
    mix_in,
    mix_mid,
    mix_out,
):
    rad_cells = flow_state.shape[3]
    padded = with_halo(flow_state, (("ax", 1),), 1, False)
    explicit = source + axial_diff[:, None, None, :] * (
        padded[:, :-2] - 2.0 * flow_state + padded[:, 2:]
    )
    section_one = mix(mix_in, explicit)
    coupling = visc_az[:, None, None, :] * cell_az[None]
    centre = 1.0 + 2.0 * coupling
    tilt = beta_az[:, None, None, :]
    lower = -coupling * (1.0 + tilt) / centre
    upper = -coupling * (1.0 - tilt) / centre
    section_two = solve_lines(lower, upper, section_one / centre, 2, "az", True)
    section_three = mix(mix_mid, section_two)
    visc_local = lax.dynamic_slice_in_dim(visc_rad, lax.axis_index("rad") * rad_cells, rad_cells, 1)
    coupling = visc_local[:, None, None, :] * cell_rad[None]
    centre = 1.0 + 2.0 * coupling
    side = -coupling / centre
    section_four = solve_lines(side, side, section_three / centre, 3, "rad", False)
    return mix(mix_out, section_four)


def solution(mesh):
    in_specs = (
        P(None, "ax", "az", "rad"),
        P(None, "ax", "az", "rad"),
        P("ax", "az", "rad"),
        P("ax", "az", "rad"),
        P(None, "rad"),
        P(None, "rad"),
        P(),
        P(None, "rad"),
        P(None, None, "rad"),
        P(None, None, "rad"),
        P(None, None, "rad"),
    )
    out_specs = P(None, "ax", "az", "rad")
    return jax.shard_map(
        per_device, mesh=mesh, in_specs=in_specs, out_specs=out_specs, check_vma=False
    )
```

```python
import jax
import jax.numpy as jnp
from jax import lax
from jax.experimental import pallas as pl
from jax.experimental.pallas import tpu as pltpu
from jax.sharding import PartitionSpec as P
import functools


def with_halo(block, sides, width, periodic):
    for axis, dim in sides:
        count = lax.axis_size(axis)
        forward = [(i, i + 1) for i in range(count - 1)]
        if periodic:
            forward.append((count - 1, 0))
        backward = [(target, source) for source, target in forward]
        low = lax.ppermute(
            lax.slice_in_dim(block, block.shape[dim] - width, None, axis=dim), axis, forward
        )
        high = lax.ppermute(lax.slice_in_dim(block, 0, width, axis=dim), axis, backward)
        block = jnp.concatenate([low, block, high], axis=dim)
    return block


def shifted(values, offset, axis, periodic):
    if periodic:
        return jnp.roll(values, offset, axis)
    length = values.shape[axis]
    zero_shape = list(values.shape)
    zero_shape[axis] = abs(offset)
    zeros = jnp.zeros(zero_shape, values.dtype)
    if offset > 0:
        kept = lax.slice_in_dim(values, 0, length - offset, axis=axis)
        return jnp.concatenate([zeros, kept], axis=axis)
    kept = lax.slice_in_dim(values, -offset, length, axis=axis)
    return jnp.concatenate([kept, zeros], axis=axis)


def cyclic_reduce(lower, upper, rhs, axis, periodic, steps_below):
    stride = 1
    while stride < steps_below:
        ll, ul = shifted(lower, stride, axis, periodic), shifted(upper, stride, axis, periodic)
        lr, ur = shifted(lower, -stride, axis, periodic), shifted(upper, -stride, axis, periodic)
        inv = 1.0 / (1.0 - lower * ul - upper * lr)
        rhs = [
            (r - lower * shifted(r, stride, axis, periodic) - upper * shifted(r, -stride, axis, periodic)) * inv
            for r in rhs
        ]
        lower, upper = -lower * ll * inv, -upper * ur * inv
        stride = stride * 2
    return lower, upper, rhs


def local_kernel(l_ref, u_ref, t_ref, ot_ref, oa_ref, ob_ref, *, axis):
    lower = l_ref[0, 0]
    upper = u_ref[0, 0]
    target = t_ref[0, 0]
    length = lower.shape[axis]
    idx = lax.broadcasted_iota(jnp.int32, lower.shape, axis)
    edge = (idx == 0) | (idx == length - 1)
    second = idx == 1
    penult = idx == length - 2
    zero = jnp.zeros_like(lower)
    il = jnp.where(edge | second, zero, lower)
    iu = jnp.where(edge | penult, zero, upper)
    rhs = [jnp.where(edge, zero, target), jnp.where(second, lower, zero), jnp.where(penult, upper, zero)]
    stride = 1
    while stride < length - 2:
        back = length - stride
        ll, ul = pltpu.roll(il, stride, axis), pltpu.roll(iu, stride, axis)
        lr, ur = pltpu.roll(il, back, axis), pltpu.roll(iu, back, axis)
        inv = 1.0 / (1.0 - il * ul - iu * lr)
        rhs = [(r - il * pltpu.roll(r, stride, axis) - iu * pltpu.roll(r, back, axis)) * inv for r in rhs]
        il, iu = -il * ll * inv, -iu * ur * inv
        stride = stride * 2
    ot_ref[0, 0] = rhs[0]
    oa_ref[0, 0] = rhs[1]
    ob_ref[0, 0] = rhs[2]


def local_reduce(lower, upper, target, axis):
    nv, nz, na, nr = lower.shape
    spec = pl.BlockSpec((1, 1, na, nr), lambda v, z: (v, z, 0, 0))
    out = jax.ShapeDtypeStruct(lower.shape, lower.dtype)
    return pl.pallas_call(
        functools.partial(local_kernel, axis=axis - 2),
        grid=(nv, nz),
        in_specs=[spec, spec, spec],
        out_specs=[spec, spec, spec],
        out_shape=[out, out, out],
    )(lower, upper, target)


def row(values, index, axis):
    return lax.slice_in_dim(values, index, index + 1, axis=axis)


def solve_lines(lower, upper, target, axis, axis_name, periodic):
    length = lower.shape[axis]
    idx = lax.broadcasted_iota(jnp.int32, lower.shape, axis)
    it, ia, ib = local_reduce(lower, upper, target, axis)
    l0, u0, t0 = row(lower, 0, axis), row(upper, 0, axis), row(target, 0, axis)
    le, ue, te = (row(v, length - 1, axis) for v in (lower, upper, target))
    a1, b1, t1 = row(ia, 1, axis), row(ib, 1, axis), row(it, 1, axis)
    a2, b2, t2 = (row(v, length - 2, axis) for v in (ia, ib, it))
    inv_f = 1.0 / (1.0 - u0 * a1)
    inv_e = 1.0 / (1.0 - le * b2)
    red = jnp.stack(
        [
            jnp.concatenate([l0 * inv_f, -le * a2 * inv_e], axis=axis),
            jnp.concatenate([-u0 * b1 * inv_f, ue * inv_e], axis=axis),
            jnp.concatenate([(t0 - u0 * t1) * inv_f, (te - le * t2) * inv_e], axis=axis),
        ]
    )
    red = lax.all_gather(red, axis_name, axis=axis + 1, tiled=True)
    count = red.shape[axis + 1]
    rl, ru, (rt,) = cyclic_reduce(red[0], red[1], [red[2]], axis, periodic, count)
    ends = rt / (1.0 + rl + ru)
    mine = lax.dynamic_slice_in_dim(ends, 2 * lax.axis_index(axis_name), 2, axis)
    first, last = row(mine, 0, axis), row(mine, 1, axis)
    inner = it - ia * first - ib * last
    return jnp.where(idx == 0, first, jnp.where(idx == length - 1, last, inner))


def mix(matrix, values):
    mixed_rows = []
    for out_var in range(values.shape[0]):
        summed = values[out_var]
        for in_var in range(values.shape[0]):
            summed = summed + matrix[out_var, in_var][None, None, :] * values[in_var]
        mixed_rows.append(summed)
    return jnp.stack(mixed_rows)


def per_device(
    flow_state,
    source,
    cell_az,
    cell_rad,
    visc_az,
    beta_az,
    visc_rad,
    axial_diff,
    mix_in,
    mix_mid,
    mix_out,
):
    rad_cells = flow_state.shape[3]
    padded = with_halo(flow_state, (("ax", 1),), 1, False)
    explicit = source + axial_diff[:, None, None, :] * (
        padded[:, :-2] - 2.0 * flow_state + padded[:, 2:]
    )
    section_one = mix(mix_in, explicit)
    coupling = visc_az[:, None, None, :] * cell_az[None]
    centre = 1.0 + 2.0 * coupling
    tilt = beta_az[:, None, None, :]
    lower = -coupling * (1.0 + tilt) / centre
    upper = -coupling * (1.0 - tilt) / centre
    section_two = solve_lines(lower, upper, section_one / centre, 2, "az", True)
    section_three = mix(mix_mid, section_two)
    visc_local = lax.dynamic_slice_in_dim(visc_rad, lax.axis_index("rad") * rad_cells, rad_cells, 1)
    coupling = visc_local[:, None, None, :] * cell_rad[None]
    centre = 1.0 + 2.0 * coupling
    side = -coupling / centre
    section_four = solve_lines(side, side, section_three / centre, 3, "rad", False)
    return mix(mix_out, section_four)


def solution(mesh):
    in_specs = (
        P(None, "ax", "az", "rad"),
        P(None, "ax", "az", "rad"),
        P("ax", "az", "rad"),
        P("ax", "az", "rad"),
        P(None, "rad"),
        P(None, "rad"),
        P(),
        P(None, "rad"),
        P(None, None, "rad"),
        P(None, None, "rad"),
        P(None, None, "rad"),
    )
    out_specs = P(None, "ax", "az", "rad")
    return jax.shard_map(
        per_device, mesh=mesh, in_specs=in_specs, out_specs=out_specs, check_vma=False
    )
```

```python
import jax
import jax.numpy as jnp
from jax import lax
from jax.experimental import pallas as pl
from jax.experimental.pallas import tpu as pltpu
from jax.sharding import PartitionSpec as P
import functools


def with_halo(block, sides, width, periodic):
    for axis, dim in sides:
        count = lax.axis_size(axis)
        forward = [(i, i + 1) for i in range(count - 1)]
        if periodic:
            forward.append((count - 1, 0))
        backward = [(target, source) for source, target in forward]
        low = lax.ppermute(
            lax.slice_in_dim(block, block.shape[dim] - width, None, axis=dim), axis, forward
        )
        high = lax.ppermute(lax.slice_in_dim(block, 0, width, axis=dim), axis, backward)
        block = jnp.concatenate([low, block, high], axis=dim)
    return block


def shifted(values, offset, axis, periodic):
    if periodic:
        return jnp.roll(values, offset, axis)
    length = values.shape[axis]
    zero_shape = list(values.shape)
    zero_shape[axis] = abs(offset)
    zeros = jnp.zeros(zero_shape, values.dtype)
    if offset > 0:
        kept = lax.slice_in_dim(values, 0, length - offset, axis=axis)
        return jnp.concatenate([zeros, kept], axis=axis)
    kept = lax.slice_in_dim(values, -offset, length, axis=axis)
    return jnp.concatenate([kept, zeros], axis=axis)


def cyclic_reduce(lower, upper, rhs, axis, periodic, steps_below):
    stride = 1
    while stride < steps_below:
        ll, ul = shifted(lower, stride, axis, periodic), shifted(upper, stride, axis, periodic)
        lr, ur = shifted(lower, -stride, axis, periodic), shifted(upper, -stride, axis, periodic)
        inv = 1.0 / (1.0 - lower * ul - upper * lr)
        rhs = [
            (r - lower * shifted(r, stride, axis, periodic) - upper * shifted(r, -stride, axis, periodic)) * inv
            for r in rhs
        ]
        lower, upper = -lower * ll * inv, -upper * ur * inv
        stride = stride * 2
    return lower, upper, rhs


def local_kernel(l_ref, u_ref, t_ref, ot_ref, oa_ref, ob_ref, *, axis):
    lower = l_ref[0, 0]
    upper = u_ref[0, 0]
    target = t_ref[0, 0]
    length = lower.shape[axis]
    idx = lax.broadcasted_iota(jnp.int32, lower.shape, axis)
    edge = (idx == 0) | (idx == length - 1)
    second = idx == 1
    penult = idx == length - 2
    zero = jnp.zeros_like(lower)
    il = jnp.where(edge | second, zero, lower)
    iu = jnp.where(edge | penult, zero, upper)
    rhs = [jnp.where(edge, zero, target), jnp.where(second, lower, zero), jnp.where(penult, upper, zero)]
    stride = 1
    while stride < length - 2:
        back = length - stride
        ll, ul = pltpu.roll(il, stride, axis), pltpu.roll(iu, stride, axis)
        lr, ur = pltpu.roll(il, back, axis), pltpu.roll(iu, back, axis)
        inv = 1.0 / (1.0 - il * ul - iu * lr)
        rhs = [(r - il * pltpu.roll(r, stride, axis) - iu * pltpu.roll(r, back, axis)) * inv for r in rhs]
        il, iu = -il * ll * inv, -iu * ur * inv
        stride = stride * 2
    ot_ref[0, 0] = rhs[0]
    oa_ref[0, 0] = rhs[1]
    ob_ref[0, 0] = rhs[2]


def local_reduce(lower, upper, target, axis):
    nv, nz, na, nr = lower.shape
    spec = pl.BlockSpec((1, 1, na, nr), lambda v, z: (v, z, 0, 0))
    out = jax.ShapeDtypeStruct(lower.shape, lower.dtype)
    return pl.pallas_call(
        functools.partial(local_kernel, axis=axis - 2),
        grid=(nv, nz),
        in_specs=[spec, spec, spec],
        out_specs=[spec, spec, spec],
        out_shape=[out, out, out],
    )(lower, upper, target)


def gathered(block, axis_name, dim):
    count = lax.axis_size(axis_name)
    received = [block]
    for offset in range(1, count):
        pairs = [((i + offset) % count, i) for i in range(count)]
        received.append(lax.ppermute(block, axis_name, pairs))
    doubled = jnp.concatenate(received + received, axis=dim)
    start = ((count - lax.axis_index(axis_name)) % count) * block.shape[dim]
    return lax.dynamic_slice_in_dim(doubled, start, count * block.shape[dim], dim)


def plane_halo(block, axis_name, dim):
    count = lax.axis_size(axis_name)
    if count != 2:
        return with_halo(block, ((axis_name, dim),), 1, False)
    swapped = lax.ppermute(block, axis_name, [(0, 1), (1, 0)])
    zero = jnp.zeros_like(swapped)
    first = lax.axis_index(axis_name) == 0
    low = jnp.where(first, zero, swapped)
    high = jnp.where(first, swapped, zero)
    return jnp.concatenate([low, block, high], axis=dim)


def row(values, index, axis):
    return lax.slice_in_dim(values, index, index + 1, axis=axis)


def solve_lines(lower, upper, target, axis, axis_name, periodic):
    length = lower.shape[axis]
    idx = lax.broadcasted_iota(jnp.int32, lower.shape, axis)
    it, ia, ib = local_reduce(lower, upper, target, axis)
    l0, u0, t0 = row(lower, 0, axis), row(upper, 0, axis), row(target, 0, axis)
    le, ue, te = (row(v, length - 1, axis) for v in (lower, upper, target))
    a1, b1, t1 = row(ia, 1, axis), row(ib, 1, axis), row(it, 1, axis)
    a2, b2, t2 = (row(v, length - 2, axis) for v in (ia, ib, it))
    inv_f = 1.0 / (1.0 - u0 * a1)
    inv_e = 1.0 / (1.0 - le * b2)
    red = jnp.stack(
        [
            jnp.concatenate([l0 * inv_f, -le * a2 * inv_e], axis=axis),
            jnp.concatenate([-u0 * b1 * inv_f, ue * inv_e], axis=axis),
            jnp.concatenate([(t0 - u0 * t1) * inv_f, (te - le * t2) * inv_e], axis=axis),
        ]
    )
    red = gathered(red, axis_name, axis + 1)
    count = red.shape[axis + 1]
    rl, ru, (rt,) = cyclic_reduce(red[0], red[1], [red[2]], axis, periodic, count)
    ends = rt / (1.0 + rl + ru)
    mine = lax.dynamic_slice_in_dim(ends, 2 * lax.axis_index(axis_name), 2, axis)
    first, last = row(mine, 0, axis), row(mine, 1, axis)
    inner = it - ia * first - ib * last
    return jnp.where(idx == 0, first, jnp.where(idx == length - 1, last, inner))


def mix(matrix, values):
    mixed_rows = []
    for out_var in range(values.shape[0]):
        summed = values[out_var]
        for in_var in range(values.shape[0]):
            summed = summed + matrix[out_var, in_var][None, None, :] * values[in_var]
        mixed_rows.append(summed)
    return jnp.stack(mixed_rows)


def per_device(
    flow_state,
    source,
    cell_az,
    cell_rad,
    visc_az,
    beta_az,
    visc_rad,
    axial_diff,
    mix_in,
    mix_mid,
    mix_out,
):
    rad_cells = flow_state.shape[3]
    padded = plane_halo(flow_state, "ax", 1)
    explicit = source + axial_diff[:, None, None, :] * (
        padded[:, :-2] - 2.0 * flow_state + padded[:, 2:]
    )
    section_one = mix(mix_in, explicit)
    coupling = visc_az[:, None, None, :] * cell_az[None]
    centre = 1.0 + 2.0 * coupling
    tilt = beta_az[:, None, None, :]
    lower = -coupling * (1.0 + tilt) / centre
    upper = -coupling * (1.0 - tilt) / centre
    section_two = solve_lines(lower, upper, section_one / centre, 2, "az", True)
    section_three = mix(mix_mid, section_two)
    visc_local = lax.dynamic_slice_in_dim(visc_rad, lax.axis_index("rad") * rad_cells, rad_cells, 1)
    coupling = visc_local[:, None, None, :] * cell_rad[None]
    centre = 1.0 + 2.0 * coupling
    side = -coupling / centre
    section_four = solve_lines(side, side, section_three / centre, 3, "rad", False)
    return mix(mix_out, section_four)


def solution(mesh):
    in_specs = (
        P(None, "ax", "az", "rad"),
        P(None, "ax", "az", "rad"),
        P("ax", "az", "rad"),
        P("ax", "az", "rad"),
        P(None, "rad"),
        P(None, "rad"),
        P(),
        P(None, "rad"),
        P(None, None, "rad"),
        P(None, None, "rad"),
        P(None, None, "rad"),
    )
    out_specs = P(None, "ax", "az", "rad")
    return jax.shard_map(
        per_device, mesh=mesh, in_specs=in_specs, out_specs=out_specs, check_vma=False
    )
```

```python
import jax
import jax.numpy as jnp
from jax import lax
from jax.experimental import pallas as pl
from jax.experimental.pallas import tpu as pltpu
from jax.sharding import PartitionSpec as P
import functools


def with_halo(block, sides, width, periodic):
    for axis, dim in sides:
        count = lax.axis_size(axis)
        forward = [(i, i + 1) for i in range(count - 1)]
        if periodic:
            forward.append((count - 1, 0))
        backward = [(target, source) for source, target in forward]
        low = lax.ppermute(
            lax.slice_in_dim(block, block.shape[dim] - width, None, axis=dim), axis, forward
        )
        high = lax.ppermute(lax.slice_in_dim(block, 0, width, axis=dim), axis, backward)
        block = jnp.concatenate([low, block, high], axis=dim)
    return block


def shifted(values, offset, axis, periodic):
    if periodic:
        return jnp.roll(values, offset, axis)
    length = values.shape[axis]
    zero_shape = list(values.shape)
    zero_shape[axis] = abs(offset)
    zeros = jnp.zeros(zero_shape, values.dtype)
    if offset > 0:
        kept = lax.slice_in_dim(values, 0, length - offset, axis=axis)
        return jnp.concatenate([zeros, kept], axis=axis)
    kept = lax.slice_in_dim(values, -offset, length, axis=axis)
    return jnp.concatenate([kept, zeros], axis=axis)


def cyclic_reduce(lower, upper, rhs, axis, periodic, steps_below):
    stride = 1
    while stride < steps_below:
        ll, ul = shifted(lower, stride, axis, periodic), shifted(upper, stride, axis, periodic)
        lr, ur = shifted(lower, -stride, axis, periodic), shifted(upper, -stride, axis, periodic)
        inv = 1.0 / (1.0 - lower * ul - upper * lr)
        rhs = [
            (r - lower * shifted(r, stride, axis, periodic) - upper * shifted(r, -stride, axis, periodic)) * inv
            for r in rhs
        ]
        lower, upper = -lower * ll * inv, -upper * ur * inv
        stride = stride * 2
    return lower, upper, rhs


def local_kernel(l_ref, u_ref, t_ref, ot_ref, oa_ref, ob_ref, *, axis):
    lower = l_ref[0, 0]
    upper = u_ref[0, 0]
    target = t_ref[0, 0]
    flip = axis == 1
    if flip:
        lower, upper, target, axis = lower.T, upper.T, target.T, 0
    length = lower.shape[axis]
    idx = lax.broadcasted_iota(jnp.int32, lower.shape, axis)
    edge = (idx == 0) | (idx == length - 1)
    second = idx == 1
    penult = idx == length - 2
    zero = jnp.zeros_like(lower)
    il = jnp.where(edge | second, zero, lower)
    iu = jnp.where(edge | penult, zero, upper)
    rhs = [jnp.where(edge, zero, target), jnp.where(second, lower, zero), jnp.where(penult, upper, zero)]
    stride = 1
    while stride < length - 2:
        back = length - stride
        ll, ul = pltpu.roll(il, stride, axis), pltpu.roll(iu, stride, axis)
        lr, ur = pltpu.roll(il, back, axis), pltpu.roll(iu, back, axis)
        inv = 1.0 / (1.0 - il * ul - iu * lr)
        rhs = [(r - il * pltpu.roll(r, stride, axis) - iu * pltpu.roll(r, back, axis)) * inv for r in rhs]
        il, iu = -il * ll * inv, -iu * ur * inv
        stride = stride * 2
    if flip:
        rhs = [r.T for r in rhs]
    ot_ref[0, 0] = rhs[0]
    oa_ref[0, 0] = rhs[1]
    ob_ref[0, 0] = rhs[2]


def local_reduce(lower, upper, target, axis):
    nv, nz, na, nr = lower.shape
    spec = pl.BlockSpec((1, 1, na, nr), lambda v, z: (v, z, 0, 0))
    out = jax.ShapeDtypeStruct(lower.shape, lower.dtype)
    return pl.pallas_call(
        functools.partial(local_kernel, axis=axis - 2),
        grid=(nv, nz),
        in_specs=[spec, spec, spec],
        out_specs=[spec, spec, spec],
        out_shape=[out, out, out],
    )(lower, upper, target)


def gathered(block, axis_name, dim):
    count = lax.axis_size(axis_name)
    received = [block]
    for offset in range(1, count):
        pairs = [((i + offset) % count, i) for i in range(count)]
        received.append(lax.ppermute(block, axis_name, pairs))
    doubled = jnp.concatenate(received + received, axis=dim)
    start = ((count - lax.axis_index(axis_name)) % count) * block.shape[dim]
    return lax.dynamic_slice_in_dim(doubled, start, count * block.shape[dim], dim)


def plane_halo(block, axis_name, dim):
    count = lax.axis_size(axis_name)
    if count != 2:
        return with_halo(block, ((axis_name, dim),), 1, False)
    swapped = lax.ppermute(block, axis_name, [(0, 1), (1, 0)])
    zero = jnp.zeros_like(swapped)
    first = lax.axis_index(axis_name) == 0
    low = jnp.where(first, zero, swapped)
    high = jnp.where(first, swapped, zero)
    return jnp.concatenate([low, block, high], axis=dim)


def row(values, index, axis):
    return lax.slice_in_dim(values, index, index + 1, axis=axis)


def solve_lines(lower, upper, target, axis, axis_name, periodic):
    length = lower.shape[axis]
    idx = lax.broadcasted_iota(jnp.int32, lower.shape, axis)
    it, ia, ib = local_reduce(lower, upper, target, axis)
    l0, u0, t0 = row(lower, 0, axis), row(upper, 0, axis), row(target, 0, axis)
    le, ue, te = (row(v, length - 1, axis) for v in (lower, upper, target))
    a1, b1, t1 = row(ia, 1, axis), row(ib, 1, axis), row(it, 1, axis)
    a2, b2, t2 = (row(v, length - 2, axis) for v in (ia, ib, it))
    inv_f = 1.0 / (1.0 - u0 * a1)
    inv_e = 1.0 / (1.0 - le * b2)
    red = jnp.stack(
        [
            jnp.concatenate([l0 * inv_f, -le * a2 * inv_e], axis=axis),
            jnp.concatenate([-u0 * b1 * inv_f, ue * inv_e], axis=axis),
            jnp.concatenate([(t0 - u0 * t1) * inv_f, (te - le * t2) * inv_e], axis=axis),
        ]
    )
    red = gathered(red, axis_name, axis + 1)
    count = red.shape[axis + 1]
    rl, ru, (rt,) = cyclic_reduce(red[0], red[1], [red[2]], axis, periodic, count)
    ends = rt / (1.0 + rl + ru)
    mine = lax.dynamic_slice_in_dim(ends, 2 * lax.axis_index(axis_name), 2, axis)
    first, last = row(mine, 0, axis), row(mine, 1, axis)
    inner = it - ia * first - ib * last
    return jnp.where(idx == 0, first, jnp.where(idx == length - 1, last, inner))


def mix(matrix, values):
    mixed_rows = []
    for out_var in range(values.shape[0]):
        summed = values[out_var]
        for in_var in range(values.shape[0]):
            summed = summed + matrix[out_var, in_var][None, None, :] * values[in_var]
        mixed_rows.append(summed)
    return jnp.stack(mixed_rows)


def per_device(
    flow_state,
    source,
    cell_az,
    cell_rad,
    visc_az,
    beta_az,
    visc_rad,
    axial_diff,
    mix_in,
    mix_mid,
    mix_out,
):
    rad_cells = flow_state.shape[3]
    padded = plane_halo(flow_state, "ax", 1)
    explicit = source + axial_diff[:, None, None, :] * (
        padded[:, :-2] - 2.0 * flow_state + padded[:, 2:]
    )
    section_one = mix(mix_in, explicit)
    coupling = visc_az[:, None, None, :] * cell_az[None]
    centre = 1.0 + 2.0 * coupling
    tilt = beta_az[:, None, None, :]
    lower = -coupling * (1.0 + tilt) / centre
    upper = -coupling * (1.0 - tilt) / centre
    section_two = solve_lines(lower, upper, section_one / centre, 2, "az", True)
    section_three = mix(mix_mid, section_two)
    visc_local = lax.dynamic_slice_in_dim(visc_rad, lax.axis_index("rad") * rad_cells, rad_cells, 1)
    coupling = visc_local[:, None, None, :] * cell_rad[None]
    centre = 1.0 + 2.0 * coupling
    side = -coupling / centre
    section_four = solve_lines(side, side, section_three / centre, 3, "rad", False)
    return mix(mix_out, section_four)


def solution(mesh):
    in_specs = (
        P(None, "ax", "az", "rad"),
        P(None, "ax", "az", "rad"),
        P("ax", "az", "rad"),
        P("ax", "az", "rad"),
        P(None, "rad"),
        P(None, "rad"),
        P(),
        P(None, "rad"),
        P(None, None, "rad"),
        P(None, None, "rad"),
        P(None, None, "rad"),
    )
    out_specs = P(None, "ax", "az", "rad")
    return jax.shard_map(
        per_device, mesh=mesh, in_specs=in_specs, out_specs=out_specs, check_vma=False
    )
```

```python
import jax
import jax.numpy as jnp
from jax import lax
from jax.experimental import pallas as pl
from jax.experimental.pallas import tpu as pltpu
from jax.sharding import PartitionSpec as P
import functools


def with_halo(block, sides, width, periodic):
    for axis, dim in sides:
        count = lax.axis_size(axis)
        forward = [(i, i + 1) for i in range(count - 1)]
        if periodic:
            forward.append((count - 1, 0))
        backward = [(target, source) for source, target in forward]
        low = lax.ppermute(
            lax.slice_in_dim(block, block.shape[dim] - width, None, axis=dim), axis, forward
        )
        high = lax.ppermute(lax.slice_in_dim(block, 0, width, axis=dim), axis, backward)
        block = jnp.concatenate([low, block, high], axis=dim)
    return block


def shifted(values, offset, axis, periodic):
    if periodic:
        return jnp.roll(values, offset, axis)
    length = values.shape[axis]
    zero_shape = list(values.shape)
    zero_shape[axis] = abs(offset)
    zeros = jnp.zeros(zero_shape, values.dtype)
    if offset > 0:
        kept = lax.slice_in_dim(values, 0, length - offset, axis=axis)
        return jnp.concatenate([zeros, kept], axis=axis)
    kept = lax.slice_in_dim(values, -offset, length, axis=axis)
    return jnp.concatenate([kept, zeros], axis=axis)


def cyclic_reduce(lower, upper, rhs, axis, periodic, steps_below):
    stride = 1
    while stride < steps_below:
        ll, ul = shifted(lower, stride, axis, periodic), shifted(upper, stride, axis, periodic)
        lr, ur = shifted(lower, -stride, axis, periodic), shifted(upper, -stride, axis, periodic)
        inv = 1.0 / (1.0 - lower * ul - upper * lr)
        rhs = [
            (r - lower * shifted(r, stride, axis, periodic) - upper * shifted(r, -stride, axis, periodic)) * inv
            for r in rhs
        ]
        lower, upper = -lower * ll * inv, -upper * ur * inv
        stride = stride * 2
    return lower, upper, rhs


def reduce_block(lower, upper, target, red_ref, index):
    length = lower.shape[0]
    idx = lax.broadcasted_iota(jnp.int32, lower.shape, 0)
    edge = (idx == 0) | (idx == length - 1)
    second = idx == 1
    penult = idx == length - 2
    zero = jnp.zeros_like(lower)
    il = jnp.where(edge | second, zero, lower)
    iu = jnp.where(edge | penult, zero, upper)
    rhs = [jnp.where(edge, zero, target), jnp.where(second, lower, zero), jnp.where(penult, upper, zero)]
    stride = 1
    while stride < length - 2:
        back = length - stride
        ll, ul = pltpu.roll(il, stride, 0), pltpu.roll(iu, stride, 0)
        lr, ur = pltpu.roll(il, back, 0), pltpu.roll(iu, back, 0)
        inv = 1.0 / (1.0 - il * ul - iu * lr)
        rhs = [(r - il * pltpu.roll(r, stride, 0) - iu * pltpu.roll(r, back, 0)) * inv for r in rhs]
        il, iu = -il * ll * inv, -iu * ur * inv
        stride = stride * 2
    it, ia, ib = rhs
    l0, u0, t0 = lower[0:1], upper[0:1], target[0:1]
    le, ue, te = lower[length - 1 :], upper[length - 1 :], target[length - 1 :]
    a1, b1, t1 = ia[1:2], ib[1:2], it[1:2]
    a2, b2, t2 = ia[length - 2 : length - 1], ib[length - 2 : length - 1], it[length - 2 : length - 1]
    inv_f = 1.0 / (1.0 - u0 * a1)
    inv_e = 1.0 / (1.0 - le * b2)
    rows = (
        l0 * inv_f,
        -le * a2 * inv_e,
        -u0 * b1 * inv_f,
        ue * inv_e,
        (t0 - u0 * t1) * inv_f,
        (te - le * t2) * inv_e,
    )
    for k, value in enumerate(rows):
        red_ref[index, 0, k : k + 1, :] = value
    return it, ia, ib


def az_kernel(fs_ref, nb_ref, src_ref, cell_ref, visc_ref, beta_ref, diff_ref, mix_ref, ot_ref, oa_ref, ob_ref, red_ref):
    count = fs_ref.shape[0]
    explicit = []
    for w in range(count):
        explicit.append(src_ref[w, 0] + diff_ref[w : w + 1, :] * (nb_ref[w, 0] - 2.0 * fs_ref[w, 0]))
    cell = cell_ref[0]
    for v in range(count):
        summed = explicit[v]
        for w in range(count):
            summed = summed + mix_ref[v, w : w + 1, :] * explicit[w]
        coupling = visc_ref[v : v + 1, :] * cell
        centre = 1.0 + 2.0 * coupling
        tilt = beta_ref[v : v + 1, :]
        lower = -coupling * (1.0 + tilt) / centre
        upper = -coupling * (1.0 - tilt) / centre
        it, ia, ib = reduce_block(lower, upper, summed / centre, red_ref, v)
        ot_ref[v, 0] = it
        oa_ref[v, 0] = ia
        ob_ref[v, 0] = ib


def rad_kernel(it_ref, ia_ref, ib_ref, ends_ref, mix_ref, cell_ref, visc_ref, ot_ref, oa_ref, ob_ref, red_ref):
    count = it_ref.shape[0]
    length = it_ref.shape[2]
    idx = lax.broadcasted_iota(jnp.int32, it_ref.shape[2:], 0)
    solved = []
    for w in range(count):
        first = ends_ref[w, 0, 0:1, :]
        last = ends_ref[w, 0, 1:2, :]
        inner = it_ref[w, 0] - ia_ref[w, 0] * first - ib_ref[w, 0] * last
        solved.append(jnp.where(idx == 0, first, jnp.where(idx == length - 1, last, inner)))
    cell = cell_ref[0]
    for v in range(count):
        summed = solved[v]
        for w in range(count):
            summed = summed + mix_ref[v, w : w + 1, :] * solved[w]
        coupling = visc_ref[v : v + 1, :] * cell
        centre = 1.0 + 2.0 * coupling
        side = (-coupling / centre).T
        it, ia, ib = reduce_block(side, side, (summed / centre).T, red_ref, v)
        ot_ref[v, 0] = it.T
        oa_ref[v, 0] = ia.T
        ob_ref[v, 0] = ib.T


def az_sweep(flow_state, nb, source, cell_az, visc_az, beta_az, axial_diff, mix_in):
    nv, nz, na, nr = flow_state.shape
    chunk = 128 if nr % 128 == 0 else nr
    big = pl.BlockSpec((nv, 1, na, chunk), lambda z, c: (0, z, 0, c))
    cell = pl.BlockSpec((1, na, chunk), lambda z, c: (z, 0, c))
    par = pl.BlockSpec((nv, chunk), lambda z, c: (0, c))
    mixs = pl.BlockSpec((nv, nv, chunk), lambda z, c: (0, 0, c))
    red = pl.BlockSpec((nv, 1, 6, chunk), lambda z, c: (0, z, 0, c))
    out = jax.ShapeDtypeStruct(flow_state.shape, flow_state.dtype)
    return pl.pallas_call(
        az_kernel,
        grid=(nz, nr // chunk),
        in_specs=[big, big, big, cell, par, par, par, mixs],
        out_specs=[big, big, big, red],
        out_shape=[out, out, out, jax.ShapeDtypeStruct((nv, nz, 6, nr), flow_state.dtype)],
    )(flow_state, nb, source, cell_az, visc_az, beta_az, axial_diff, mix_in)


def rad_sweep(it, ia, ib, ends, mix_mid, cell_rad, visc_local):
    nv, nz, na, nr = it.shape
    big = pl.BlockSpec((nv, 1, na, nr), lambda z: (0, z, 0, 0))
    endspec = pl.BlockSpec((nv, 1, 2, nr), lambda z: (0, z, 0, 0))
    mixs = pl.BlockSpec((nv, nv, nr), lambda z: (0, 0, 0))
    cell = pl.BlockSpec((1, na, nr), lambda z: (z, 0, 0))
    par = pl.BlockSpec((nv, nr), lambda z: (0, 0))
    red = pl.BlockSpec((nv, 1, 6, na), lambda z: (0, z, 0, 0))
    out = jax.ShapeDtypeStruct(it.shape, it.dtype)
    return pl.pallas_call(
        rad_kernel,
        grid=(nz,),
        in_specs=[big, big, big, endspec, mixs, cell, par],
        out_specs=[big, big, big, red],
        out_shape=[out, out, out, jax.ShapeDtypeStruct((nv, nz, 6, na), it.dtype)],
    )(it, ia, ib, ends, mix_mid, cell_rad, visc_local)


def gathered(block, axis_name, dim):
    count = lax.axis_size(axis_name)
    received = [block]
    for offset in range(1, count):
        pairs = [((i + offset) % count, i) for i in range(count)]
        received.append(lax.ppermute(block, axis_name, pairs))
    doubled = jnp.concatenate(received + received, axis=dim)
    start = ((count - lax.axis_index(axis_name)) % count) * block.shape[dim]
    return lax.dynamic_slice_in_dim(doubled, start, count * block.shape[dim], dim)


def reduced_solve(red, axis_name, periodic):
    stacked = jnp.stack([red[:, :, 0:2], red[:, :, 2:4], red[:, :, 4:6]])
    full = gathered(stacked, axis_name, 3)
    rl, ru, (rt,) = cyclic_reduce(full[0], full[1], [full[2]], 2, periodic, full.shape[3])
    ends = rt / (1.0 + rl + ru)
    return lax.dynamic_slice_in_dim(ends, 2 * lax.axis_index(axis_name), 2, 2)


def neighbour_planes(block, axis_name):
    count = lax.axis_size(axis_name)
    if count == 2:
        return lax.ppermute(block, axis_name, [(0, 1), (1, 0)])
    padded = with_halo(block, ((axis_name, 1),), 1, False)
    return padded[:, :-2] + padded[:, 2:]


def mix(matrix, values):
    mixed_rows = []
    for out_var in range(values.shape[0]):
        summed = values[out_var]
        for in_var in range(values.shape[0]):
            summed = summed + matrix[out_var, in_var][None, None, :] * values[in_var]
        mixed_rows.append(summed)
    return jnp.stack(mixed_rows)


def per_device(
    flow_state,
    source,
    cell_az,
    cell_rad,
    visc_az,
    beta_az,
    visc_rad,
    axial_diff,
    mix_in,
    mix_mid,
    mix_out,
):
    rad_cells = flow_state.shape[3]
    nb = neighbour_planes(flow_state, "ax")
    it, ia, ib, red = az_sweep(flow_state, nb, source, cell_az, visc_az, beta_az, axial_diff, mix_in)
    ends = reduced_solve(red, "az", True)
    visc_local = lax.dynamic_slice_in_dim(visc_rad, lax.axis_index("rad") * rad_cells, rad_cells, 1)
    it, ia, ib, red = rad_sweep(it, ia, ib, ends, mix_mid, cell_rad, visc_local)
    ends = reduced_solve(red, "rad", False)
    first = ends[:, :, 0, :, None]
    last = ends[:, :, 1, :, None]
    idx = lax.broadcasted_iota(jnp.int32, it.shape, 3)
    inner = it - ia * first - ib * last
    section_four = jnp.where(idx == 0, first, jnp.where(idx == rad_cells - 1, last, inner))
    return mix(mix_out, section_four)


def solution(mesh):
    in_specs = (
        P(None, "ax", "az", "rad"),
        P(None, "ax", "az", "rad"),
        P("ax", "az", "rad"),
        P("ax", "az", "rad"),
        P(None, "rad"),
        P(None, "rad"),
        P(),
        P(None, "rad"),
        P(None, None, "rad"),
        P(None, None, "rad"),
        P(None, None, "rad"),
    )
    out_specs = P(None, "ax", "az", "rad")
    return jax.shard_map(
        per_device, mesh=mesh, in_specs=in_specs, out_specs=out_specs, check_vma=False
    )
```

```python
import jax
import jax.numpy as jnp
from jax import lax
from jax.experimental import pallas as pl
from jax.experimental.pallas import tpu as pltpu
from jax.sharding import PartitionSpec as P
import functools


def with_halo(block, sides, width, periodic):
    for axis, dim in sides:
        count = lax.axis_size(axis)
        forward = [(i, i + 1) for i in range(count - 1)]
        if periodic:
            forward.append((count - 1, 0))
        backward = [(target, source) for source, target in forward]
        low = lax.ppermute(
            lax.slice_in_dim(block, block.shape[dim] - width, None, axis=dim), axis, forward
        )
        high = lax.ppermute(lax.slice_in_dim(block, 0, width, axis=dim), axis, backward)
        block = jnp.concatenate([low, block, high], axis=dim)
    return block


def shifted(values, offset, axis, periodic):
    if periodic:
        return jnp.roll(values, offset, axis)
    length = values.shape[axis]
    zero_shape = list(values.shape)
    zero_shape[axis] = abs(offset)
    zeros = jnp.zeros(zero_shape, values.dtype)
    if offset > 0:
        kept = lax.slice_in_dim(values, 0, length - offset, axis=axis)
        return jnp.concatenate([zeros, kept], axis=axis)
    kept = lax.slice_in_dim(values, -offset, length, axis=axis)
    return jnp.concatenate([kept, zeros], axis=axis)


def cyclic_reduce(lower, upper, rhs, axis, periodic, steps_below):
    stride = 1
    while stride < steps_below:
        ll, ul = shifted(lower, stride, axis, periodic), shifted(upper, stride, axis, periodic)
        lr, ur = shifted(lower, -stride, axis, periodic), shifted(upper, -stride, axis, periodic)
        inv = 1.0 / (1.0 - lower * ul - upper * lr)
        rhs = [
            (r - lower * shifted(r, stride, axis, periodic) - upper * shifted(r, -stride, axis, periodic)) * inv
            for r in rhs
        ]
        lower, upper = -lower * ll * inv, -upper * ur * inv
        stride = stride * 2
    return lower, upper, rhs


def reduce_block(lower, upper, target):
    length = lower.shape[0]
    idx = lax.broadcasted_iota(jnp.int32, lower.shape, 0)
    edge = (idx == 0) | (idx == length - 1)
    second = idx == 1
    penult = idx == length - 2
    zero = jnp.zeros_like(lower)
    il = jnp.where(edge | second, zero, lower)
    iu = jnp.where(edge | penult, zero, upper)
    rhs = [jnp.where(edge, zero, target), jnp.where(second, lower, zero), jnp.where(penult, upper, zero)]
    stride = 1
    while stride < length - 2:
        back = length - stride
        ll, ul = pltpu.roll(il, stride, 0), pltpu.roll(iu, stride, 0)
        lr, ur = pltpu.roll(il, back, 0), pltpu.roll(iu, back, 0)
        inv = 1.0 / (1.0 - il * ul - iu * lr)
        rhs = [(r - il * pltpu.roll(r, stride, 0) - iu * pltpu.roll(r, back, 0)) * inv for r in rhs]
        il, iu = -il * ll * inv, -iu * ur * inv
        stride = stride * 2
    it, ia, ib = rhs
    l0, u0, t0 = lower[0:1], upper[0:1], target[0:1]
    le, ue, te = lower[length - 1 :], upper[length - 1 :], target[length - 1 :]
    a1, b1, t1 = ia[1:2], ib[1:2], it[1:2]
    a2, b2, t2 = ia[length - 2 : length - 1], ib[length - 2 : length - 1], it[length - 2 : length - 1]
    inv_f = 1.0 / (1.0 - u0 * a1)
    inv_e = 1.0 / (1.0 - le * b2)
    rows = (
        (l0 * inv_f, -le * a2 * inv_e),
        (-u0 * b1 * inv_f, ue * inv_e),
        ((t0 - u0 * t1) * inv_f, (te - le * t2) * inv_e),
    )
    return it, ia, ib, rows


def store_rows(red_ref, v, rows):
    for q, pair in enumerate(rows):
        for i, value in enumerate(pair):
            red_ref[v, 0, q, i : i + 1, :] = value


def reduced_ends(red_ref, v):
    lower, upper, target = red_ref[v, 0, 0], red_ref[v, 0, 1], red_ref[v, 0, 2]
    length = lower.shape[0]
    stride = 1
    while stride < length:
        back = length - stride
        ll, ul = pltpu.roll(lower, stride, 0), pltpu.roll(upper, stride, 0)
        lr, ur = pltpu.roll(lower, back, 0), pltpu.roll(upper, back, 0)
        inv = 1.0 / (1.0 - lower * ul - upper * lr)
        target = (target - lower * pltpu.roll(target, stride, 0) - upper * pltpu.roll(target, back, 0)) * inv
        lower, upper = -lower * ll * inv, -upper * ur * inv
        stride = stride * 2
    ends = target / (1.0 + lower + upper)
    return ends[0:1], ends[1:2]


def back_substitute(it, ia, ib, first, last):
    length = it.shape[0]
    idx = lax.broadcasted_iota(jnp.int32, it.shape, 0)
    inner = it - ia * first - ib * last
    return jnp.where(idx == 0, first, jnp.where(idx == length - 1, last, inner))


def mixed(mix_ref, values):
    out = []
    for v in range(len(values)):
        summed = values[v]
        for w in range(len(values)):
            summed = summed + mix_ref[v, w : w + 1, :] * values[w]
        out.append(summed)
    return out


def az_kernel(fs_ref, nb_ref, src_ref, cell_ref, visc_ref, beta_ref, diff_ref, mix_ref, ot_ref, oa_ref, ob_ref, red_ref):
    count = fs_ref.shape[0]
    explicit = []
    for w in range(count):
        explicit.append(src_ref[w, 0] + diff_ref[w : w + 1, :] * (nb_ref[w, 0] - 2.0 * fs_ref[w, 0]))
    section_one = mixed(mix_ref, explicit)
    cell = cell_ref[0]
    for v in range(count):
        coupling = visc_ref[v : v + 1, :] * cell
        centre = 1.0 + 2.0 * coupling
        tilt = beta_ref[v : v + 1, :]
        lower = -coupling * (1.0 + tilt) / centre
        upper = -coupling * (1.0 - tilt) / centre
        it, ia, ib, rows = reduce_block(lower, upper, section_one[v] / centre)
        store_rows(red_ref, v, rows)
        ot_ref[v, 0] = it
        oa_ref[v, 0] = ia
        ob_ref[v, 0] = ib


def rad_kernel(it_ref, ia_ref, ib_ref, red_in_ref, mix_ref, cell_ref, visc_ref, ot_ref, oa_ref, ob_ref, red_ref, *, axis_name, devices):
    count = it_ref.shape[0]
    solved = []
    for w in range(count):
        first, last = reduced_ends(red_in_ref, w)
        solved.append(back_substitute(it_ref[w, 0], ia_ref[w, 0], ib_ref[w, 0], first, last))
    section_three = mixed(mix_ref, solved)
    cell = cell_ref[0]
    place = lax.axis_index(axis_name)
    for v in range(count):
        coupling = visc_ref[v : v + 1, :] * cell
        centre = 1.0 + 2.0 * coupling
        side = (-coupling / centre).T
        it, ia, ib, rows = reduce_block(side, side, (section_three[v] / centre).T)
        (lf, le), (uf, ue), trow = rows
        lf = jnp.where(place == 0, jnp.zeros_like(lf), lf)
        ue = jnp.where(place == devices - 1, jnp.zeros_like(ue), ue)
        store_rows(red_ref, v, ((lf, le), (uf, ue), trow))
        ot_ref[v, 0] = it
        oa_ref[v, 0] = ia
        ob_ref[v, 0] = ib


def out_kernel(it_ref, ia_ref, ib_ref, red_in_ref, mix_ref, out_ref):
    count = it_ref.shape[0]
    solved = []
    for w in range(count):
        first, last = reduced_ends(red_in_ref, w)
        solved.append(back_substitute(it_ref[w, 0], ia_ref[w, 0], ib_ref[w, 0], first, last).T)
    for v, value in enumerate(mixed(mix_ref, solved)):
        out_ref[v, 0] = value


def az_sweep(flow_state, nb, source, cell_az, visc_az, beta_az, axial_diff, mix_in):
    nv, nz, na, nr = flow_state.shape
    chunk = 128 if nr % 128 == 0 else nr
    big = pl.BlockSpec((nv, 1, na, chunk), lambda z, c: (0, z, 0, c))
    cell = pl.BlockSpec((1, na, chunk), lambda z, c: (z, 0, c))
    par = pl.BlockSpec((nv, chunk), lambda z, c: (0, c))
    mixs = pl.BlockSpec((nv, nv, chunk), lambda z, c: (0, 0, c))
    red = pl.BlockSpec((nv, 1, 3, 2, chunk), lambda z, c: (0, z, 0, 0, c))
    out = jax.ShapeDtypeStruct(flow_state.shape, flow_state.dtype)
    return pl.pallas_call(
        az_kernel,
        grid=(nz, nr // chunk),
        in_specs=[big, big, big, cell, par, par, par, mixs],
        out_specs=[big, big, big, red],
        out_shape=[out, out, out, jax.ShapeDtypeStruct((nv, nz, 3, 2, nr), flow_state.dtype)],
    )(flow_state, nb, source, cell_az, visc_az, beta_az, axial_diff, mix_in)


def rad_sweep(it, ia, ib, red_in, mix_mid, cell_rad, visc_local):
    nv, nz, na, nr = it.shape
    big = pl.BlockSpec((nv, 1, na, nr), lambda z: (0, z, 0, 0))
    big_t = pl.BlockSpec((nv, 1, nr, na), lambda z: (0, z, 0, 0))
    red_in_spec = pl.BlockSpec((nv, 1) + red_in.shape[2:], lambda z: (0, z, 0, 0, 0))
    mixs = pl.BlockSpec((nv, nv, nr), lambda z: (0, 0, 0))
    cell = pl.BlockSpec((1, na, nr), lambda z: (z, 0, 0))
    par = pl.BlockSpec((nv, nr), lambda z: (0, 0))
    red = pl.BlockSpec((nv, 1, 3, 2, na), lambda z: (0, z, 0, 0, 0))
    out = jax.ShapeDtypeStruct((nv, nz, nr, na), it.dtype)
    kernel = functools.partial(rad_kernel, axis_name="rad", devices=lax.axis_size("rad"))
    return pl.pallas_call(
        kernel,
        grid=(nz,),
        in_specs=[big, big, big, red_in_spec, mixs, cell, par],
        out_specs=[big_t, big_t, big_t, red],
        out_shape=[out, out, out, jax.ShapeDtypeStruct((nv, nz, 3, 2, na), it.dtype)],
    )(it, ia, ib, red_in, mix_mid, cell_rad, visc_local)


def out_sweep(it, ia, ib, red_in, mix_out):
    nv, nz, nr, na = it.shape
    big_t = pl.BlockSpec((nv, 1, nr, na), lambda z: (0, z, 0, 0))
    big = pl.BlockSpec((nv, 1, na, nr), lambda z: (0, z, 0, 0))
    red_in_spec = pl.BlockSpec((nv, 1) + red_in.shape[2:], lambda z: (0, z, 0, 0, 0))
    mixs = pl.BlockSpec((nv, nv, nr), lambda z: (0, 0, 0))
    return pl.pallas_call(
        out_kernel,
        grid=(nz,),
        in_specs=[big_t, big_t, big_t, red_in_spec, mixs],
        out_specs=big,
        out_shape=jax.ShapeDtypeStruct((nv, nz, na, nr), it.dtype),
    )(it, ia, ib, red_in, mix_out)


def gathered(block, axis_name, dim):
    count = lax.axis_size(axis_name)
    received = [block]
    for offset in range(1, count):
        pairs = [((i + offset) % count, i) for i in range(count)]
        received.append(lax.ppermute(block, axis_name, pairs))
    return jnp.concatenate(received, axis=dim)


def neighbour_planes(block, axis_name):
    count = lax.axis_size(axis_name)
    if count == 2:
        return lax.ppermute(block, axis_name, [(0, 1), (1, 0)])
    padded = with_halo(block, ((axis_name, 1),), 1, False)
    return padded[:, :-2] + padded[:, 2:]


def mix(matrix, values):
    mixed_rows = []
    for out_var in range(values.shape[0]):
        summed = values[out_var]
        for in_var in range(values.shape[0]):
            summed = summed + matrix[out_var, in_var][None, None, :] * values[in_var]
        mixed_rows.append(summed)
    return jnp.stack(mixed_rows)


def per_device(
    flow_state,
    source,
    cell_az,
    cell_rad,
    visc_az,
    beta_az,
    visc_rad,
    axial_diff,
    mix_in,
    mix_mid,
    mix_out,
):
    rad_cells = flow_state.shape[3]
    nb = neighbour_planes(flow_state, "ax")
    it, ia, ib, red = az_sweep(flow_state, nb, source, cell_az, visc_az, beta_az, axial_diff, mix_in)
    red = gathered(red, "az", 3)
    visc_local = lax.dynamic_slice_in_dim(visc_rad, lax.axis_index("rad") * rad_cells, rad_cells, 1)
    it, ia, ib, red = rad_sweep(it, ia, ib, red, mix_mid, cell_rad, visc_local)
    red = gathered(red, "rad", 3)
    return out_sweep(it, ia, ib, red, mix_out)


def solution(mesh):
    in_specs = (
        P(None, "ax", "az", "rad"),
        P(None, "ax", "az", "rad"),
        P("ax", "az", "rad"),
        P("ax", "az", "rad"),
        P(None, "rad"),
        P(None, "rad"),
        P(),
        P(None, "rad"),
        P(None, None, "rad"),
        P(None, None, "rad"),
        P(None, None, "rad"),
    )
    out_specs = P(None, "ax", "az", "rad")
    return jax.shard_map(
        per_device, mesh=mesh, in_specs=in_specs, out_specs=out_specs, check_vma=False
    )
```

```python
import jax
import jax.numpy as jnp
from jax import lax
from jax.experimental import pallas as pl
from jax.experimental.pallas import tpu as pltpu
from jax.sharding import PartitionSpec as P
import functools


def with_halo(block, sides, width, periodic):
    for axis, dim in sides:
        count = lax.axis_size(axis)
        forward = [(i, i + 1) for i in range(count - 1)]
        if periodic:
            forward.append((count - 1, 0))
        backward = [(target, source) for source, target in forward]
        low = lax.ppermute(
            lax.slice_in_dim(block, block.shape[dim] - width, None, axis=dim), axis, forward
        )
        high = lax.ppermute(lax.slice_in_dim(block, 0, width, axis=dim), axis, backward)
        block = jnp.concatenate([low, block, high], axis=dim)
    return block


def shifted(values, offset, axis, periodic):
    if periodic:
        return jnp.roll(values, offset, axis)
    length = values.shape[axis]
    zero_shape = list(values.shape)
    zero_shape[axis] = abs(offset)
    zeros = jnp.zeros(zero_shape, values.dtype)
    if offset > 0:
        kept = lax.slice_in_dim(values, 0, length - offset, axis=axis)
        return jnp.concatenate([zeros, kept], axis=axis)
    kept = lax.slice_in_dim(values, -offset, length, axis=axis)
    return jnp.concatenate([kept, zeros], axis=axis)


def cyclic_reduce(lower, upper, rhs, axis, periodic, steps_below):
    stride = 1
    while stride < steps_below:
        ll, ul = shifted(lower, stride, axis, periodic), shifted(upper, stride, axis, periodic)
        lr, ur = shifted(lower, -stride, axis, periodic), shifted(upper, -stride, axis, periodic)
        inv = 1.0 / (1.0 - lower * ul - upper * lr)
        rhs = [
            (r - lower * shifted(r, stride, axis, periodic) - upper * shifted(r, -stride, axis, periodic)) * inv
            for r in rhs
        ]
        lower, upper = -lower * ll * inv, -upper * ur * inv
        stride = stride * 2
    return lower, upper, rhs


def reduce_block(lower, upper, target):
    length = lower.shape[0]
    idx = lax.broadcasted_iota(jnp.int32, lower.shape, 0)
    edge = (idx == 0) | (idx == length - 1)
    second = idx == 1
    penult = idx == length - 2
    zero = jnp.zeros_like(lower)
    il = jnp.where(edge | second, zero, lower)
    iu = jnp.where(edge | penult, zero, upper)
    rhs = [jnp.where(edge, zero, target), jnp.where(second, lower, zero), jnp.where(penult, upper, zero)]
    stride = 1
    while stride < length - 2:
        back = length - stride
        ll, ul = pltpu.roll(il, stride, 0), pltpu.roll(iu, stride, 0)
        lr, ur = pltpu.roll(il, back, 0), pltpu.roll(iu, back, 0)
        inv = 1.0 / (1.0 - il * ul - iu * lr)
        rhs = [(r - il * pltpu.roll(r, stride, 0) - iu * pltpu.roll(r, back, 0)) * inv for r in rhs]
        il, iu = -il * ll * inv, -iu * ur * inv
        stride = stride * 2
    it, ia, ib = rhs
    l0, u0, t0 = lower[0:1], upper[0:1], target[0:1]
    le, ue, te = lower[length - 1 :], upper[length - 1 :], target[length - 1 :]
    a1, b1, t1 = ia[1:2], ib[1:2], it[1:2]
    a2, b2, t2 = ia[length - 2 : length - 1], ib[length - 2 : length - 1], it[length - 2 : length - 1]
    inv_f = 1.0 / (1.0 - u0 * a1)
    inv_e = 1.0 / (1.0 - le * b2)
    rows = (
        (l0 * inv_f, -le * a2 * inv_e),
        (-u0 * b1 * inv_f, ue * inv_e),
        ((t0 - u0 * t1) * inv_f, (te - le * t2) * inv_e),
    )
    return it, ia, ib, rows


def store_rows(red_ref, v, rows):
    for q, pair in enumerate(rows):
        for i, value in enumerate(pair):
            red_ref[v, 0, q, i : i + 1, :] = value


def reduced_ends(red_refs, rows_ref, v):
    for k, ref in enumerate(red_refs):
        rows_ref[:, 2 * k : 2 * k + 2, :] = ref[v, 0]
    lower, upper, target = rows_ref[0], rows_ref[1], rows_ref[2]
    length = lower.shape[0]
    stride = 1
    while stride < length:
        back = length - stride
        ll, ul = pltpu.roll(lower, stride, 0), pltpu.roll(upper, stride, 0)
        lr, ur = pltpu.roll(lower, back, 0), pltpu.roll(upper, back, 0)
        inv = 1.0 / (1.0 - lower * ul - upper * lr)
        target = (target - lower * pltpu.roll(target, stride, 0) - upper * pltpu.roll(target, back, 0)) * inv
        lower, upper = -lower * ll * inv, -upper * ur * inv
        stride = stride * 2
    ends = target / (1.0 + lower + upper)
    return ends[0:1], ends[1:2]


def back_substitute(it, ia, ib, first, last):
    length = it.shape[0]
    idx = lax.broadcasted_iota(jnp.int32, it.shape, 0)
    inner = it - ia * first - ib * last
    return jnp.where(idx == 0, first, jnp.where(idx == length - 1, last, inner))


def mixed(mix_ref, values):
    out = []
    for v in range(len(values)):
        summed = values[v]
        for w in range(len(values)):
            summed = summed + mix_ref[v, w : w + 1, :] * values[w]
        out.append(summed)
    return out


def az_kernel(fs_ref, nb_ref, src_ref, cell_ref, visc_ref, beta_ref, diff_ref, mix_ref, ot_ref, oa_ref, ob_ref, red_ref):
    count = fs_ref.shape[0]
    explicit = []
    for w in range(count):
        explicit.append(src_ref[w, 0] + diff_ref[w : w + 1, :] * (nb_ref[w, 0] - 2.0 * fs_ref[w, 0]))
    section_one = mixed(mix_ref, explicit)
    cell = cell_ref[0]
    for v in range(count):
        coupling = visc_ref[v : v + 1, :] * cell
        centre = 1.0 + 2.0 * coupling
        tilt = beta_ref[v : v + 1, :]
        lower = -coupling * (1.0 + tilt) / centre
        upper = -coupling * (1.0 - tilt) / centre
        it, ia, ib, rows = reduce_block(lower, upper, section_one[v] / centre)
        store_rows(red_ref, v, rows)
        ot_ref[v, 0] = it
        oa_ref[v, 0] = ia
        ob_ref[v, 0] = ib


def rad_kernel(*refs, axis_name, devices, pieces):
    it_ref, ia_ref, ib_ref = refs[:3]
    red_in = refs[3 : 3 + pieces]
    mix_ref, cell_ref, visc_ref, ot_ref, oa_ref, ob_ref, red_ref, rows_ref = refs[3 + pieces :]
    count = it_ref.shape[0]
    cells = it_ref.shape[3]
    place = lax.axis_index(axis_name)
    visc = visc_ref[:, pl.ds(pl.multiple_of(place * cells, cells), cells)]
    solved = []
    for w in range(count):
        first, last = reduced_ends(red_in, rows_ref, w)
        solved.append(back_substitute(it_ref[w, 0], ia_ref[w, 0], ib_ref[w, 0], first, last))
    section_three = mixed(mix_ref, solved)
    cell = cell_ref[0]
    for v in range(count):
        coupling = visc[v : v + 1, :] * cell
        centre = 1.0 + 2.0 * coupling
        side = (-coupling / centre).T
        it, ia, ib, rows = reduce_block(side, side, (section_three[v] / centre).T)
        (lf, le), (uf, ue), trow = rows
        lf = jnp.where(place == 0, jnp.zeros_like(lf), lf)
        ue = jnp.where(place == devices - 1, jnp.zeros_like(ue), ue)
        store_rows(red_ref, v, ((lf, le), (uf, ue), trow))
        ot_ref[v, 0] = it
        oa_ref[v, 0] = ia
        ob_ref[v, 0] = ib


def out_kernel(*refs, pieces):
    it_ref, ia_ref, ib_ref = refs[:3]
    red_in = refs[3 : 3 + pieces]
    mix_ref, out_ref, rows_ref = refs[3 + pieces :]
    count = it_ref.shape[0]
    solved = []
    for w in range(count):
        first, last = reduced_ends(red_in, rows_ref, w)
        solved.append(back_substitute(it_ref[w, 0], ia_ref[w, 0], ib_ref[w, 0], first, last).T)
    for v, value in enumerate(mixed(mix_ref, solved)):
        out_ref[v, 0] = value


def az_sweep(flow_state, nb, source, cell_az, visc_az, beta_az, axial_diff, mix_in):
    nv, nz, na, nr = flow_state.shape
    chunk = 128 if nr % 128 == 0 else nr
    big = pl.BlockSpec((nv, 1, na, chunk), lambda z, c: (0, z, 0, c))
    cell = pl.BlockSpec((1, na, chunk), lambda z, c: (z, 0, c))
    par = pl.BlockSpec((nv, chunk), lambda z, c: (0, c))
    mixs = pl.BlockSpec((nv, nv, chunk), lambda z, c: (0, 0, c))
    red = pl.BlockSpec((nv, 1, 3, 2, chunk), lambda z, c: (0, z, 0, 0, c))
    out = jax.ShapeDtypeStruct(flow_state.shape, flow_state.dtype)
    return pl.pallas_call(
        az_kernel,
        grid=(nz, nr // chunk),
        in_specs=[big, big, big, cell, par, par, par, mixs],
        out_specs=[big, big, big, red],
        out_shape=[out, out, out, jax.ShapeDtypeStruct((nv, nz, 3, 2, nr), flow_state.dtype)],
    )(flow_state, nb, source, cell_az, visc_az, beta_az, axial_diff, mix_in)


def rad_sweep(it, ia, ib, red_in, mix_mid, cell_rad, visc_rad):
    nv, nz, na, nr = it.shape
    big = pl.BlockSpec((nv, 1, na, nr), lambda z: (0, z, 0, 0))
    big_t = pl.BlockSpec((nv, 1, nr, na), lambda z: (0, z, 0, 0))
    red_in_spec = pl.BlockSpec((nv, 1) + red_in[0].shape[2:], lambda z: (0, z, 0, 0, 0))
    mixs = pl.BlockSpec((nv, nv, nr), lambda z: (0, 0, 0))
    cell = pl.BlockSpec((1, na, nr), lambda z: (z, 0, 0))
    par = pl.BlockSpec(visc_rad.shape, lambda z: (0, 0))
    red = pl.BlockSpec((nv, 1, 3, 2, na), lambda z: (0, z, 0, 0, 0))
    out = jax.ShapeDtypeStruct((nv, nz, nr, na), it.dtype)
    pieces = len(red_in)
    kernel = functools.partial(rad_kernel, axis_name="rad", devices=lax.axis_size("rad"), pieces=pieces)
    return pl.pallas_call(
        kernel,
        grid=(nz,),
        in_specs=[big, big, big] + [red_in_spec] * pieces + [mixs, cell, par],
        out_specs=[big_t, big_t, big_t, red],
        out_shape=[out, out, out, jax.ShapeDtypeStruct((nv, nz, 3, 2, na), it.dtype)],
        scratch_shapes=[pltpu.VMEM((3, 2 * pieces, nr), it.dtype)],
    )(it, ia, ib, *red_in, mix_mid, cell_rad, visc_rad)


def out_sweep(it, ia, ib, red_in, mix_out):
    nv, nz, nr, na = it.shape
    big_t = pl.BlockSpec((nv, 1, nr, na), lambda z: (0, z, 0, 0))
    big = pl.BlockSpec((nv, 1, na, nr), lambda z: (0, z, 0, 0))
    red_in_spec = pl.BlockSpec((nv, 1) + red_in[0].shape[2:], lambda z: (0, z, 0, 0, 0))
    mixs = pl.BlockSpec((nv, nv, nr), lambda z: (0, 0, 0))
    pieces = len(red_in)
    return pl.pallas_call(
        functools.partial(out_kernel, pieces=pieces),
        grid=(nz,),
        in_specs=[big_t, big_t, big_t] + [red_in_spec] * pieces + [mixs],
        out_specs=big,
        out_shape=jax.ShapeDtypeStruct((nv, nz, na, nr), it.dtype),
        scratch_shapes=[pltpu.VMEM((3, 2 * pieces, na), it.dtype)],
    )(it, ia, ib, *red_in, mix_out)


def gathered(block, axis_name):
    count = lax.axis_size(axis_name)
    received = [block]
    for offset in range(1, count):
        pairs = [((i + offset) % count, i) for i in range(count)]
        received.append(lax.ppermute(block, axis_name, pairs))
    return received


def neighbour_planes(block, axis_name):
    count = lax.axis_size(axis_name)
    if count == 2:
        return lax.ppermute(block, axis_name, [(0, 1), (1, 0)])
    padded = with_halo(block, ((axis_name, 1),), 1, False)
    return padded[:, :-2] + padded[:, 2:]


def mix(matrix, values):
    mixed_rows = []
    for out_var in range(values.shape[0]):
        summed = values[out_var]
        for in_var in range(values.shape[0]):
            summed = summed + matrix[out_var, in_var][None, None, :] * values[in_var]
        mixed_rows.append(summed)
    return jnp.stack(mixed_rows)


def per_device(
    flow_state,
    source,
    cell_az,
    cell_rad,
    visc_az,
    beta_az,
    visc_rad,
    axial_diff,
    mix_in,
    mix_mid,
    mix_out,
):
    rad_cells = flow_state.shape[3]
    nb = neighbour_planes(flow_state, "ax")
    it, ia, ib, red = az_sweep(flow_state, nb, source, cell_az, visc_az, beta_az, axial_diff, mix_in)
    red = gathered(red, "az")
    it, ia, ib, red = rad_sweep(it, ia, ib, red, mix_mid, cell_rad, visc_rad)
    red = gathered(red, "rad")
    return out_sweep(it, ia, ib, red, mix_out)


def solution(mesh):
    in_specs = (
        P(None, "ax", "az", "rad"),
        P(None, "ax", "az", "rad"),
        P("ax", "az", "rad"),
        P("ax", "az", "rad"),
        P(None, "rad"),
        P(None, "rad"),
        P(),
        P(None, "rad"),
        P(None, None, "rad"),
        P(None, None, "rad"),
        P(None, None, "rad"),
    )
    out_specs = P(None, "ax", "az", "rad")
    return jax.shard_map(
        per_device, mesh=mesh, in_specs=in_specs, out_specs=out_specs, check_vma=False
    )
```

```python
import jax
import jax.numpy as jnp
from jax import lax
from jax.experimental import pallas as pl
from jax.experimental.pallas import tpu as pltpu
from jax.sharding import PartitionSpec as P
import functools


def with_halo(block, sides, width, periodic):
    for axis, dim in sides:
        count = lax.axis_size(axis)
        forward = [(i, i + 1) for i in range(count - 1)]
        if periodic:
            forward.append((count - 1, 0))
        backward = [(target, source) for source, target in forward]
        low = lax.ppermute(
            lax.slice_in_dim(block, block.shape[dim] - width, None, axis=dim), axis, forward
        )
        high = lax.ppermute(lax.slice_in_dim(block, 0, width, axis=dim), axis, backward)
        block = jnp.concatenate([low, block, high], axis=dim)
    return block


def shifted(values, offset, axis, periodic):
    if periodic:
        return jnp.roll(values, offset, axis)
    length = values.shape[axis]
    zero_shape = list(values.shape)
    zero_shape[axis] = abs(offset)
    zeros = jnp.zeros(zero_shape, values.dtype)
    if offset > 0:
        kept = lax.slice_in_dim(values, 0, length - offset, axis=axis)
        return jnp.concatenate([zeros, kept], axis=axis)
    kept = lax.slice_in_dim(values, -offset, length, axis=axis)
    return jnp.concatenate([kept, zeros], axis=axis)


def cyclic_reduce(lower, upper, rhs, axis, periodic, steps_below):
    stride = 1
    while stride < steps_below:
        ll, ul = shifted(lower, stride, axis, periodic), shifted(upper, stride, axis, periodic)
        lr, ur = shifted(lower, -stride, axis, periodic), shifted(upper, -stride, axis, periodic)
        inv = 1.0 / (1.0 - lower * ul - upper * lr)
        rhs = [
            (r - lower * shifted(r, stride, axis, periodic) - upper * shifted(r, -stride, axis, periodic)) * inv
            for r in rhs
        ]
        lower, upper = -lower * ll * inv, -upper * ur * inv
        stride = stride * 2
    return lower, upper, rhs


def reduce_block(lower, upper, target):
    length = lower.shape[0]
    idx = lax.broadcasted_iota(jnp.int32, lower.shape, 0)
    edge = (idx == 0) | (idx == length - 1)
    second = idx == 1
    penult = idx == length - 2
    zero = jnp.zeros_like(lower)
    il = jnp.where(edge | second, zero, lower)
    iu = jnp.where(edge | penult, zero, upper)
    rhs = [jnp.where(edge, zero, target), jnp.where(second, lower, zero), jnp.where(penult, upper, zero)]
    stride = 1
    while stride < length - 2:
        back = length - stride
        ll, ul = pltpu.roll(il, stride, 0), pltpu.roll(iu, stride, 0)
        lr, ur = pltpu.roll(il, back, 0), pltpu.roll(iu, back, 0)
        inv = 1.0 / (1.0 - il * ul - iu * lr)
        rhs = [(r - il * pltpu.roll(r, stride, 0) - iu * pltpu.roll(r, back, 0)) * inv for r in rhs]
        il, iu = -il * ll * inv, -iu * ur * inv
        stride = stride * 2
    it, ia, ib = rhs
    l0, u0, t0 = lower[0:1], upper[0:1], target[0:1]
    le, ue, te = lower[length - 1 :], upper[length - 1 :], target[length - 1 :]
    a1, b1, t1 = ia[1:2], ib[1:2], it[1:2]
    a2, b2, t2 = ia[length - 2 : length - 1], ib[length - 2 : length - 1], it[length - 2 : length - 1]
    inv_f = 1.0 / (1.0 - u0 * a1)
    inv_e = 1.0 / (1.0 - le * b2)
    rows = (
        (l0 * inv_f, -le * a2 * inv_e),
        (-u0 * b1 * inv_f, ue * inv_e),
        ((t0 - u0 * t1) * inv_f, (te - le * t2) * inv_e),
    )
    return it, ia, ib, rows


def store_rows(red_ref, v, rows):
    for q, pair in enumerate(rows):
        for i, value in enumerate(pair):
            red_ref[v, 0, q, i : i + 1, :] = value


def reduced_ends(red_refs, rows_ref, v):
    for k, ref in enumerate(red_refs):
        rows_ref[:, 2 * k : 2 * k + 2, :] = ref[v, 0]
    lower, upper, target = rows_ref[0], rows_ref[1], rows_ref[2]
    length = lower.shape[0]
    stride = 1
    while stride < length:
        back = length - stride
        ll, ul = pltpu.roll(lower, stride, 0), pltpu.roll(upper, stride, 0)
        lr, ur = pltpu.roll(lower, back, 0), pltpu.roll(upper, back, 0)
        inv = 1.0 / (1.0 - lower * ul - upper * lr)
        target = (target - lower * pltpu.roll(target, stride, 0) - upper * pltpu.roll(target, back, 0)) * inv
        lower, upper = -lower * ll * inv, -upper * ur * inv
        stride = stride * 2
    ends = target / (1.0 + lower + upper)
    return ends[0:1], ends[1:2]


def back_substitute(it, ia, ib, first, last):
    length = it.shape[0]
    idx = lax.broadcasted_iota(jnp.int32, it.shape, 0)
    inner = it - ia * first - ib * last
    return jnp.where(idx == 0, first, jnp.where(idx == length - 1, last, inner))


def mixed(mix_ref, values):
    out = []
    for v in range(len(values)):
        summed = values[v]
        for w in range(len(values)):
            summed = summed + mix_ref[v, w : w + 1, :] * values[w]
        out.append(summed)
    return out


def az_kernel(fs_ref, nb_lo_ref, nb_hi_ref, src_ref, cell_ref, visc_ref, beta_ref, diff_ref, mix_ref, ot_ref, oa_ref, ob_ref, red_ref):
    count = fs_ref.shape[0]
    split = nb_lo_ref.shape[0]
    explicit = []
    for w in range(count):
        nb = nb_lo_ref[w, 0] if w < split else nb_hi_ref[w - split, 0]
        explicit.append(src_ref[w, 0] + diff_ref[w : w + 1, :] * (nb - 2.0 * fs_ref[w, 0]))
    section_one = mixed(mix_ref, explicit)
    cell = cell_ref[0]
    for v in range(count):
        coupling = visc_ref[v : v + 1, :] * cell
        centre = 1.0 + 2.0 * coupling
        tilt = beta_ref[v : v + 1, :]
        lower = -coupling * (1.0 + tilt) / centre
        upper = -coupling * (1.0 - tilt) / centre
        it, ia, ib, rows = reduce_block(lower, upper, section_one[v] / centre)
        store_rows(red_ref, v, rows)
        ot_ref[v, 0] = it
        oa_ref[v, 0] = ia
        ob_ref[v, 0] = ib


def rad_kernel(*refs, axis_name, devices, pieces):
    it_ref, ia_ref, ib_ref = refs[:3]
    red_in = refs[3 : 3 + pieces]
    mix_ref, cell_ref, visc_ref, ot_ref, oa_ref, ob_ref, red_ref, rows_ref = refs[3 + pieces :]
    count = it_ref.shape[0]
    cells = it_ref.shape[3]
    place = lax.axis_index(axis_name)
    visc = visc_ref[:, pl.ds(pl.multiple_of(place * cells, cells), cells)]
    solved = []
    for w in range(count):
        first, last = reduced_ends(red_in, rows_ref, w)
        solved.append(back_substitute(it_ref[w, 0], ia_ref[w, 0], ib_ref[w, 0], first, last))
    section_three = mixed(mix_ref, solved)
    cell = cell_ref[0]
    for v in range(count):
        coupling = visc[v : v + 1, :] * cell
        centre = 1.0 + 2.0 * coupling
        side = (-coupling / centre).T
        it, ia, ib, rows = reduce_block(side, side, (section_three[v] / centre).T)
        (lf, le), (uf, ue), trow = rows
        lf = jnp.where(place == 0, jnp.zeros_like(lf), lf)
        ue = jnp.where(place == devices - 1, jnp.zeros_like(ue), ue)
        store_rows(red_ref, v, ((lf, le), (uf, ue), trow))
        ot_ref[v, 0] = it
        oa_ref[v, 0] = ia
        ob_ref[v, 0] = ib


def out_kernel(*refs, pieces):
    it_ref, ia_ref, ib_ref = refs[:3]
    red_in = refs[3 : 3 + pieces]
    mix_ref, out_ref, rows_ref = refs[3 + pieces :]
    count = it_ref.shape[0]
    solved = []
    for w in range(count):
        first, last = reduced_ends(red_in, rows_ref, w)
        solved.append(back_substitute(it_ref[w, 0], ia_ref[w, 0], ib_ref[w, 0], first, last).T)
    for v, value in enumerate(mixed(mix_ref, solved)):
        out_ref[v, 0] = value


def az_sweep(flow_state, nb, source, cell_az, visc_az, beta_az, axial_diff, mix_in):
    nv, nz, na, nr = flow_state.shape
    chunk = 128 if nr % 128 == 0 else nr
    big = pl.BlockSpec((nv, 1, na, chunk), lambda z, c: (0, z, 0, c))
    lo = pl.BlockSpec((nb[0].shape[0], 1, na, chunk), lambda z, c: (0, z, 0, c))
    hi = pl.BlockSpec((nb[1].shape[0], 1, na, chunk), lambda z, c: (0, z, 0, c))
    cell = pl.BlockSpec((1, na, chunk), lambda z, c: (z, 0, c))
    par = pl.BlockSpec((nv, chunk), lambda z, c: (0, c))
    mixs = pl.BlockSpec((nv, nv, chunk), lambda z, c: (0, 0, c))
    red = pl.BlockSpec((nv, 1, 3, 2, chunk), lambda z, c: (0, z, 0, 0, c))
    out = jax.ShapeDtypeStruct(flow_state.shape, flow_state.dtype)
    return pl.pallas_call(
        az_kernel,
        grid=(nz, nr // chunk),
        in_specs=[big, lo, hi, big, cell, par, par, par, mixs],
        out_specs=[big, big, big, red],
        out_shape=[out, out, out, jax.ShapeDtypeStruct((nv, nz, 3, 2, nr), flow_state.dtype)],
    )(flow_state, nb[0], nb[1], source, cell_az, visc_az, beta_az, axial_diff, mix_in)


def rad_sweep(it, ia, ib, red_in, mix_mid, cell_rad, visc_rad):
    nv, nz, na, nr = it.shape
    big = pl.BlockSpec((nv, 1, na, nr), lambda z: (0, z, 0, 0))
    big_t = pl.BlockSpec((nv, 1, nr, na), lambda z: (0, z, 0, 0))
    red_in_spec = pl.BlockSpec((nv, 1) + red_in[0].shape[2:], lambda z: (0, z, 0, 0, 0))
    mixs = pl.BlockSpec((nv, nv, nr), lambda z: (0, 0, 0))
    cell = pl.BlockSpec((1, na, nr), lambda z: (z, 0, 0))
    par = pl.BlockSpec(visc_rad.shape, lambda z: (0, 0))
    red = pl.BlockSpec((nv, 1, 3, 2, na), lambda z: (0, z, 0, 0, 0))
    out = jax.ShapeDtypeStruct((nv, nz, nr, na), it.dtype)
    pieces = len(red_in)
    kernel = functools.partial(rad_kernel, axis_name="rad", devices=lax.axis_size("rad"), pieces=pieces)
    return pl.pallas_call(
        kernel,
        grid=(nz,),
        in_specs=[big, big, big] + [red_in_spec] * pieces + [mixs, cell, par],
        out_specs=[big_t, big_t, big_t, red],
        out_shape=[out, out, out, jax.ShapeDtypeStruct((nv, nz, 3, 2, na), it.dtype)],
        scratch_shapes=[pltpu.VMEM((3, 2 * pieces, nr), it.dtype)],
    )(it, ia, ib, *red_in, mix_mid, cell_rad, visc_rad)


def out_sweep(it, ia, ib, red_in, mix_out):
    nv, nz, nr, na = it.shape
    big_t = pl.BlockSpec((nv, 1, nr, na), lambda z: (0, z, 0, 0))
    big = pl.BlockSpec((nv, 1, na, nr), lambda z: (0, z, 0, 0))
    red_in_spec = pl.BlockSpec((nv, 1) + red_in[0].shape[2:], lambda z: (0, z, 0, 0, 0))
    mixs = pl.BlockSpec((nv, nv, nr), lambda z: (0, 0, 0))
    pieces = len(red_in)
    return pl.pallas_call(
        functools.partial(out_kernel, pieces=pieces),
        grid=(nz,),
        in_specs=[big_t, big_t, big_t] + [red_in_spec] * pieces + [mixs],
        out_specs=big,
        out_shape=jax.ShapeDtypeStruct((nv, nz, na, nr), it.dtype),
        scratch_shapes=[pltpu.VMEM((3, 2 * pieces, na), it.dtype)],
    )(it, ia, ib, *red_in, mix_out)


def gathered(block, axis_name):
    count = lax.axis_size(axis_name)
    received = [block]
    for offset in range(1, count):
        pairs = [((i + offset) % count, i) for i in range(count)]
        received.append(lax.ppermute(block, axis_name, pairs))
    return received


def neighbour_planes(block, axis_name):
    count = lax.axis_size(axis_name)
    split = (block.shape[0] + 1) // 2
    pieces = (block[:split], block[split:])
    if count == 2:
        return [lax.ppermute(piece, axis_name, [(0, 1), (1, 0)]) for piece in pieces]
    out = []
    for piece in pieces:
        padded = with_halo(piece, ((axis_name, 1),), 1, False)
        out.append(padded[:, :-2] + padded[:, 2:])
    return out


def mix(matrix, values):
    mixed_rows = []
    for out_var in range(values.shape[0]):
        summed = values[out_var]
        for in_var in range(values.shape[0]):
            summed = summed + matrix[out_var, in_var][None, None, :] * values[in_var]
        mixed_rows.append(summed)
    return jnp.stack(mixed_rows)


def per_device(
    flow_state,
    source,
    cell_az,
    cell_rad,
    visc_az,
    beta_az,
    visc_rad,
    axial_diff,
    mix_in,
    mix_mid,
    mix_out,
):
    rad_cells = flow_state.shape[3]
    nb = neighbour_planes(flow_state, "ax")
    it, ia, ib, red = az_sweep(flow_state, nb, source, cell_az, visc_az, beta_az, axial_diff, mix_in)
    red = gathered(red, "az")
    it, ia, ib, red = rad_sweep(it, ia, ib, red, mix_mid, cell_rad, visc_rad)
    red = gathered(red, "rad")
    return out_sweep(it, ia, ib, red, mix_out)


def solution(mesh):
    in_specs = (
        P(None, "ax", "az", "rad"),
        P(None, "ax", "az", "rad"),
        P("ax", "az", "rad"),
        P("ax", "az", "rad"),
        P(None, "rad"),
        P(None, "rad"),
        P(),
        P(None, "rad"),
        P(None, None, "rad"),
        P(None, None, "rad"),
        P(None, None, "rad"),
    )
    out_specs = P(None, "ax", "az", "rad")
    return jax.shard_map(
        per_device, mesh=mesh, in_specs=in_specs, out_specs=out_specs, check_vma=False
    )
```

```python
import jax
import jax.numpy as jnp
from jax import lax
from jax.experimental import pallas as pl
from jax.experimental.pallas import tpu as pltpu
from jax.sharding import PartitionSpec as P
import functools


def with_halo(block, sides, width, periodic):
    for axis, dim in sides:
        count = lax.axis_size(axis)
        forward = [(i, i + 1) for i in range(count - 1)]
        if periodic:
            forward.append((count - 1, 0))
        backward = [(target, source) for source, target in forward]
        low = lax.ppermute(
            lax.slice_in_dim(block, block.shape[dim] - width, None, axis=dim), axis, forward
        )
        high = lax.ppermute(lax.slice_in_dim(block, 0, width, axis=dim), axis, backward)
        block = jnp.concatenate([low, block, high], axis=dim)
    return block


def shifted(values, offset, axis, periodic):
    if periodic:
        return jnp.roll(values, offset, axis)
    length = values.shape[axis]
    zero_shape = list(values.shape)
    zero_shape[axis] = abs(offset)
    zeros = jnp.zeros(zero_shape, values.dtype)
    if offset > 0:
        kept = lax.slice_in_dim(values, 0, length - offset, axis=axis)
        return jnp.concatenate([zeros, kept], axis=axis)
    kept = lax.slice_in_dim(values, -offset, length, axis=axis)
    return jnp.concatenate([kept, zeros], axis=axis)


def cyclic_reduce(lower, upper, rhs, axis, periodic, steps_below):
    stride = 1
    while stride < steps_below:
        ll, ul = shifted(lower, stride, axis, periodic), shifted(upper, stride, axis, periodic)
        lr, ur = shifted(lower, -stride, axis, periodic), shifted(upper, -stride, axis, periodic)
        inv = 1.0 / (1.0 - lower * ul - upper * lr)
        rhs = [
            (r - lower * shifted(r, stride, axis, periodic) - upper * shifted(r, -stride, axis, periodic)) * inv
            for r in rhs
        ]
        lower, upper = -lower * ll * inv, -upper * ur * inv
        stride = stride * 2
    return lower, upper, rhs


def interior(lower, upper):
    length = lower.shape[0]
    idx = lax.broadcasted_iota(jnp.int32, lower.shape, 0)
    edge = (idx == 0) | (idx == length - 1)
    second = idx == 1
    penult = idx == length - 2
    zero = jnp.zeros_like(lower)
    il = jnp.where(edge | second, zero, lower)
    iu = jnp.where(edge | penult, zero, upper)
    return il, iu, jnp.where(edge, zero, 1.0), jnp.where(second, lower, zero), jnp.where(penult, upper, zero)


def pcr_levels(il, iu, rhs):
    length = il.shape[0]
    stride = 1
    while stride < length - 2:
        back = length - stride
        ll, ul = pltpu.roll(il, stride, 0), pltpu.roll(iu, stride, 0)
        lr, ur = pltpu.roll(il, back, 0), pltpu.roll(iu, back, 0)
        inv = 1.0 / (1.0 - il * ul - iu * lr)
        rhs = [(r - il * pltpu.roll(r, stride, 0) - iu * pltpu.roll(r, back, 0)) * inv for r in rhs]
        il, iu = -il * ll * inv, -iu * ur * inv
        stride = stride * 2
    return rhs


def interface_rows(lower, upper, t0, te, t1, t2, a1, b1, a2, b2):
    length = lower.shape[0]
    l0, u0 = lower[0:1], upper[0:1]
    le, ue = lower[length - 1 :], upper[length - 1 :]
    inv_f = 1.0 / (1.0 - u0 * a1)
    inv_e = 1.0 / (1.0 - le * b2)
    return (
        (l0 * inv_f, -le * a2 * inv_e),
        (-u0 * b1 * inv_f, ue * inv_e),
        ((t0 - u0 * t1) * inv_f, (te - le * t2) * inv_e),
    )


def reduce_block(lower, upper, target):
    length = lower.shape[0]
    il, iu, keep, a_init, b_init = interior(lower, upper)
    it, ia, ib = pcr_levels(il, iu, [target * keep, a_init, b_init])
    n2 = length - 2
    rows = interface_rows(
        lower, upper, target[0:1], target[length - 1 :], it[1:2], it[n2 : n2 + 1],
        ia[1:2], ib[1:2], ia[n2 : n2 + 1], ib[n2 : n2 + 1],
    )
    return it, ia, ib, rows


def store_rows(red_ref, v, rows):
    for q, pair in enumerate(rows):
        for i, value in enumerate(pair):
            red_ref[v, 0, q, i : i + 1, :] = value


def reduced_ends(red_refs, rows_ref, v):
    for k, ref in enumerate(red_refs):
        rows_ref[:, 2 * k : 2 * k + 2, :] = ref[v, 0]
    lower, upper, target = rows_ref[0], rows_ref[1], rows_ref[2]
    length = lower.shape[0]
    stride = 1
    while stride < length:
        back = length - stride
        ll, ul = pltpu.roll(lower, stride, 0), pltpu.roll(upper, stride, 0)
        lr, ur = pltpu.roll(lower, back, 0), pltpu.roll(upper, back, 0)
        inv = 1.0 / (1.0 - lower * ul - upper * lr)
        target = (target - lower * pltpu.roll(target, stride, 0) - upper * pltpu.roll(target, back, 0)) * inv
        lower, upper = -lower * ll * inv, -upper * ur * inv
        stride = stride * 2
    ends = target / (1.0 + lower + upper)
    return ends[0:1], ends[1:2]


def back_substitute(it, ia, ib, first, last):
    length = it.shape[0]
    idx = lax.broadcasted_iota(jnp.int32, it.shape, 0)
    inner = it - ia * first - ib * last
    return jnp.where(idx == 0, first, jnp.where(idx == length - 1, last, inner))


def mixed(mix_ref, values):
    out = []
    for v in range(len(values)):
        summed = values[v]
        for w in range(len(values)):
            summed = summed + mix_ref[v, w : w + 1, :] * values[w]
        out.append(summed)
    return out


def az_coefficients(cell, visc_ref, beta_ref, v):
    coupling = visc_ref[v : v + 1, :] * cell
    centre = 1.0 + 2.0 * coupling
    tilt = beta_ref[v : v + 1, :]
    lower = -coupling * (1.0 + tilt) / centre
    upper = -coupling * (1.0 - tilt) / centre
    return lower, upper, centre


def az_local_kernel(fs_ref, src_ref, cell_ref, visc_ref, beta_ref, diff_ref, mix_ref, ot_ref, oa_ref, ob_ref, edge_ref):
    count = fs_ref.shape[0]
    explicit = [src_ref[w, 0] + diff_ref[w : w + 1, :] * (-2.0 * fs_ref[w, 0]) for w in range(count)]
    section_one = mixed(mix_ref, explicit)
    cell = cell_ref[0]
    for v in range(count):
        lower, upper, centre = az_coefficients(cell, visc_ref, beta_ref, v)
        target = section_one[v] / centre
        length = lower.shape[0]
        il, iu, keep, a_init, b_init = interior(lower, upper)
        it, ia, ib = pcr_levels(il, iu, [target * keep, a_init, b_init])
        ot_ref[v, 0] = it
        oa_ref[v, 0] = ia
        ob_ref[v, 0] = ib
        n2 = length - 2
        for k, value in enumerate(
            (target[0:1], target[length - 1 :], ia[1:2], ib[1:2], ia[n2 : n2 + 1], ib[n2 : n2 + 1])
        ):
            edge_ref[v, 0, k : k + 1, :] = value


def az_plane_kernel(nb_ref, cell_ref, visc_ref, beta_ref, diff_ref, mix_ref, it_in_ref, edge_ref, ot_ref, red_ref):
    count = nb_ref.shape[0]
    explicit = [diff_ref[w : w + 1, :] * nb_ref[w, 0] for w in range(count)]
    section_one = mixed(mix_ref, explicit)
    cell = cell_ref[0]
    for v in range(count):
        lower, upper, centre = az_coefficients(cell, visc_ref, beta_ref, v)
        target = section_one[v] / centre
        length = lower.shape[0]
        il, iu, keep, _, _ = interior(lower, upper)
        (it,) = pcr_levels(il, iu, [target * keep])
        it = it_in_ref[v, 0] + it
        ot_ref[v, 0] = it
        edge = edge_ref[v, 0]
        n2 = length - 2
        rows = interface_rows(
            lower, upper, edge[0:1] + target[0:1], edge[1:2] + target[length - 1 :], it[1:2], it[n2 : n2 + 1],
            edge[2:3], edge[3:4], edge[4:5], edge[5:6],
        )
        store_rows(red_ref, v, rows)


def rad_kernel(*refs, axis_name, devices, pieces):
    it_ref, ia_ref, ib_ref = refs[:3]
    red_in = refs[3 : 3 + pieces]
    mix_ref, cell_ref, visc_ref, ot_ref, oa_ref, ob_ref, red_ref, rows_ref = refs[3 + pieces :]
    count = it_ref.shape[0]
    cells = it_ref.shape[3]
    place = lax.axis_index(axis_name)
    visc = visc_ref[:, pl.ds(pl.multiple_of(place * cells, cells), cells)]
    solved = []
    for w in range(count):
        first, last = reduced_ends(red_in, rows_ref, w)
        solved.append(back_substitute(it_ref[w, 0], ia_ref[w, 0], ib_ref[w, 0], first, last))
    section_three = mixed(mix_ref, solved)
    cell = cell_ref[0]
    for v in range(count):
        coupling = visc[v : v + 1, :] * cell
        centre = 1.0 + 2.0 * coupling
        side = (-coupling / centre).T
        it, ia, ib, rows = reduce_block(side, side, (section_three[v] / centre).T)
        (lf, le), (uf, ue), trow = rows
        lf = jnp.where(place == 0, jnp.zeros_like(lf), lf)
        ue = jnp.where(place == devices - 1, jnp.zeros_like(ue), ue)
        store_rows(red_ref, v, ((lf, le), (uf, ue), trow))
        ot_ref[v, 0] = it
        oa_ref[v, 0] = ia
        ob_ref[v, 0] = ib


def out_kernel(*refs, pieces):
    it_ref, ia_ref, ib_ref = refs[:3]
    red_in = refs[3 : 3 + pieces]
    mix_ref, out_ref, rows_ref = refs[3 + pieces :]
    count = it_ref.shape[0]
    solved = []
    for w in range(count):
        first, last = reduced_ends(red_in, rows_ref, w)
        solved.append(back_substitute(it_ref[w, 0], ia_ref[w, 0], ib_ref[w, 0], first, last).T)
    for v, value in enumerate(mixed(mix_ref, solved)):
        out_ref[v, 0] = value


def az_sweep(flow_state, nb, source, cell_az, visc_az, beta_az, axial_diff, mix_in):
    nv, nz, na, nr = flow_state.shape
    chunk = 128 if nr % 128 == 0 else nr
    grid = (nz, nr // chunk)
    big = pl.BlockSpec((nv, 1, na, chunk), lambda z, c: (0, z, 0, c))
    cell = pl.BlockSpec((1, na, chunk), lambda z, c: (z, 0, c))
    par = pl.BlockSpec((nv, chunk), lambda z, c: (0, c))
    mixs = pl.BlockSpec((nv, nv, chunk), lambda z, c: (0, 0, c))
    edge = pl.BlockSpec((nv, 1, 6, chunk), lambda z, c: (0, z, 0, c))
    red = pl.BlockSpec((nv, 1, 3, 2, chunk), lambda z, c: (0, z, 0, 0, c))
    out = jax.ShapeDtypeStruct(flow_state.shape, flow_state.dtype)
    it, ia, ib, edges = pl.pallas_call(
        az_local_kernel,
        grid=grid,
        in_specs=[big, big, cell, par, par, par, mixs],
        out_specs=[big, big, big, edge],
        out_shape=[out, out, out, jax.ShapeDtypeStruct((nv, nz, 6, nr), flow_state.dtype)],
    )(flow_state, source, cell_az, visc_az, beta_az, axial_diff, mix_in)
    it, red = pl.pallas_call(
        az_plane_kernel,
        grid=grid,
        in_specs=[big, cell, par, par, par, mixs, big, edge],
        out_specs=[big, red],
        out_shape=[out, jax.ShapeDtypeStruct((nv, nz, 3, 2, nr), flow_state.dtype)],
        input_output_aliases={6: 0},
    )(nb, cell_az, visc_az, beta_az, axial_diff, mix_in, it, edges)
    return it, ia, ib, red


def rad_sweep(it, ia, ib, red_in, mix_mid, cell_rad, visc_rad):
    nv, nz, na, nr = it.shape
    big = pl.BlockSpec((nv, 1, na, nr), lambda z: (0, z, 0, 0))
    big_t = pl.BlockSpec((nv, 1, nr, na), lambda z: (0, z, 0, 0))
    red_in_spec = pl.BlockSpec((nv, 1) + red_in[0].shape[2:], lambda z: (0, z, 0, 0, 0))
    mixs = pl.BlockSpec((nv, nv, nr), lambda z: (0, 0, 0))
    cell = pl.BlockSpec((1, na, nr), lambda z: (z, 0, 0))
    par = pl.BlockSpec(visc_rad.shape, lambda z: (0, 0))
    red = pl.BlockSpec((nv, 1, 3, 2, na), lambda z: (0, z, 0, 0, 0))
    out = jax.ShapeDtypeStruct((nv, nz, nr, na), it.dtype)
    pieces = len(red_in)
    kernel = functools.partial(rad_kernel, axis_name="rad", devices=lax.axis_size("rad"), pieces=pieces)
    return pl.pallas_call(
        kernel,
        grid=(nz,),
        in_specs=[big, big, big] + [red_in_spec] * pieces + [mixs, cell, par],
        out_specs=[big_t, big_t, big_t, red],
        out_shape=[out, out, out, jax.ShapeDtypeStruct((nv, nz, 3, 2, na), it.dtype)],
        scratch_shapes=[pltpu.VMEM((3, 2 * pieces, nr), it.dtype)],
    )(it, ia, ib, *red_in, mix_mid, cell_rad, visc_rad)


def out_sweep(it, ia, ib, red_in, mix_out):
    nv, nz, nr, na = it.shape
    big_t = pl.BlockSpec((nv, 1, nr, na), lambda z: (0, z, 0, 0))
    big = pl.BlockSpec((nv, 1, na, nr), lambda z: (0, z, 0, 0))
    red_in_spec = pl.BlockSpec((nv, 1) + red_in[0].shape[2:], lambda z: (0, z, 0, 0, 0))
    mixs = pl.BlockSpec((nv, nv, nr), lambda z: (0, 0, 0))
    pieces = len(red_in)
    return pl.pallas_call(
        functools.partial(out_kernel, pieces=pieces),
        grid=(nz,),
        in_specs=[big_t, big_t, big_t] + [red_in_spec] * pieces + [mixs],
        out_specs=big,
        out_shape=jax.ShapeDtypeStruct((nv, nz, na, nr), it.dtype),
        scratch_shapes=[pltpu.VMEM((3, 2 * pieces, na), it.dtype)],
    )(it, ia, ib, *red_in, mix_out)


def gathered(block, axis_name):
    count = lax.axis_size(axis_name)
    received = [block]
    for offset in range(1, count):
        pairs = [((i + offset) % count, i) for i in range(count)]
        received.append(lax.ppermute(block, axis_name, pairs))
    return received


def neighbour_planes(block, axis_name):
    count = lax.axis_size(axis_name)
    if count == 2:
        return lax.ppermute(block, axis_name, [(0, 1), (1, 0)])
    padded = with_halo(block, ((axis_name, 1),), 1, False)
    return padded[:, :-2] + padded[:, 2:]


def mix(matrix, values):
    mixed_rows = []
    for out_var in range(values.shape[0]):
        summed = values[out_var]
        for in_var in range(values.shape[0]):
            summed = summed + matrix[out_var, in_var][None, None, :] * values[in_var]
        mixed_rows.append(summed)
    return jnp.stack(mixed_rows)


def per_device(
    flow_state,
    source,
    cell_az,
    cell_rad,
    visc_az,
    beta_az,
    visc_rad,
    axial_diff,
    mix_in,
    mix_mid,
    mix_out,
):
    rad_cells = flow_state.shape[3]
    nb = neighbour_planes(flow_state, "ax")
    it, ia, ib, red = az_sweep(flow_state, nb, source, cell_az, visc_az, beta_az, axial_diff, mix_in)
    red = gathered(red, "az")
    it, ia, ib, red = rad_sweep(it, ia, ib, red, mix_mid, cell_rad, visc_rad)
    red = gathered(red, "rad")
    return out_sweep(it, ia, ib, red, mix_out)


def solution(mesh):
    in_specs = (
        P(None, "ax", "az", "rad"),
        P(None, "ax", "az", "rad"),
        P("ax", "az", "rad"),
        P("ax", "az", "rad"),
        P(None, "rad"),
        P(None, "rad"),
        P(),
        P(None, "rad"),
        P(None, None, "rad"),
        P(None, None, "rad"),
        P(None, None, "rad"),
    )
    out_specs = P(None, "ax", "az", "rad")
    return jax.shard_map(
        per_device, mesh=mesh, in_specs=in_specs, out_specs=out_specs, check_vma=False
    )
```

```python
import jax
import jax.numpy as jnp
from jax import lax
from jax.experimental import pallas as pl
from jax.experimental.pallas import tpu as pltpu
from jax.sharding import PartitionSpec as P
import functools


def with_halo(block, sides, width, periodic):
    for axis, dim in sides:
        count = lax.axis_size(axis)
        forward = [(i, i + 1) for i in range(count - 1)]
        if periodic:
            forward.append((count - 1, 0))
        backward = [(target, source) for source, target in forward]
        low = lax.ppermute(
            lax.slice_in_dim(block, block.shape[dim] - width, None, axis=dim), axis, forward
        )
        high = lax.ppermute(lax.slice_in_dim(block, 0, width, axis=dim), axis, backward)
        block = jnp.concatenate([low, block, high], axis=dim)
    return block


def shifted(values, offset, axis, periodic):
    if periodic:
        return jnp.roll(values, offset, axis)
    length = values.shape[axis]
    zero_shape = list(values.shape)
    zero_shape[axis] = abs(offset)
    zeros = jnp.zeros(zero_shape, values.dtype)
    if offset > 0:
        kept = lax.slice_in_dim(values, 0, length - offset, axis=axis)
        return jnp.concatenate([zeros, kept], axis=axis)
    kept = lax.slice_in_dim(values, -offset, length, axis=axis)
    return jnp.concatenate([kept, zeros], axis=axis)


def cyclic_reduce(lower, upper, rhs, axis, periodic, steps_below):
    stride = 1
    while stride < steps_below:
        ll, ul = shifted(lower, stride, axis, periodic), shifted(upper, stride, axis, periodic)
        lr, ur = shifted(lower, -stride, axis, periodic), shifted(upper, -stride, axis, periodic)
        inv = 1.0 / (1.0 - lower * ul - upper * lr)
        rhs = [
            (r - lower * shifted(r, stride, axis, periodic) - upper * shifted(r, -stride, axis, periodic)) * inv
            for r in rhs
        ]
        lower, upper = -lower * ll * inv, -upper * ur * inv
        stride = stride * 2
    return lower, upper, rhs


def interior(lower, upper):
    length = lower.shape[0]
    idx = lax.broadcasted_iota(jnp.int32, lower.shape, 0)
    edge = (idx == 0) | (idx == length - 1)
    second = idx == 1
    penult = idx == length - 2
    zero = jnp.zeros_like(lower)
    il = jnp.where(edge | second, zero, lower)
    iu = jnp.where(edge | penult, zero, upper)
    return il, iu, jnp.where(edge, zero, 1.0), jnp.where(second, lower, zero), jnp.where(penult, upper, zero)


def pcr_levels(il, iu, rhs):
    length = il.shape[0]
    stride = 1
    while stride < length - 2:
        back = length - stride
        ll, ul = pltpu.roll(il, stride, 0), pltpu.roll(iu, stride, 0)
        lr, ur = pltpu.roll(il, back, 0), pltpu.roll(iu, back, 0)
        inv = 1.0 / (1.0 - il * ul - iu * lr)
        rhs = [(r - il * pltpu.roll(r, stride, 0) - iu * pltpu.roll(r, back, 0)) * inv for r in rhs]
        il, iu = -il * ll * inv, -iu * ur * inv
        stride = stride * 2
    return rhs


def interface_rows(lower, upper, t0, te, t1, t2, a1, b1, a2, b2):
    length = lower.shape[0]
    l0, u0 = lower[0:1], upper[0:1]
    le, ue = lower[length - 1 :], upper[length - 1 :]
    inv_f = 1.0 / (1.0 - u0 * a1)
    inv_e = 1.0 / (1.0 - le * b2)
    return (
        (l0 * inv_f, -le * a2 * inv_e),
        (-u0 * b1 * inv_f, ue * inv_e),
        ((t0 - u0 * t1) * inv_f, (te - le * t2) * inv_e),
    )


def reduce_block(lower, upper, target):
    length = lower.shape[0]
    il, iu, keep, a_init, b_init = interior(lower, upper)
    it, ia, ib = pcr_levels(il, iu, [target * keep, a_init, b_init])
    n2 = length - 2
    rows = interface_rows(
        lower, upper, target[0:1], target[length - 1 :], it[1:2], it[n2 : n2 + 1],
        ia[1:2], ib[1:2], ia[n2 : n2 + 1], ib[n2 : n2 + 1],
    )
    return it, ia, ib, rows


def store_rows(red_ref, v, rows):
    for q, pair in enumerate(rows):
        for i, value in enumerate(pair):
            red_ref[v, 0, q, i : i + 1, :] = value


def reduced_ends(red_refs, rows_ref, v):
    for k, ref in enumerate(red_refs):
        rows_ref[:, 2 * k : 2 * k + 2, :] = ref[v, 0]
    lower, upper, target = rows_ref[0], rows_ref[1], rows_ref[2]
    length = lower.shape[0]
    stride = 1
    while stride < length:
        back = length - stride
        ll, ul = pltpu.roll(lower, stride, 0), pltpu.roll(upper, stride, 0)
        lr, ur = pltpu.roll(lower, back, 0), pltpu.roll(upper, back, 0)
        inv = 1.0 / (1.0 - lower * ul - upper * lr)
        target = (target - lower * pltpu.roll(target, stride, 0) - upper * pltpu.roll(target, back, 0)) * inv
        lower, upper = -lower * ll * inv, -upper * ur * inv
        stride = stride * 2
    ends = target / (1.0 + lower + upper)
    return ends[0:1], ends[1:2]


def back_substitute(it, ia, ib, first, last):
    length = it.shape[0]
    idx = lax.broadcasted_iota(jnp.int32, it.shape, 0)
    inner = it - ia * first - ib * last
    return jnp.where(idx == 0, first, jnp.where(idx == length - 1, last, inner))


def mixed(mix_ref, values):
    out = []
    for v in range(len(values)):
        summed = values[v]
        for w in range(len(values)):
            summed = summed + mix_ref[v, w : w + 1, :] * values[w]
        out.append(summed)
    return out


def az_coefficients(cell, visc_ref, beta_ref, v):
    coupling = visc_ref[v : v + 1, :] * cell
    centre = 1.0 + 2.0 * coupling
    tilt = beta_ref[v : v + 1, :]
    lower = -coupling * (1.0 + tilt) / centre
    upper = -coupling * (1.0 - tilt) / centre
    return lower, upper, centre


def az_local_kernel(fs_ref, src_ref, cell_ref, visc_ref, beta_ref, diff_ref, mix_ref, ot_ref, oa_ref, ob_ref, edge_ref):
    count = fs_ref.shape[0]
    explicit = [src_ref[w, 0] + diff_ref[w : w + 1, :] * (-2.0 * fs_ref[w, 0]) for w in range(count)]
    section_one = mixed(mix_ref, explicit)
    cell = cell_ref[0]
    for v in range(count):
        lower, upper, centre = az_coefficients(cell, visc_ref, beta_ref, v)
        target = section_one[v] / centre
        length = lower.shape[0]
        il, iu, keep, a_init, b_init = interior(lower, upper)
        it, ia, ib = pcr_levels(il, iu, [target * keep, a_init, b_init])
        ot_ref[v, 0] = it
        oa_ref[v, 0] = ia
        ob_ref[v, 0] = ib
        n2 = length - 2
        for k, value in enumerate(
            (target[0:1], target[length - 1 :], ia[1:2], ib[1:2], ia[n2 : n2 + 1], ib[n2 : n2 + 1])
        ):
            edge_ref[v, 0, k : k + 1, :] = value


def az_plane_kernel(nb_ref, cell_ref, visc_ref, beta_ref, diff_ref, mix_ref, it_in_ref, edge_ref, order_ref, ot_ref, red_ref):
    count = nb_ref.shape[0]
    explicit = [diff_ref[w : w + 1, :] * nb_ref[w, 0] for w in range(count)]
    section_one = mixed(mix_ref, explicit)
    cell = cell_ref[0]
    for v in range(count):
        lower, upper, centre = az_coefficients(cell, visc_ref, beta_ref, v)
        target = section_one[v] / centre
        length = lower.shape[0]
        il, iu, keep, _, _ = interior(lower, upper)
        (it,) = pcr_levels(il, iu, [target * keep])
        it = it_in_ref[v, 0] + it
        ot_ref[v, 0] = it
        edge = edge_ref[v, 0]
        n2 = length - 2
        rows = interface_rows(
            lower, upper, edge[0:1] + target[0:1], edge[1:2] + target[length - 1 :], it[1:2], it[n2 : n2 + 1],
            edge[2:3], edge[3:4], edge[4:5], edge[5:6],
        )
        store_rows(red_ref, v, rows)


def rad_side(cell, visc, v):
    coupling = visc[v : v + 1, :] * cell
    centre = 1.0 + 2.0 * coupling
    return -coupling / centre, centre


def local_visc(visc_ref, axis_name, cells):
    place = lax.axis_index(axis_name)
    return visc_ref[:, pl.ds(pl.multiple_of(place * cells, cells), cells)]


def rad_pre_kernel(cell_ref, visc_ref, oa_ref, ob_ref, edge_ref, *, axis_name):
    count = oa_ref.shape[0]
    cells = cell_ref.shape[2]
    visc = local_visc(visc_ref, axis_name, cells)
    cell = cell_ref[0]
    for v in range(count):
        side, _ = rad_side(cell, visc, v)
        side = side.T
        length = side.shape[0]
        il, iu, _, a_init, b_init = interior(side, side)
        ia, ib = pcr_levels(il, iu, [a_init, b_init])
        oa_ref[v, 0] = ia
        ob_ref[v, 0] = ib
        n2 = length - 2
        for k, value in enumerate((ia[1:2], ib[1:2], ia[n2 : n2 + 1], ib[n2 : n2 + 1])):
            edge_ref[v, 0, k : k + 1, :] = value


def rad_kernel(*refs, axis_name, devices, pieces):
    it_ref, ia_ref, ib_ref = refs[:3]
    red_in = refs[3 : 3 + pieces]
    mix_ref, cell_ref, visc_ref, edge_ref, ot_ref, red_ref, rows_ref = refs[3 + pieces :]
    count = it_ref.shape[0]
    cells = it_ref.shape[3]
    place = lax.axis_index(axis_name)
    visc = local_visc(visc_ref, axis_name, cells)
    solved = []
    for w in range(count):
        first, last = reduced_ends(red_in, rows_ref, w)
        solved.append(back_substitute(it_ref[w, 0], ia_ref[w, 0], ib_ref[w, 0], first, last))
    section_three = mixed(mix_ref, solved)
    cell = cell_ref[0]
    for v in range(count):
        side, centre = rad_side(cell, visc, v)
        side = side.T
        target = (section_three[v] / centre).T
        length = side.shape[0]
        il, iu, keep, _, _ = interior(side, side)
        (it,) = pcr_levels(il, iu, [target * keep])
        edge = edge_ref[v, 0]
        n2 = length - 2
        (lf, le), (uf, ue), trow = interface_rows(
            side, side, target[0:1], target[length - 1 :], it[1:2], it[n2 : n2 + 1],
            edge[0:1], edge[1:2], edge[2:3], edge[3:4],
        )
        lf = jnp.where(place == 0, jnp.zeros_like(lf), lf)
        ue = jnp.where(place == devices - 1, jnp.zeros_like(ue), ue)
        store_rows(red_ref, v, ((lf, le), (uf, ue), trow))
        ot_ref[v, 0] = it


def out_kernel(*refs, pieces):
    it_ref, ia_ref, ib_ref = refs[:3]
    red_in = refs[3 : 3 + pieces]
    mix_ref, out_ref, rows_ref = refs[3 + pieces :]
    count = it_ref.shape[0]
    solved = []
    for w in range(count):
        first, last = reduced_ends(red_in, rows_ref, w)
        solved.append(back_substitute(it_ref[w, 0], ia_ref[w, 0], ib_ref[w, 0], first, last).T)
    for v, value in enumerate(mixed(mix_ref, solved)):
        out_ref[v, 0] = value


def az_sweep(flow_state, nb, source, cell_az, visc_az, beta_az, axial_diff, mix_in, order):
    nv, nz, na, nr = flow_state.shape
    chunk = 128 if nr % 128 == 0 else nr
    grid = (nz, nr // chunk)
    big = pl.BlockSpec((nv, 1, na, chunk), lambda z, c: (0, z, 0, c))
    cell = pl.BlockSpec((1, na, chunk), lambda z, c: (z, 0, c))
    par = pl.BlockSpec((nv, chunk), lambda z, c: (0, c))
    mixs = pl.BlockSpec((nv, nv, chunk), lambda z, c: (0, 0, c))
    edge = pl.BlockSpec((nv, 1, 6, chunk), lambda z, c: (0, z, 0, c))
    red = pl.BlockSpec((nv, 1, 3, 2, chunk), lambda z, c: (0, z, 0, 0, c))
    out = jax.ShapeDtypeStruct(flow_state.shape, flow_state.dtype)
    it, ia, ib, edges = pl.pallas_call(
        az_local_kernel,
        grid=grid,
        in_specs=[big, big, cell, par, par, par, mixs],
        out_specs=[big, big, big, edge],
        out_shape=[out, out, out, jax.ShapeDtypeStruct((nv, nz, 6, nr), flow_state.dtype)],
    )(flow_state, source, cell_az, visc_az, beta_az, axial_diff, mix_in)
    it, red = pl.pallas_call(
        az_plane_kernel,
        grid=grid,
        in_specs=[big, cell, par, par, par, mixs, big, edge, pl.BlockSpec(memory_space=pl.ANY)],
        out_specs=[big, red],
        out_shape=[out, jax.ShapeDtypeStruct((nv, nz, 3, 2, nr), flow_state.dtype)],
        input_output_aliases={6: 0},
    )(nb, cell_az, visc_az, beta_az, axial_diff, mix_in, it, edges, order)
    return it, ia, ib, red


def rad_pre(cell_rad, visc_rad, nv):
    nz, na, nr = cell_rad.shape
    big_t = pl.BlockSpec((nv, 1, nr, na), lambda z: (0, z, 0, 0))
    cell = pl.BlockSpec((1, na, nr), lambda z: (z, 0, 0))
    par = pl.BlockSpec(visc_rad.shape, lambda z: (0, 0))
    edge = pl.BlockSpec((nv, 1, 4, na), lambda z: (0, z, 0, 0))
    out = jax.ShapeDtypeStruct((nv, nz, nr, na), cell_rad.dtype)
    return pl.pallas_call(
        functools.partial(rad_pre_kernel, axis_name="rad"),
        grid=(nz,),
        in_specs=[cell, par],
        out_specs=[big_t, big_t, edge],
        out_shape=[out, out, jax.ShapeDtypeStruct((nv, nz, 4, na), cell_rad.dtype)],
    )(cell_rad, visc_rad)


def rad_sweep(it, ia, ib, red_in, mix_mid, cell_rad, visc_rad, edges):
    nv, nz, na, nr = it.shape
    big = pl.BlockSpec((nv, 1, na, nr), lambda z: (0, z, 0, 0))
    big_t = pl.BlockSpec((nv, 1, nr, na), lambda z: (0, z, 0, 0))
    red_in_spec = pl.BlockSpec((nv, 1) + red_in[0].shape[2:], lambda z: (0, z, 0, 0, 0))
    mixs = pl.BlockSpec((nv, nv, nr), lambda z: (0, 0, 0))
    cell = pl.BlockSpec((1, na, nr), lambda z: (z, 0, 0))
    par = pl.BlockSpec(visc_rad.shape, lambda z: (0, 0))
    edge = pl.BlockSpec((nv, 1, 4, na), lambda z: (0, z, 0, 0))
    red = pl.BlockSpec((nv, 1, 3, 2, na), lambda z: (0, z, 0, 0, 0))
    out = jax.ShapeDtypeStruct((nv, nz, nr, na), it.dtype)
    pieces = len(red_in)
    kernel = functools.partial(rad_kernel, axis_name="rad", devices=lax.axis_size("rad"), pieces=pieces)
    return pl.pallas_call(
        kernel,
        grid=(nz,),
        in_specs=[big, big, big] + [red_in_spec] * pieces + [mixs, cell, par, edge],
        out_specs=[big_t, red],
        out_shape=[out, jax.ShapeDtypeStruct((nv, nz, 3, 2, na), it.dtype)],
        scratch_shapes=[pltpu.VMEM((3, 2 * pieces, nr), it.dtype)],
    )(it, ia, ib, *red_in, mix_mid, cell_rad, visc_rad, edges)


def out_sweep(it, ia, ib, red_in, mix_out):
    nv, nz, nr, na = it.shape
    big_t = pl.BlockSpec((nv, 1, nr, na), lambda z: (0, z, 0, 0))
    big = pl.BlockSpec((nv, 1, na, nr), lambda z: (0, z, 0, 0))
    red_in_spec = pl.BlockSpec((nv, 1) + red_in[0].shape[2:], lambda z: (0, z, 0, 0, 0))
    mixs = pl.BlockSpec((nv, nv, nr), lambda z: (0, 0, 0))
    pieces = len(red_in)
    return pl.pallas_call(
        functools.partial(out_kernel, pieces=pieces),
        grid=(nz,),
        in_specs=[big_t, big_t, big_t] + [red_in_spec] * pieces + [mixs],
        out_specs=big,
        out_shape=jax.ShapeDtypeStruct((nv, nz, na, nr), it.dtype),
        scratch_shapes=[pltpu.VMEM((3, 2 * pieces, na), it.dtype)],
    )(it, ia, ib, *red_in, mix_out)


def gathered(block, axis_name):
    count = lax.axis_size(axis_name)
    received = [block]
    for offset in range(1, count):
        pairs = [((i + offset) % count, i) for i in range(count)]
        received.append(lax.ppermute(block, axis_name, pairs))
    return received


def neighbour_planes(block, axis_name):
    count = lax.axis_size(axis_name)
    if count == 2:
        return lax.ppermute(block, axis_name, [(0, 1), (1, 0)])
    padded = with_halo(block, ((axis_name, 1),), 1, False)
    return padded[:, :-2] + padded[:, 2:]


def mix(matrix, values):
    mixed_rows = []
    for out_var in range(values.shape[0]):
        summed = values[out_var]
        for in_var in range(values.shape[0]):
            summed = summed + matrix[out_var, in_var][None, None, :] * values[in_var]
        mixed_rows.append(summed)
    return jnp.stack(mixed_rows)


def per_device(
    flow_state,
    source,
    cell_az,
    cell_rad,
    visc_az,
    beta_az,
    visc_rad,
    axial_diff,
    mix_in,
    mix_mid,
    mix_out,
):
    rad_cells = flow_state.shape[3]
    nb = neighbour_planes(flow_state, "ax")
    rad_a, rad_b, rad_edges = rad_pre(cell_rad, visc_rad, flow_state.shape[0])
    it, ia, ib, red = az_sweep(flow_state, nb, source, cell_az, visc_az, beta_az, axial_diff, mix_in, rad_edges)
    red = gathered(red, "az")
    it, red = rad_sweep(it, ia, ib, red, mix_mid, cell_rad, visc_rad, rad_edges)
    ia, ib = rad_a, rad_b
    red = gathered(red, "rad")
    return out_sweep(it, ia, ib, red, mix_out)


def solution(mesh):
    in_specs = (
        P(None, "ax", "az", "rad"),
        P(None, "ax", "az", "rad"),
        P("ax", "az", "rad"),
        P("ax", "az", "rad"),
        P(None, "rad"),
        P(None, "rad"),
        P(),
        P(None, "rad"),
        P(None, None, "rad"),
        P(None, None, "rad"),
        P(None, None, "rad"),
    )
    out_specs = P(None, "ax", "az", "rad")
    return jax.shard_map(
        per_device, mesh=mesh, in_specs=in_specs, out_specs=out_specs, check_vma=False
    )
```

```python
import jax
import jax.numpy as jnp
from jax import lax
from jax.experimental import pallas as pl
from jax.experimental.pallas import tpu as pltpu
from jax.sharding import PartitionSpec as P
import functools


def with_halo(block, sides, width, periodic):
    for axis, dim in sides:
        count = lax.axis_size(axis)
        forward = [(i, i + 1) for i in range(count - 1)]
        if periodic:
            forward.append((count - 1, 0))
        backward = [(target, source) for source, target in forward]
        low = lax.ppermute(
            lax.slice_in_dim(block, block.shape[dim] - width, None, axis=dim), axis, forward
        )
        high = lax.ppermute(lax.slice_in_dim(block, 0, width, axis=dim), axis, backward)
        block = jnp.concatenate([low, block, high], axis=dim)
    return block


def shifted(values, offset, axis, periodic):
    if periodic:
        return jnp.roll(values, offset, axis)
    length = values.shape[axis]
    zero_shape = list(values.shape)
    zero_shape[axis] = abs(offset)
    zeros = jnp.zeros(zero_shape, values.dtype)
    if offset > 0:
        kept = lax.slice_in_dim(values, 0, length - offset, axis=axis)
        return jnp.concatenate([zeros, kept], axis=axis)
    kept = lax.slice_in_dim(values, -offset, length, axis=axis)
    return jnp.concatenate([kept, zeros], axis=axis)


def cyclic_reduce(lower, upper, rhs, axis, periodic, steps_below):
    stride = 1
    while stride < steps_below:
        ll, ul = shifted(lower, stride, axis, periodic), shifted(upper, stride, axis, periodic)
        lr, ur = shifted(lower, -stride, axis, periodic), shifted(upper, -stride, axis, periodic)
        inv = 1.0 / (1.0 - lower * ul - upper * lr)
        rhs = [
            (r - lower * shifted(r, stride, axis, periodic) - upper * shifted(r, -stride, axis, periodic)) * inv
            for r in rhs
        ]
        lower, upper = -lower * ll * inv, -upper * ur * inv
        stride = stride * 2
    return lower, upper, rhs


def interior(lower, upper):
    length = lower.shape[0]
    idx = lax.broadcasted_iota(jnp.int32, lower.shape, 0)
    edge = (idx == 0) | (idx == length - 1)
    second = idx == 1
    penult = idx == length - 2
    zero = jnp.zeros_like(lower)
    il = jnp.where(edge | second, zero, lower)
    iu = jnp.where(edge | penult, zero, upper)
    return il, iu, jnp.where(edge, zero, 1.0), jnp.where(second, lower, zero), jnp.where(penult, upper, zero)


def pcr_levels(il, iu, rhs):
    length = il.shape[0]
    stride = 1
    while stride < length - 2:
        back = length - stride
        ll, ul = pltpu.roll(il, stride, 0), pltpu.roll(iu, stride, 0)
        lr, ur = pltpu.roll(il, back, 0), pltpu.roll(iu, back, 0)
        inv = 1.0 / (1.0 - il * ul - iu * lr)
        rhs = [(r - il * pltpu.roll(r, stride, 0) - iu * pltpu.roll(r, back, 0)) * inv for r in rhs]
        flip = -inv
        il, iu = il * ll * flip, iu * ur * flip
        stride = stride * 2
    return rhs


def interface_rows(lower, upper, t0, te, t1, t2, a1, b1, a2, b2):
    length = lower.shape[0]
    l0, u0 = lower[0:1], upper[0:1]
    le, ue = lower[length - 1 :], upper[length - 1 :]
    inv_f = 1.0 / (1.0 - u0 * a1)
    inv_e = 1.0 / (1.0 - le * b2)
    return (
        (l0 * inv_f, -le * a2 * inv_e),
        (-u0 * b1 * inv_f, ue * inv_e),
        ((t0 - u0 * t1) * inv_f, (te - le * t2) * inv_e),
    )


def reduce_block(lower, upper, target):
    length = lower.shape[0]
    il, iu, keep, a_init, b_init = interior(lower, upper)
    it, ia, ib = pcr_levels(il, iu, [target * keep, a_init, b_init])
    n2 = length - 2
    rows = interface_rows(
        lower, upper, target[0:1], target[length - 1 :], it[1:2], it[n2 : n2 + 1],
        ia[1:2], ib[1:2], ia[n2 : n2 + 1], ib[n2 : n2 + 1],
    )
    return it, ia, ib, rows


def store_rows(red_ref, v, rows):
    for q, pair in enumerate(rows):
        for i, value in enumerate(pair):
            red_ref[v, 0, q, i : i + 1, :] = value


def reduced_ends(red_refs, rows_ref, v):
    for k, ref in enumerate(red_refs):
        rows_ref[:, 2 * k : 2 * k + 2, :] = ref[v, 0]
    lower, upper, target = rows_ref[0], rows_ref[1], rows_ref[2]
    length = lower.shape[0]
    stride = 1
    while stride < length:
        back = length - stride
        ll, ul = pltpu.roll(lower, stride, 0), pltpu.roll(upper, stride, 0)
        lr, ur = pltpu.roll(lower, back, 0), pltpu.roll(upper, back, 0)
        inv = 1.0 / (1.0 - lower * ul - upper * lr)
        target = (target - lower * pltpu.roll(target, stride, 0) - upper * pltpu.roll(target, back, 0)) * inv
        lower, upper = -lower * ll * inv, -upper * ur * inv
        stride = stride * 2
    ends = target / (1.0 + lower + upper)
    return ends[0:1], ends[1:2]


def back_substitute(it, ia, ib, first, last):
    length = it.shape[0]
    idx = lax.broadcasted_iota(jnp.int32, it.shape, 0)
    inner = it - ia * first - ib * last
    return jnp.where(idx == 0, first, jnp.where(idx == length - 1, last, inner))


def mixed(mix_ref, values):
    out = []
    for v in range(len(values)):
        summed = values[v]
        for w in range(len(values)):
            summed = summed + mix_ref[v, w : w + 1, :] * values[w]
        out.append(summed)
    return out


def az_coefficients(cell, visc_ref, beta_ref, v):
    coupling = visc_ref[v : v + 1, :] * cell
    scale = -1.0 / (1.0 + 2.0 * coupling)
    tilt = beta_ref[v : v + 1, :]
    lower = coupling * (1.0 + tilt) * scale
    upper = coupling * (1.0 - tilt) * scale
    return lower, upper, scale


def az_local_kernel(fs_ref, src_ref, cell_ref, visc_ref, beta_ref, diff_ref, mix_ref, ot_ref, oa_ref, ob_ref, edge_ref):
    count = fs_ref.shape[0]
    explicit = [src_ref[w, 0] + diff_ref[w : w + 1, :] * (-2.0 * fs_ref[w, 0]) for w in range(count)]
    section_one = mixed(mix_ref, explicit)
    cell = cell_ref[0]
    for v in range(count):
        lower, upper, scale = az_coefficients(cell, visc_ref, beta_ref, v)
        target = section_one[v] * -scale
        length = lower.shape[0]
        il, iu, keep, a_init, b_init = interior(lower, upper)
        it, ia, ib = pcr_levels(il, iu, [target * keep, a_init, b_init])
        ot_ref[v, 0] = it
        oa_ref[v, 0] = ia
        ob_ref[v, 0] = ib
        n2 = length - 2
        for k, value in enumerate(
            (target[0:1], target[length - 1 :], ia[1:2], ib[1:2], ia[n2 : n2 + 1], ib[n2 : n2 + 1])
        ):
            edge_ref[v, 0, k : k + 1, :] = value


def az_plane_kernel(nb_ref, cell_ref, visc_ref, beta_ref, diff_ref, mix_ref, it_in_ref, edge_ref, order_ref, ot_ref, red_ref):
    count = nb_ref.shape[0]
    explicit = [diff_ref[w : w + 1, :] * nb_ref[w, 0] for w in range(count)]
    section_one = mixed(mix_ref, explicit)
    cell = cell_ref[0]
    for v in range(count):
        lower, upper, scale = az_coefficients(cell, visc_ref, beta_ref, v)
        target = section_one[v] * -scale
        length = lower.shape[0]
        il, iu, keep, _, _ = interior(lower, upper)
        (it,) = pcr_levels(il, iu, [target * keep])
        it = it_in_ref[v, 0] + it
        ot_ref[v, 0] = it
        edge = edge_ref[v, 0]
        n2 = length - 2
        rows = interface_rows(
            lower, upper, edge[0:1] + target[0:1], edge[1:2] + target[length - 1 :], it[1:2], it[n2 : n2 + 1],
            edge[2:3], edge[3:4], edge[4:5], edge[5:6],
        )
        store_rows(red_ref, v, rows)


def rad_side(cell, visc, v):
    coupling = visc[v : v + 1, :] * cell
    scale = 1.0 / (1.0 + 2.0 * coupling)
    return -coupling * scale, scale


def local_visc(visc_ref, axis_name, cells):
    place = lax.axis_index(axis_name)
    return visc_ref[:, pl.ds(pl.multiple_of(place * cells, cells), cells)]


def rad_pre_kernel(cell_ref, visc_ref, oa_ref, ob_ref, edge_ref, *, axis_name):
    count = oa_ref.shape[0]
    cells = cell_ref.shape[2]
    visc = local_visc(visc_ref, axis_name, cells)
    cell = cell_ref[0]
    for v in range(count):
        side, _ = rad_side(cell, visc, v)
        side = side.T
        length = side.shape[0]
        il, iu, _, a_init, b_init = interior(side, side)
        ia, ib = pcr_levels(il, iu, [a_init, b_init])
        oa_ref[v, 0] = ia
        ob_ref[v, 0] = ib
        n2 = length - 2
        for k, value in enumerate((ia[1:2], ib[1:2], ia[n2 : n2 + 1], ib[n2 : n2 + 1])):
            edge_ref[v, 0, k : k + 1, :] = value


def rad_kernel(*refs, axis_name, devices, pieces):
    it_ref, ia_ref, ib_ref = refs[:3]
    red_in = refs[3 : 3 + pieces]
    mix_ref, cell_ref, visc_ref, edge_ref, ot_ref, red_ref, rows_ref = refs[3 + pieces :]
    count = it_ref.shape[0]
    cells = it_ref.shape[3]
    place = lax.axis_index(axis_name)
    visc = local_visc(visc_ref, axis_name, cells)
    solved = []
    for w in range(count):
        first, last = reduced_ends(red_in, rows_ref, w)
        solved.append(back_substitute(it_ref[w, 0], ia_ref[w, 0], ib_ref[w, 0], first, last))
    section_three = mixed(mix_ref, solved)
    cell = cell_ref[0]
    for v in range(count):
        side, scale = rad_side(cell, visc, v)
        side = side.T
        target = (section_three[v] * scale).T
        length = side.shape[0]
        il, iu, keep, _, _ = interior(side, side)
        (it,) = pcr_levels(il, iu, [target * keep])
        edge = edge_ref[v, 0]
        n2 = length - 2
        (lf, le), (uf, ue), trow = interface_rows(
            side, side, target[0:1], target[length - 1 :], it[1:2], it[n2 : n2 + 1],
            edge[0:1], edge[1:2], edge[2:3], edge[3:4],
        )
        lf = jnp.where(place == 0, jnp.zeros_like(lf), lf)
        ue = jnp.where(place == devices - 1, jnp.zeros_like(ue), ue)
        store_rows(red_ref, v, ((lf, le), (uf, ue), trow))
        ot_ref[v, 0] = it


def out_kernel(*refs, pieces):
    it_ref, ia_ref, ib_ref = refs[:3]
    red_in = refs[3 : 3 + pieces]
    mix_ref, out_ref, rows_ref = refs[3 + pieces :]
    count = it_ref.shape[0]
    solved = []
    for w in range(count):
        first, last = reduced_ends(red_in, rows_ref, w)
        solved.append(back_substitute(it_ref[w, 0], ia_ref[w, 0], ib_ref[w, 0], first, last).T)
    for v, value in enumerate(mixed(mix_ref, solved)):
        out_ref[v, 0] = value


def az_sweep(flow_state, nb, source, cell_az, visc_az, beta_az, axial_diff, mix_in, order):
    nv, nz, na, nr = flow_state.shape
    chunk = 128 if nr % 128 == 0 else nr
    grid = (nz, nr // chunk)
    big = pl.BlockSpec((nv, 1, na, chunk), lambda z, c: (0, z, 0, c))
    cell = pl.BlockSpec((1, na, chunk), lambda z, c: (z, 0, c))
    par = pl.BlockSpec((nv, chunk), lambda z, c: (0, c))
    mixs = pl.BlockSpec((nv, nv, chunk), lambda z, c: (0, 0, c))
    edge = pl.BlockSpec((nv, 1, 6, chunk), lambda z, c: (0, z, 0, c))
    red = pl.BlockSpec((nv, 1, 3, 2, chunk), lambda z, c: (0, z, 0, 0, c))
    out = jax.ShapeDtypeStruct(flow_state.shape, flow_state.dtype)
    it, ia, ib, edges = pl.pallas_call(
        az_local_kernel,
        grid=grid,
        in_specs=[big, big, cell, par, par, par, mixs],
        out_specs=[big, big, big, edge],
        out_shape=[out, out, out, jax.ShapeDtypeStruct((nv, nz, 6, nr), flow_state.dtype)],
    )(flow_state, source, cell_az, visc_az, beta_az, axial_diff, mix_in)
    it, red = pl.pallas_call(
        az_plane_kernel,
        grid=grid,
        in_specs=[big, cell, par, par, par, mixs, big, edge, pl.BlockSpec(memory_space=pl.ANY)],
        out_specs=[big, red],
        out_shape=[out, jax.ShapeDtypeStruct((nv, nz, 3, 2, nr), flow_state.dtype)],
        input_output_aliases={6: 0},
    )(nb, cell_az, visc_az, beta_az, axial_diff, mix_in, it, edges, order)
    return it, ia, ib, red


def rad_pre(cell_rad, visc_rad, nv):
    nz, na, nr = cell_rad.shape
    big_t = pl.BlockSpec((nv, 1, nr, na), lambda z: (0, z, 0, 0))
    cell = pl.BlockSpec((1, na, nr), lambda z: (z, 0, 0))
    par = pl.BlockSpec(visc_rad.shape, lambda z: (0, 0))
    edge = pl.BlockSpec((nv, 1, 4, na), lambda z: (0, z, 0, 0))
    out = jax.ShapeDtypeStruct((nv, nz, nr, na), cell_rad.dtype)
    return pl.pallas_call(
        functools.partial(rad_pre_kernel, axis_name="rad"),
        grid=(nz,),
        in_specs=[cell, par],
        out_specs=[big_t, big_t, edge],
        out_shape=[out, out, jax.ShapeDtypeStruct((nv, nz, 4, na), cell_rad.dtype)],
    )(cell_rad, visc_rad)


def rad_sweep(it, ia, ib, red_in, mix_mid, cell_rad, visc_rad, edges):
    nv, nz, na, nr = it.shape
    big = pl.BlockSpec((nv, 1, na, nr), lambda z: (0, z, 0, 0))
    big_t = pl.BlockSpec((nv, 1, nr, na), lambda z: (0, z, 0, 0))
    red_in_spec = pl.BlockSpec((nv, 1) + red_in[0].shape[2:], lambda z: (0, z, 0, 0, 0))
    mixs = pl.BlockSpec((nv, nv, nr), lambda z: (0, 0, 0))
    cell = pl.BlockSpec((1, na, nr), lambda z: (z, 0, 0))
    par = pl.BlockSpec(visc_rad.shape, lambda z: (0, 0))
    edge = pl.BlockSpec((nv, 1, 4, na), lambda z: (0, z, 0, 0))
    red = pl.BlockSpec((nv, 1, 3, 2, na), lambda z: (0, z, 0, 0, 0))
    out = jax.ShapeDtypeStruct((nv, nz, nr, na), it.dtype)
    pieces = len(red_in)
    kernel = functools.partial(rad_kernel, axis_name="rad", devices=lax.axis_size("rad"), pieces=pieces)
    return pl.pallas_call(
        kernel,
        grid=(nz,),
        in_specs=[big, big, big] + [red_in_spec] * pieces + [mixs, cell, par, edge],
        out_specs=[big_t, red],
        out_shape=[out, jax.ShapeDtypeStruct((nv, nz, 3, 2, na), it.dtype)],
        scratch_shapes=[pltpu.VMEM((3, 2 * pieces, nr), it.dtype)],
    )(it, ia, ib, *red_in, mix_mid, cell_rad, visc_rad, edges)


def out_sweep(it, ia, ib, red_in, mix_out):
    nv, nz, nr, na = it.shape
    big_t = pl.BlockSpec((nv, 1, nr, na), lambda z: (0, z, 0, 0))
    big = pl.BlockSpec((nv, 1, na, nr), lambda z: (0, z, 0, 0))
    red_in_spec = pl.BlockSpec((nv, 1) + red_in[0].shape[2:], lambda z: (0, z, 0, 0, 0))
    mixs = pl.BlockSpec((nv, nv, nr), lambda z: (0, 0, 0))
    pieces = len(red_in)
    return pl.pallas_call(
        functools.partial(out_kernel, pieces=pieces),
        grid=(nz,),
        in_specs=[big_t, big_t, big_t] + [red_in_spec] * pieces + [mixs],
        out_specs=big,
        out_shape=jax.ShapeDtypeStruct((nv, nz, na, nr), it.dtype),
        scratch_shapes=[pltpu.VMEM((3, 2 * pieces, na), it.dtype)],
    )(it, ia, ib, *red_in, mix_out)


def gathered(block, axis_name):
    count = lax.axis_size(axis_name)
    received = [block]
    for offset in range(1, count):
        pairs = [((i + offset) % count, i) for i in range(count)]
        received.append(lax.ppermute(block, axis_name, pairs))
    return received


def neighbour_planes(block, axis_name):
    count = lax.axis_size(axis_name)
    if count == 2:
        return lax.ppermute(block, axis_name, [(0, 1), (1, 0)])
    padded = with_halo(block, ((axis_name, 1),), 1, False)
    return padded[:, :-2] + padded[:, 2:]


def mix(matrix, values):
    mixed_rows = []
    for out_var in range(values.shape[0]):
        summed = values[out_var]
        for in_var in range(values.shape[0]):
            summed = summed + matrix[out_var, in_var][None, None, :] * values[in_var]
        mixed_rows.append(summed)
    return jnp.stack(mixed_rows)


def per_device(
    flow_state,
    source,
    cell_az,
    cell_rad,
    visc_az,
    beta_az,
    visc_rad,
    axial_diff,
    mix_in,
    mix_mid,
    mix_out,
):
    rad_cells = flow_state.shape[3]
    nb = neighbour_planes(flow_state, "ax")
    rad_a, rad_b, rad_edges = rad_pre(cell_rad, visc_rad, flow_state.shape[0])
    it, ia, ib, red = az_sweep(flow_state, nb, source, cell_az, visc_az, beta_az, axial_diff, mix_in, rad_edges)
    red = gathered(red, "az")
    it, red = rad_sweep(it, ia, ib, red, mix_mid, cell_rad, visc_rad, rad_edges)
    ia, ib = rad_a, rad_b
    red = gathered(red, "rad")
    return out_sweep(it, ia, ib, red, mix_out)


def solution(mesh):
    in_specs = (
        P(None, "ax", "az", "rad"),
        P(None, "ax", "az", "rad"),
        P("ax", "az", "rad"),
        P("ax", "az", "rad"),
        P(None, "rad"),
        P(None, "rad"),
        P(),
        P(None, "rad"),
        P(None, None, "rad"),
        P(None, None, "rad"),
        P(None, None, "rad"),
    )
    out_specs = P(None, "ax", "az", "rad")
    return jax.shard_map(
        per_device, mesh=mesh, in_specs=in_specs, out_specs=out_specs, check_vma=False
    )
```

```python
import jax
import jax.numpy as jnp
from jax import lax
from jax.experimental import pallas as pl
from jax.experimental.pallas import tpu as pltpu
from jax.sharding import PartitionSpec as P
import functools


def with_halo(block, sides, width, periodic):
    for axis, dim in sides:
        count = lax.axis_size(axis)
        forward = [(i, i + 1) for i in range(count - 1)]
        if periodic:
            forward.append((count - 1, 0))
        backward = [(target, source) for source, target in forward]
        low = lax.ppermute(
            lax.slice_in_dim(block, block.shape[dim] - width, None, axis=dim), axis, forward
        )
        high = lax.ppermute(lax.slice_in_dim(block, 0, width, axis=dim), axis, backward)
        block = jnp.concatenate([low, block, high], axis=dim)
    return block


def shifted(values, offset, axis, periodic):
    if periodic:
        return jnp.roll(values, offset, axis)
    length = values.shape[axis]
    zero_shape = list(values.shape)
    zero_shape[axis] = abs(offset)
    zeros = jnp.zeros(zero_shape, values.dtype)
    if offset > 0:
        kept = lax.slice_in_dim(values, 0, length - offset, axis=axis)
        return jnp.concatenate([zeros, kept], axis=axis)
    kept = lax.slice_in_dim(values, -offset, length, axis=axis)
    return jnp.concatenate([kept, zeros], axis=axis)


def cyclic_reduce(lower, upper, rhs, axis, periodic, steps_below):
    stride = 1
    while stride < steps_below:
        ll, ul = shifted(lower, stride, axis, periodic), shifted(upper, stride, axis, periodic)
        lr, ur = shifted(lower, -stride, axis, periodic), shifted(upper, -stride, axis, periodic)
        inv = 1.0 / (1.0 - lower * ul - upper * lr)
        rhs = [
            (r - lower * shifted(r, stride, axis, periodic) - upper * shifted(r, -stride, axis, periodic)) * inv
            for r in rhs
        ]
        lower, upper = -lower * ll * inv, -upper * ur * inv
        stride = stride * 2
    return lower, upper, rhs


def interior(lower, upper, block):
    idx = lax.broadcasted_iota(jnp.int32, lower.shape, 0) % block
    edge = (idx == 0) | (idx == block - 1)
    second = idx == 1
    penult = idx == block - 2
    zero = jnp.zeros_like(lower)
    il = jnp.where(edge | second, zero, lower)
    iu = jnp.where(edge | penult, zero, upper)
    return il, iu, jnp.where(edge, zero, 1.0), jnp.where(second, lower, zero), jnp.where(penult, upper, zero)


def pcr_levels(il, iu, rhs, block):
    length = il.shape[0]
    stride = 1
    while stride < block - 2:
        back = length - stride
        ll, ul = pltpu.roll(il, stride, 0), pltpu.roll(iu, stride, 0)
        lr, ur = pltpu.roll(il, back, 0), pltpu.roll(iu, back, 0)
        inv = 1.0 / (1.0 - il * ul - iu * lr)
        rhs = [(r - il * pltpu.roll(r, stride, 0) - iu * pltpu.roll(r, back, 0)) * inv for r in rhs]
        flip = -inv
        il, iu = il * ll * flip, iu * ur * flip
        stride = stride * 2
    return rhs


def interface_rows(l0, u0, le, ue, t0, te, t1, t2, a1, b1, a2, b2):
    inv_f = 1.0 / (1.0 - u0 * a1)
    inv_e = 1.0 / (1.0 - le * b2)
    return (
        (l0 * inv_f, -le * a2 * inv_e),
        (-u0 * b1 * inv_f, ue * inv_e),
        ((t0 - u0 * t1) * inv_f, (te - le * t2) * inv_e),
    )


def picked(values, block, offset):
    return [values[k + offset : k + offset + 1] for k in range(0, values.shape[0], block)]


def edge_rows(target, ia, ib, block):
    return [
        picked(target, block, 0), picked(target, block, block - 1),
        picked(ia, block, 1), picked(ib, block, 1), picked(ia, block, block - 2), picked(ib, block, block - 2),
    ]


def block_rows(lower, upper, t0, te, it, edges, block):
    parts = zip(
        picked(lower, block, 0), picked(upper, block, 0), picked(lower, block, block - 1), picked(upper, block, block - 1),
        t0, te, picked(it, block, 1), picked(it, block, block - 2), *edges,
    )
    return [interface_rows(*p) for p in parts]


def store_rows(red_ref, v, rows):
    for k, sub in enumerate(rows):
        for q, pair in enumerate(sub):
            for i, value in enumerate(pair):
                red_ref[v, 0, q, 2 * k + i : 2 * k + i + 1, :] = value


def reduced_ends(red_refs, rows_ref, v):
    own = red_refs[0].shape[3]
    for k, ref in enumerate(red_refs):
        rows_ref[:, own * k : own * (k + 1), :] = ref[v, 0]
    lower, upper, target = rows_ref[0], rows_ref[1], rows_ref[2]
    length = lower.shape[0]
    stride = 1
    while stride < length:
        back = length - stride
        ll, ul = pltpu.roll(lower, stride, 0), pltpu.roll(upper, stride, 0)
        lr, ur = pltpu.roll(lower, back, 0), pltpu.roll(upper, back, 0)
        inv = 1.0 / (1.0 - lower * ul - upper * lr)
        target = (target - lower * pltpu.roll(target, stride, 0) - upper * pltpu.roll(target, back, 0)) * inv
        lower, upper = -lower * ll * inv, -upper * ur * inv
        stride = stride * 2
    ends = target / (1.0 + lower + upper)
    return ends[:own]


def back_substitute(it, ia, ib, ends, block):
    idx = lax.broadcasted_iota(jnp.int32, it.shape, 0)
    first = jnp.zeros_like(it)
    last = jnp.zeros_like(it)
    for k in range(it.shape[0] // block):
        inside = idx // block == k
        first = jnp.where(inside, ends[2 * k : 2 * k + 1], first)
        last = jnp.where(inside, ends[2 * k + 1 : 2 * k + 2], last)
    inner = it - ia * first - ib * last
    local = idx % block
    return jnp.where(local == 0, first, jnp.where(local == block - 1, last, inner))


def mixed(mix_ref, values):
    out = []
    for v in range(len(values)):
        summed = values[v]
        for w in range(len(values)):
            summed = summed + mix_ref[v, w : w + 1, :] * values[w]
        out.append(summed)
    return out


def az_coefficients(cell, visc_ref, beta_ref, v):
    coupling = visc_ref[v : v + 1, :] * cell
    scale = -1.0 / (1.0 + 2.0 * coupling)
    tilt = beta_ref[v : v + 1, :]
    lower = coupling * (1.0 + tilt) * scale
    upper = coupling * (1.0 - tilt) * scale
    return lower, upper, scale


def az_local_kernel(fs_ref, src_ref, cell_ref, visc_ref, beta_ref, diff_ref, mix_ref, ot_ref, oa_ref, ob_ref, edge_ref, *, block):
    count = fs_ref.shape[0]
    explicit = [src_ref[w, 0] + diff_ref[w : w + 1, :] * (-2.0 * fs_ref[w, 0]) for w in range(count)]
    section_one = mixed(mix_ref, explicit)
    cell = cell_ref[0]
    for v in range(count):
        lower, upper, scale = az_coefficients(cell, visc_ref, beta_ref, v)
        target = section_one[v] * -scale
        il, iu, keep, a_init, b_init = interior(lower, upper, block)
        it, ia, ib = pcr_levels(il, iu, [target * keep, a_init, b_init], block)
        ot_ref[v, 0] = it
        oa_ref[v, 0] = ia
        ob_ref[v, 0] = ib
        rows = [value for group in edge_rows(target, ia, ib, block) for value in group]
        for k, value in enumerate(rows):
            edge_ref[v, 0, k : k + 1, :] = value


def az_plane_kernel(nb_ref, cell_ref, visc_ref, beta_ref, diff_ref, mix_ref, it_in_ref, edge_ref, order_ref, ot_ref, red_ref, *, block):
    count = nb_ref.shape[0]
    explicit = [diff_ref[w : w + 1, :] * nb_ref[w, 0] for w in range(count)]
    section_one = mixed(mix_ref, explicit)
    cell = cell_ref[0]
    for v in range(count):
        lower, upper, scale = az_coefficients(cell, visc_ref, beta_ref, v)
        target = section_one[v] * -scale
        il, iu, keep, _, _ = interior(lower, upper, block)
        (it,) = pcr_levels(il, iu, [target * keep], block)
        it = it_in_ref[v, 0] + it
        ot_ref[v, 0] = it
        edge = edge_ref[v, 0]
        count_sub = lower.shape[0] // block
        groups = [[edge[g * count_sub + k : g * count_sub + k + 1] for k in range(count_sub)] for g in range(6)]
        t0 = [a + b for a, b in zip(groups[0], picked(target, block, 0))]
        te = [a + b for a, b in zip(groups[1], picked(target, block, block - 1))]
        store_rows(red_ref, v, block_rows(lower, upper, t0, te, it, groups[2:], block))


def rad_side(cell, visc, v):
    coupling = visc[v : v + 1, :] * cell
    scale = 1.0 / (1.0 + 2.0 * coupling)
    return -coupling * scale, scale


def local_visc(visc_ref, axis_name, cells):
    place = lax.axis_index(axis_name)
    return visc_ref[:, pl.ds(pl.multiple_of(place * cells, cells), cells)]


def rad_pre_kernel(cell_ref, visc_ref, oa_ref, ob_ref, edge_ref, *, axis_name, block):
    count = oa_ref.shape[0]
    cells = cell_ref.shape[2]
    visc = local_visc(visc_ref, axis_name, cells)
    cell = cell_ref[0]
    for v in range(count):
        side, _ = rad_side(cell, visc, v)
        side = side.T
        il, iu, _, a_init, b_init = interior(side, side, block)
        ia, ib = pcr_levels(il, iu, [a_init, b_init], block)
        oa_ref[v, 0] = ia
        ob_ref[v, 0] = ib
        rows = [value for group in edge_rows(ia, ia, ib, block)[2:] for value in group]
        for k, value in enumerate(rows):
            edge_ref[v, 0, k : k + 1, :] = value


def rad_kernel(*refs, axis_name, devices, pieces, block, az_block):
    it_ref, ia_ref, ib_ref = refs[:3]
    red_in = refs[3 : 3 + pieces]
    mix_ref, cell_ref, visc_ref, edge_ref, ot_ref, red_ref, rows_ref = refs[3 + pieces :]
    count = it_ref.shape[0]
    cells = it_ref.shape[3]
    place = lax.axis_index(axis_name)
    visc = local_visc(visc_ref, axis_name, cells)
    solved = []
    for w in range(count):
        ends = reduced_ends(red_in, rows_ref, w)
        solved.append(back_substitute(it_ref[w, 0], ia_ref[w, 0], ib_ref[w, 0], ends, az_block))
    section_three = mixed(mix_ref, solved)
    cell = cell_ref[0]
    for v in range(count):
        side, scale = rad_side(cell, visc, v)
        side = side.T
        target = (section_three[v] * scale).T
        il, iu, keep, _, _ = interior(side, side, block)
        (it,) = pcr_levels(il, iu, [target * keep], block)
        edge = edge_ref[v, 0]
        count_sub = side.shape[0] // block
        groups = [[edge[g * count_sub + k : g * count_sub + k + 1] for k in range(count_sub)] for g in range(4)]
        rows = block_rows(side, side, picked(target, block, 0), picked(target, block, block - 1), it, groups, block)
        (lf, le), upper_rows, trow = rows[0]
        rows[0] = ((jnp.where(place == 0, jnp.zeros_like(lf), lf), le), upper_rows, trow)
        lower_rows, (uf, ue), trow = rows[-1]
        rows[-1] = (lower_rows, (uf, jnp.where(place == devices - 1, jnp.zeros_like(ue), ue)), trow)
        store_rows(red_ref, v, rows)
        ot_ref[v, 0] = it


def out_kernel(*refs, pieces, block):
    it_ref, ia_ref, ib_ref = refs[:3]
    red_in = refs[3 : 3 + pieces]
    mix_ref, out_ref, rows_ref = refs[3 + pieces :]
    count = it_ref.shape[0]
    solved = []
    for w in range(count):
        ends = reduced_ends(red_in, rows_ref, w)
        solved.append(back_substitute(it_ref[w, 0], ia_ref[w, 0], ib_ref[w, 0], ends, block).T)
    for v, value in enumerate(mixed(mix_ref, solved)):
        out_ref[v, 0] = value


def sub_block(length, size):
    return size if length % size == 0 and length > size else length


def az_sweep(flow_state, nb, source, cell_az, visc_az, beta_az, axial_diff, mix_in, order):
    nv, nz, na, nr = flow_state.shape
    chunk = 128 if nr % 128 == 0 else nr
    grid = (nz, nr // chunk)
    big = pl.BlockSpec((nv, 1, na, chunk), lambda z, c: (0, z, 0, c))
    cell = pl.BlockSpec((1, na, chunk), lambda z, c: (z, 0, c))
    par = pl.BlockSpec((nv, chunk), lambda z, c: (0, c))
    mixs = pl.BlockSpec((nv, nv, chunk), lambda z, c: (0, 0, c))
    block = sub_block(na, 32)
    subs = na // block
    edge = pl.BlockSpec((nv, 1, 6 * subs, chunk), lambda z, c: (0, z, 0, c))
    red = pl.BlockSpec((nv, 1, 3, 2 * subs, chunk), lambda z, c: (0, z, 0, 0, c))
    out = jax.ShapeDtypeStruct(flow_state.shape, flow_state.dtype)
    it, ia, ib, edges = pl.pallas_call(
        functools.partial(az_local_kernel, block=block),
        grid=grid,
        in_specs=[big, big, cell, par, par, par, mixs],
        out_specs=[big, big, big, edge],
        out_shape=[out, out, out, jax.ShapeDtypeStruct((nv, nz, 6 * subs, nr), flow_state.dtype)],
    )(flow_state, source, cell_az, visc_az, beta_az, axial_diff, mix_in)
    it, red = pl.pallas_call(
        functools.partial(az_plane_kernel, block=block),
        grid=grid,
        in_specs=[big, cell, par, par, par, mixs, big, edge, pl.BlockSpec(memory_space=pl.ANY)],
        out_specs=[big, red],
        out_shape=[out, jax.ShapeDtypeStruct((nv, nz, 3, 2 * subs, nr), flow_state.dtype)],
        input_output_aliases={6: 0},
    )(nb, cell_az, visc_az, beta_az, axial_diff, mix_in, it, edges, order)
    return it, ia, ib, red


def rad_pre(cell_rad, visc_rad, nv):
    nz, na, nr = cell_rad.shape
    big_t = pl.BlockSpec((nv, 1, nr, na), lambda z: (0, z, 0, 0))
    cell = pl.BlockSpec((1, na, nr), lambda z: (z, 0, 0))
    par = pl.BlockSpec(visc_rad.shape, lambda z: (0, 0))
    block = sub_block(nr, 64)
    subs = nr // block
    edge = pl.BlockSpec((nv, 1, 4 * subs, na), lambda z: (0, z, 0, 0))
    out = jax.ShapeDtypeStruct((nv, nz, nr, na), cell_rad.dtype)
    return pl.pallas_call(
        functools.partial(rad_pre_kernel, axis_name="rad", block=block),
        grid=(nz,),
        in_specs=[cell, par],
        out_specs=[big_t, big_t, edge],
        out_shape=[out, out, jax.ShapeDtypeStruct((nv, nz, 4 * subs, na), cell_rad.dtype)],
    )(cell_rad, visc_rad)


def rad_sweep(it, ia, ib, red_in, mix_mid, cell_rad, visc_rad, edges):
    nv, nz, na, nr = it.shape
    big = pl.BlockSpec((nv, 1, na, nr), lambda z: (0, z, 0, 0))
    big_t = pl.BlockSpec((nv, 1, nr, na), lambda z: (0, z, 0, 0))
    red_in_spec = pl.BlockSpec((nv, 1) + red_in[0].shape[2:], lambda z: (0, z, 0, 0, 0))
    mixs = pl.BlockSpec((nv, nv, nr), lambda z: (0, 0, 0))
    cell = pl.BlockSpec((1, na, nr), lambda z: (z, 0, 0))
    par = pl.BlockSpec(visc_rad.shape, lambda z: (0, 0))
    block = sub_block(nr, 64)
    subs = nr // block
    edge = pl.BlockSpec((nv, 1, 4 * subs, na), lambda z: (0, z, 0, 0))
    red = pl.BlockSpec((nv, 1, 3, 2 * subs, na), lambda z: (0, z, 0, 0, 0))
    out = jax.ShapeDtypeStruct((nv, nz, nr, na), it.dtype)
    pieces = len(red_in)
    kernel = functools.partial(
        rad_kernel, axis_name="rad", devices=lax.axis_size("rad"), pieces=pieces, block=block, az_block=sub_block(na, 32)
    )
    return pl.pallas_call(
        kernel,
        grid=(nz,),
        in_specs=[big, big, big] + [red_in_spec] * pieces + [mixs, cell, par, edge],
        out_specs=[big_t, red],
        out_shape=[out, jax.ShapeDtypeStruct((nv, nz, 3, 2 * subs, na), it.dtype)],
        scratch_shapes=[pltpu.VMEM((3, red_in[0].shape[3] * pieces, nr), it.dtype)],
    )(it, ia, ib, *red_in, mix_mid, cell_rad, visc_rad, edges)


def out_sweep(it, ia, ib, red_in, mix_out):
    nv, nz, nr, na = it.shape
    big_t = pl.BlockSpec((nv, 1, nr, na), lambda z: (0, z, 0, 0))
    big = pl.BlockSpec((nv, 1, na, nr), lambda z: (0, z, 0, 0))
    red_in_spec = pl.BlockSpec((nv, 1) + red_in[0].shape[2:], lambda z: (0, z, 0, 0, 0))
    mixs = pl.BlockSpec((nv, nv, nr), lambda z: (0, 0, 0))
    pieces = len(red_in)
    return pl.pallas_call(
        functools.partial(out_kernel, pieces=pieces, block=sub_block(nr, 64)),
        grid=(nz,),
        in_specs=[big_t, big_t, big_t] + [red_in_spec] * pieces + [mixs],
        out_specs=big,
        out_shape=jax.ShapeDtypeStruct((nv, nz, na, nr), it.dtype),
        scratch_shapes=[pltpu.VMEM((3, red_in[0].shape[3] * pieces, na), it.dtype)],
    )(it, ia, ib, *red_in, mix_out)


def gathered(block, axis_name):
    count = lax.axis_size(axis_name)
    received = [block]
    for offset in range(1, count):
        pairs = [((i + offset) % count, i) for i in range(count)]
        received.append(lax.ppermute(block, axis_name, pairs))
    return received


def neighbour_planes(block, axis_name):
    count = lax.axis_size(axis_name)
    if count == 2:
        return lax.ppermute(block, axis_name, [(0, 1), (1, 0)])
    padded = with_halo(block, ((axis_name, 1),), 1, False)
    return padded[:, :-2] + padded[:, 2:]


def mix(matrix, values):
    mixed_rows = []
    for out_var in range(values.shape[0]):
        summed = values[out_var]
        for in_var in range(values.shape[0]):
            summed = summed + matrix[out_var, in_var][None, None, :] * values[in_var]
        mixed_rows.append(summed)
    return jnp.stack(mixed_rows)


def per_device(
    flow_state,
    source,
    cell_az,
    cell_rad,
    visc_az,
    beta_az,
    visc_rad,
    axial_diff,
    mix_in,
    mix_mid,
    mix_out,
):
    rad_cells = flow_state.shape[3]
    nb = neighbour_planes(flow_state, "ax")
    rad_a, rad_b, rad_edges = rad_pre(cell_rad, visc_rad, flow_state.shape[0])
    it, ia, ib, red = az_sweep(flow_state, nb, source, cell_az, visc_az, beta_az, axial_diff, mix_in, rad_edges)
    red = gathered(red, "az")
    it, red = rad_sweep(it, ia, ib, red, mix_mid, cell_rad, visc_rad, rad_edges)
    ia, ib = rad_a, rad_b
    red = gathered(red, "rad")
    return out_sweep(it, ia, ib, red, mix_out)


def solution(mesh):
    in_specs = (
        P(None, "ax", "az", "rad"),
        P(None, "ax", "az", "rad"),
        P("ax", "az", "rad"),
        P("ax", "az", "rad"),
        P(None, "rad"),
        P(None, "rad"),
        P(),
        P(None, "rad"),
        P(None, None, "rad"),
        P(None, None, "rad"),
        P(None, None, "rad"),
    )
    out_specs = P(None, "ax", "az", "rad")
    return jax.shard_map(
        per_device, mesh=mesh, in_specs=in_specs, out_specs=out_specs, check_vma=False
    )
```

```python
import jax
import jax.numpy as jnp
from jax import lax
from jax.experimental import pallas as pl
from jax.experimental.pallas import tpu as pltpu
from jax.sharding import PartitionSpec as P
import functools


def with_halo(block, sides, width, periodic):
    for axis, dim in sides:
        count = lax.axis_size(axis)
        forward = [(i, i + 1) for i in range(count - 1)]
        if periodic:
            forward.append((count - 1, 0))
        backward = [(target, source) for source, target in forward]
        low = lax.ppermute(
            lax.slice_in_dim(block, block.shape[dim] - width, None, axis=dim), axis, forward
        )
        high = lax.ppermute(lax.slice_in_dim(block, 0, width, axis=dim), axis, backward)
        block = jnp.concatenate([low, block, high], axis=dim)
    return block


def shifted(values, offset, axis, periodic):
    if periodic:
        return jnp.roll(values, offset, axis)
    length = values.shape[axis]
    zero_shape = list(values.shape)
    zero_shape[axis] = abs(offset)
    zeros = jnp.zeros(zero_shape, values.dtype)
    if offset > 0:
        kept = lax.slice_in_dim(values, 0, length - offset, axis=axis)
        return jnp.concatenate([zeros, kept], axis=axis)
    kept = lax.slice_in_dim(values, -offset, length, axis=axis)
    return jnp.concatenate([kept, zeros], axis=axis)


def cyclic_reduce(lower, upper, rhs, axis, periodic, steps_below):
    stride = 1
    while stride < steps_below:
        ll, ul = shifted(lower, stride, axis, periodic), shifted(upper, stride, axis, periodic)
        lr, ur = shifted(lower, -stride, axis, periodic), shifted(upper, -stride, axis, periodic)
        inv = 1.0 / (1.0 - lower * ul - upper * lr)
        rhs = [
            (r - lower * shifted(r, stride, axis, periodic) - upper * shifted(r, -stride, axis, periodic)) * inv
            for r in rhs
        ]
        lower, upper = -lower * ll * inv, -upper * ur * inv
        stride = stride * 2
    return lower, upper, rhs


def interior(lower, upper):
    length = lower.shape[0]
    idx = lax.broadcasted_iota(jnp.int32, lower.shape, 0)
    edge = (idx == 0) | (idx == length - 1)
    second = idx == 1
    penult = idx == length - 2
    zero = jnp.zeros_like(lower)
    il = jnp.where(edge | second, zero, lower)
    iu = jnp.where(edge | penult, zero, upper)
    return il, iu, jnp.where(edge, zero, 1.0), jnp.where(second, lower, zero), jnp.where(penult, upper, zero)


def pcr_levels(il, iu, rhs):
    length = il.shape[0]
    stride = 1
    while stride < length - 2:
        back = length - stride
        ll, ul = pltpu.roll(il, stride, 0), pltpu.roll(iu, stride, 0)
        lr, ur = pltpu.roll(il, back, 0), pltpu.roll(iu, back, 0)
        inv = 1.0 / (1.0 - il * ul - iu * lr)
        rhs = [(r - il * pltpu.roll(r, stride, 0) - iu * pltpu.roll(r, back, 0)) * inv for r in rhs]
        flip = -inv
        il, iu = il * ll * flip, iu * ur * flip
        stride = stride * 2
    return rhs


def interface_rows(lower, upper, t0, te, t1, t2, a1, b1, a2, b2):
    length = lower.shape[0]
    l0, u0 = lower[0:1], upper[0:1]
    le, ue = lower[length - 1 :], upper[length - 1 :]
    inv_f = 1.0 / (1.0 - u0 * a1)
    inv_e = 1.0 / (1.0 - le * b2)
    return (
        (l0 * inv_f, -le * a2 * inv_e),
        (-u0 * b1 * inv_f, ue * inv_e),
        ((t0 - u0 * t1) * inv_f, (te - le * t2) * inv_e),
    )


def reduce_block(lower, upper, target):
    length = lower.shape[0]
    il, iu, keep, a_init, b_init = interior(lower, upper)
    it, ia, ib = pcr_levels(il, iu, [target * keep, a_init, b_init])
    n2 = length - 2
    rows = interface_rows(
        lower, upper, target[0:1], target[length - 1 :], it[1:2], it[n2 : n2 + 1],
        ia[1:2], ib[1:2], ia[n2 : n2 + 1], ib[n2 : n2 + 1],
    )
    return it, ia, ib, rows


def store_rows(red_ref, v, rows):
    for q, pair in enumerate(rows):
        for i, value in enumerate(pair):
            red_ref[v, 0, q, i : i + 1, :] = value


def reduced_ends(red_refs, rows_ref, v):
    for k, ref in enumerate(red_refs):
        rows_ref[:, 2 * k : 2 * k + 2, :] = ref[v, 0]
    lower, upper, target = rows_ref[0], rows_ref[1], rows_ref[2]
    length = lower.shape[0]
    stride = 1
    while stride < length:
        back = length - stride
        ll, ul = pltpu.roll(lower, stride, 0), pltpu.roll(upper, stride, 0)
        lr, ur = pltpu.roll(lower, back, 0), pltpu.roll(upper, back, 0)
        inv = 1.0 / (1.0 - lower * ul - upper * lr)
        target = (target - lower * pltpu.roll(target, stride, 0) - upper * pltpu.roll(target, back, 0)) * inv
        lower, upper = -lower * ll * inv, -upper * ur * inv
        stride = stride * 2
    ends = target / (1.0 + lower + upper)
    return ends[0:1], ends[1:2]


def back_substitute(it, ia, ib, first, last):
    length = it.shape[0]
    idx = lax.broadcasted_iota(jnp.int32, it.shape, 0)
    inner = it - ia * first - ib * last
    return jnp.where(idx == 0, first, jnp.where(idx == length - 1, last, inner))


def mixed(mix_ref, values):
    out = []
    for v in range(len(values)):
        summed = values[v]
        for w in range(len(values)):
            summed = summed + mix_ref[v, w : w + 1, :] * values[w]
        out.append(summed)
    return out


def az_coefficients(cell, visc_ref, beta_ref, v):
    coupling = visc_ref[v : v + 1, :] * cell
    scale = -1.0 / (1.0 + 2.0 * coupling)
    tilt = beta_ref[v : v + 1, :]
    lower = coupling * (1.0 + tilt) * scale
    upper = coupling * (1.0 - tilt) * scale
    return lower, upper, scale


def az_local_kernel(fs_ref, src_ref, cell_ref, visc_ref, beta_ref, diff_ref, mix_ref, ot_ref, oa_ref, ob_ref, edge_ref):
    count = fs_ref.shape[0]
    explicit = [src_ref[w, 0] + diff_ref[w : w + 1, :] * (-2.0 * fs_ref[w, 0]) for w in range(count)]
    section_one = mixed(mix_ref, explicit)
    cell = cell_ref[0]
    for v in range(count):
        lower, upper, scale = az_coefficients(cell, visc_ref, beta_ref, v)
        target = section_one[v] * -scale
        length = lower.shape[0]
        il, iu, keep, a_init, b_init = interior(lower, upper)
        it, ia, ib = pcr_levels(il, iu, [target * keep, a_init, b_init])
        ot_ref[v, 0] = it
        oa_ref[v, 0] = ia
        ob_ref[v, 0] = ib
        n2 = length - 2
        for k, value in enumerate(
            (target[0:1], target[length - 1 :], ia[1:2], ib[1:2], ia[n2 : n2 + 1], ib[n2 : n2 + 1])
        ):
            edge_ref[v, 0, k : k + 1, :] = value


def az_plane_kernel(nb_ref, cell_ref, visc_ref, beta_ref, diff_ref, mix_ref, it_in_ref, edge_ref, order_ref, ot_ref, red_ref):
    count = nb_ref.shape[0]
    explicit = [diff_ref[w : w + 1, :] * nb_ref[w, 0] for w in range(count)]
    section_one = mixed(mix_ref, explicit)
    cell = cell_ref[0]
    for v in range(count):
        lower, upper, scale = az_coefficients(cell, visc_ref, beta_ref, v)
        target = section_one[v] * -scale
        length = lower.shape[0]
        il, iu, keep, _, _ = interior(lower, upper)
        (it,) = pcr_levels(il, iu, [target * keep])
        it = it_in_ref[v, 0] + it
        ot_ref[v, 0] = it
        edge = edge_ref[v, 0]
        n2 = length - 2
        rows = interface_rows(
            lower, upper, edge[0:1] + target[0:1], edge[1:2] + target[length - 1 :], it[1:2], it[n2 : n2 + 1],
            edge[2:3], edge[3:4], edge[4:5], edge[5:6],
        )
        store_rows(red_ref, v, rows)


def rad_side(cell, visc, v):
    coupling = visc[v : v + 1, :] * cell
    scale = 1.0 / (1.0 + 2.0 * coupling)
    return -coupling * scale, scale


def local_visc(visc_ref, axis_name, cells):
    place = lax.axis_index(axis_name)
    return visc_ref[:, pl.ds(pl.multiple_of(place * cells, cells), cells)]


def rad_pre_kernel(cell_ref, visc_ref, oa_ref, ob_ref, edge_ref, *, axis_name):
    count = oa_ref.shape[0]
    cells = cell_ref.shape[2]
    visc = local_visc(visc_ref, axis_name, cells)
    cell = cell_ref[0]
    for v in range(count):
        side, _ = rad_side(cell, visc, v)
        side = side.T
        length = side.shape[0]
        il, iu, _, a_init, b_init = interior(side, side)
        ia, ib = pcr_levels(il, iu, [a_init, b_init])
        oa_ref[v, 0] = ia
        ob_ref[v, 0] = ib
        n2 = length - 2
        for k, value in enumerate((ia[1:2], ib[1:2], ia[n2 : n2 + 1], ib[n2 : n2 + 1])):
            edge_ref[v, 0, k : k + 1, :] = value


def rad_kernel(*refs, axis_name, devices, pieces):
    it_ref, ia_ref, ib_ref = refs[:3]
    red_in = refs[3 : 3 + pieces]
    mix_ref, cell_ref, visc_ref, edge_ref, ra_ref, rb_ref, tt_ref, red_ref, rows_ref = refs[3 + pieces :]
    count = it_ref.shape[0]
    cells = it_ref.shape[3]
    place = lax.axis_index(axis_name)
    visc = local_visc(visc_ref, axis_name, cells)
    solved = []
    for w in range(count):
        first, last = reduced_ends(red_in, rows_ref, w)
        solved.append(back_substitute(it_ref[w, 0], ia_ref[w, 0], ib_ref[w, 0], first, last))
    section_three = mixed(mix_ref, solved)
    cell = cell_ref[0]
    for v in range(count):
        side, scale = rad_side(cell, visc, v)
        side = side.T
        target = (section_three[v] * scale).T
        length = side.shape[0]
        _, _, keep, _, _ = interior(side, side)
        inner = target * keep
        tt_ref[v, 0] = inner
        t1 = jnp.sum(ra_ref[v, 0] / side * inner, axis=0, keepdims=True)
        t2 = jnp.sum(rb_ref[v, 0] / side * inner, axis=0, keepdims=True)
        edge = edge_ref[v, 0]
        (lf, le), (uf, ue), trow = interface_rows(
            side, side, target[0:1], target[length - 1 :], t1, t2,
            edge[0:1], edge[1:2], edge[2:3], edge[3:4],
        )
        lf = jnp.where(place == 0, jnp.zeros_like(lf), lf)
        ue = jnp.where(place == devices - 1, jnp.zeros_like(ue), ue)
        store_rows(red_ref, v, ((lf, le), (uf, ue), trow))


def rad_solve_kernel(tt_ref, cell_ref, visc_ref, ot_ref, *, axis_name):
    count = tt_ref.shape[0]
    cells = cell_ref.shape[2]
    visc = local_visc(visc_ref, axis_name, cells)
    cell = cell_ref[0]
    for v in range(count):
        side, _ = rad_side(cell, visc, v)
        side = side.T
        il, iu, _, _, _ = interior(side, side)
        (it,) = pcr_levels(il, iu, [tt_ref[v, 0]])
        ot_ref[v, 0] = it


def out_kernel(*refs, pieces):
    it_ref, ia_ref, ib_ref = refs[:3]
    red_in = refs[3 : 3 + pieces]
    mix_ref, out_ref, rows_ref = refs[3 + pieces :]
    count = it_ref.shape[0]
    solved = []
    for w in range(count):
        first, last = reduced_ends(red_in, rows_ref, w)
        solved.append(back_substitute(it_ref[w, 0], ia_ref[w, 0], ib_ref[w, 0], first, last).T)
    for v, value in enumerate(mixed(mix_ref, solved)):
        out_ref[v, 0] = value


def az_sweep(flow_state, nb, source, cell_az, visc_az, beta_az, axial_diff, mix_in, order):
    nv, nz, na, nr = flow_state.shape
    chunk = 128 if nr % 128 == 0 else nr
    grid = (nz, nr // chunk)
    big = pl.BlockSpec((nv, 1, na, chunk), lambda z, c: (0, z, 0, c))
    cell = pl.BlockSpec((1, na, chunk), lambda z, c: (z, 0, c))
    par = pl.BlockSpec((nv, chunk), lambda z, c: (0, c))
    mixs = pl.BlockSpec((nv, nv, chunk), lambda z, c: (0, 0, c))
    edge = pl.BlockSpec((nv, 1, 6, chunk), lambda z, c: (0, z, 0, c))
    red = pl.BlockSpec((nv, 1, 3, 2, chunk), lambda z, c: (0, z, 0, 0, c))
    out = jax.ShapeDtypeStruct(flow_state.shape, flow_state.dtype)
    it, ia, ib, edges = pl.pallas_call(
        az_local_kernel,
        grid=grid,
        in_specs=[big, big, cell, par, par, par, mixs],
        out_specs=[big, big, big, edge],
        out_shape=[out, out, out, jax.ShapeDtypeStruct((nv, nz, 6, nr), flow_state.dtype)],
    )(flow_state, source, cell_az, visc_az, beta_az, axial_diff, mix_in)
    it, red = pl.pallas_call(
        az_plane_kernel,
        grid=grid,
        in_specs=[big, cell, par, par, par, mixs, big, edge, pl.BlockSpec(memory_space=pl.ANY)],
        out_specs=[big, red],
        out_shape=[out, jax.ShapeDtypeStruct((nv, nz, 3, 2, nr), flow_state.dtype)],
        input_output_aliases={6: 0},
    )(nb, cell_az, visc_az, beta_az, axial_diff, mix_in, it, edges, order)
    return it, ia, ib, red


def rad_pre(cell_rad, visc_rad, nv):
    nz, na, nr = cell_rad.shape
    big_t = pl.BlockSpec((nv, 1, nr, na), lambda z: (0, z, 0, 0))
    cell = pl.BlockSpec((1, na, nr), lambda z: (z, 0, 0))
    par = pl.BlockSpec(visc_rad.shape, lambda z: (0, 0))
    edge = pl.BlockSpec((nv, 1, 4, na), lambda z: (0, z, 0, 0))
    out = jax.ShapeDtypeStruct((nv, nz, nr, na), cell_rad.dtype)
    return pl.pallas_call(
        functools.partial(rad_pre_kernel, axis_name="rad"),
        grid=(nz,),
        in_specs=[cell, par],
        out_specs=[big_t, big_t, edge],
        out_shape=[out, out, jax.ShapeDtypeStruct((nv, nz, 4, na), cell_rad.dtype)],
    )(cell_rad, visc_rad)


def rad_sweep(it, ia, ib, red_in, mix_mid, cell_rad, visc_rad, edges, rad_a, rad_b):
    nv, nz, na, nr = it.shape
    big = pl.BlockSpec((nv, 1, na, nr), lambda z: (0, z, 0, 0))
    big_t = pl.BlockSpec((nv, 1, nr, na), lambda z: (0, z, 0, 0))
    red_in_spec = pl.BlockSpec((nv, 1) + red_in[0].shape[2:], lambda z: (0, z, 0, 0, 0))
    mixs = pl.BlockSpec((nv, nv, nr), lambda z: (0, 0, 0))
    cell = pl.BlockSpec((1, na, nr), lambda z: (z, 0, 0))
    par = pl.BlockSpec(visc_rad.shape, lambda z: (0, 0))
    edge = pl.BlockSpec((nv, 1, 4, na), lambda z: (0, z, 0, 0))
    red = pl.BlockSpec((nv, 1, 3, 2, na), lambda z: (0, z, 0, 0, 0))
    out = jax.ShapeDtypeStruct((nv, nz, nr, na), it.dtype)
    pieces = len(red_in)
    kernel = functools.partial(rad_kernel, axis_name="rad", devices=lax.axis_size("rad"), pieces=pieces)
    targets, red_out = pl.pallas_call(
        kernel,
        grid=(nz,),
        in_specs=[big, big, big] + [red_in_spec] * pieces + [mixs, cell, par, edge, big_t, big_t],
        out_specs=[big_t, red],
        out_shape=[out, jax.ShapeDtypeStruct((nv, nz, 3, 2, na), it.dtype)],
        scratch_shapes=[pltpu.VMEM((3, 2 * pieces, nr), it.dtype)],
    )(it, ia, ib, *red_in, mix_mid, cell_rad, visc_rad, edges, rad_a, rad_b)
    return targets, red_out


def rad_solve(targets, cell_rad, visc_rad):
    nv, nz, nr, na = targets.shape
    big_t = pl.BlockSpec((nv, 1, nr, na), lambda z: (0, z, 0, 0))
    cell = pl.BlockSpec((1, na, nr), lambda z: (z, 0, 0))
    par = pl.BlockSpec(visc_rad.shape, lambda z: (0, 0))
    return pl.pallas_call(
        functools.partial(rad_solve_kernel, axis_name="rad"),
        grid=(nz,),
        in_specs=[big_t, cell, par],
        out_specs=big_t,
        out_shape=jax.ShapeDtypeStruct(targets.shape, targets.dtype),
    )(targets, cell_rad, visc_rad)


def out_sweep(it, ia, ib, red_in, mix_out):
    nv, nz, nr, na = it.shape
    big_t = pl.BlockSpec((nv, 1, nr, na), lambda z: (0, z, 0, 0))
    big = pl.BlockSpec((nv, 1, na, nr), lambda z: (0, z, 0, 0))
    red_in_spec = pl.BlockSpec((nv, 1) + red_in[0].shape[2:], lambda z: (0, z, 0, 0, 0))
    mixs = pl.BlockSpec((nv, nv, nr), lambda z: (0, 0, 0))
    pieces = len(red_in)
    return pl.pallas_call(
        functools.partial(out_kernel, pieces=pieces),
        grid=(nz,),
        in_specs=[big_t, big_t, big_t] + [red_in_spec] * pieces + [mixs],
        out_specs=big,
        out_shape=jax.ShapeDtypeStruct((nv, nz, na, nr), it.dtype),
        scratch_shapes=[pltpu.VMEM((3, 2 * pieces, na), it.dtype)],
    )(it, ia, ib, *red_in, mix_out)


def gathered(block, axis_name):
    count = lax.axis_size(axis_name)
    received = [block]
    for offset in range(1, count):
        pairs = [((i + offset) % count, i) for i in range(count)]
        received.append(lax.ppermute(block, axis_name, pairs))
    return received


def neighbour_planes(block, axis_name):
    count = lax.axis_size(axis_name)
    if count == 2:
        return lax.ppermute(block, axis_name, [(0, 1), (1, 0)])
    padded = with_halo(block, ((axis_name, 1),), 1, False)
    return padded[:, :-2] + padded[:, 2:]


def mix(matrix, values):
    mixed_rows = []
    for out_var in range(values.shape[0]):
        summed = values[out_var]
        for in_var in range(values.shape[0]):
            summed = summed + matrix[out_var, in_var][None, None, :] * values[in_var]
        mixed_rows.append(summed)
    return jnp.stack(mixed_rows)


def per_device(
    flow_state,
    source,
    cell_az,
    cell_rad,
    visc_az,
    beta_az,
    visc_rad,
    axial_diff,
    mix_in,
    mix_mid,
    mix_out,
):
    rad_cells = flow_state.shape[3]
    nb = neighbour_planes(flow_state, "ax")
    rad_a, rad_b, rad_edges = rad_pre(cell_rad, visc_rad, flow_state.shape[0])
    it, ia, ib, red = az_sweep(flow_state, nb, source, cell_az, visc_az, beta_az, axial_diff, mix_in, rad_edges)
    red = gathered(red, "az")
    targets, red = rad_sweep(it, ia, ib, red, mix_mid, cell_rad, visc_rad, rad_edges, rad_a, rad_b)
    red = gathered(red, "rad")
    it = rad_solve(targets, cell_rad, visc_rad)
    ia, ib = rad_a, rad_b
    return out_sweep(it, ia, ib, red, mix_out)


def solution(mesh):
    in_specs = (
        P(None, "ax", "az", "rad"),
        P(None, "ax", "az", "rad"),
        P("ax", "az", "rad"),
        P("ax", "az", "rad"),
        P(None, "rad"),
        P(None, "rad"),
        P(),
        P(None, "rad"),
        P(None, None, "rad"),
        P(None, None, "rad"),
        P(None, None, "rad"),
    )
    out_specs = P(None, "ax", "az", "rad")
    return jax.shard_map(
        per_device, mesh=mesh, in_specs=in_specs, out_specs=out_specs, check_vma=False
    )
```

```python
import jax
import jax.numpy as jnp
from jax import lax
from jax.experimental import pallas as pl
from jax.experimental.pallas import tpu as pltpu
from jax.sharding import PartitionSpec as P
import functools


def with_halo(block, sides, width, periodic):
    for axis, dim in sides:
        count = lax.axis_size(axis)
        forward = [(i, i + 1) for i in range(count - 1)]
        if periodic:
            forward.append((count - 1, 0))
        backward = [(target, source) for source, target in forward]
        low = lax.ppermute(
            lax.slice_in_dim(block, block.shape[dim] - width, None, axis=dim), axis, forward
        )
        high = lax.ppermute(lax.slice_in_dim(block, 0, width, axis=dim), axis, backward)
        block = jnp.concatenate([low, block, high], axis=dim)
    return block


def shifted(values, offset, axis, periodic):
    if periodic:
        return jnp.roll(values, offset, axis)
    length = values.shape[axis]
    zero_shape = list(values.shape)
    zero_shape[axis] = abs(offset)
    zeros = jnp.zeros(zero_shape, values.dtype)
    if offset > 0:
        kept = lax.slice_in_dim(values, 0, length - offset, axis=axis)
        return jnp.concatenate([zeros, kept], axis=axis)
    kept = lax.slice_in_dim(values, -offset, length, axis=axis)
    return jnp.concatenate([kept, zeros], axis=axis)


def cyclic_reduce(lower, upper, rhs, axis, periodic, steps_below):
    stride = 1
    while stride < steps_below:
        ll, ul = shifted(lower, stride, axis, periodic), shifted(upper, stride, axis, periodic)
        lr, ur = shifted(lower, -stride, axis, periodic), shifted(upper, -stride, axis, periodic)
        inv = 1.0 / (1.0 - lower * ul - upper * lr)
        rhs = [
            (r - lower * shifted(r, stride, axis, periodic) - upper * shifted(r, -stride, axis, periodic)) * inv
            for r in rhs
        ]
        lower, upper = -lower * ll * inv, -upper * ur * inv
        stride = stride * 2
    return lower, upper, rhs


def interior(lower, upper):
    length = lower.shape[0]
    idx = lax.broadcasted_iota(jnp.int32, lower.shape, 0)
    edge = (idx == 0) | (idx == length - 1)
    second = idx == 1
    penult = idx == length - 2
    zero = jnp.zeros_like(lower)
    il = jnp.where(edge | second, zero, lower)
    iu = jnp.where(edge | penult, zero, upper)
    return il, iu, jnp.where(edge, zero, 1.0), jnp.where(second, lower, zero), jnp.where(penult, upper, zero)


def pcr_levels(il, iu, rhs):
    length = il.shape[0]
    stride = 1
    while stride < length - 2:
        back = length - stride
        ll, ul = pltpu.roll(il, stride, 0), pltpu.roll(iu, stride, 0)
        lr, ur = pltpu.roll(il, back, 0), pltpu.roll(iu, back, 0)
        inv = 1.0 / (1.0 - il * ul - iu * lr)
        rhs = [(r - il * pltpu.roll(r, stride, 0) - iu * pltpu.roll(r, back, 0)) * inv for r in rhs]
        flip = -inv
        il, iu = il * ll * flip, iu * ur * flip
        stride = stride * 2
    return rhs


def interface_rows(lower, upper, t0, te, t1, t2, a1, b1, a2, b2):
    length = lower.shape[0]
    l0, u0 = lower[0:1], upper[0:1]
    le, ue = lower[length - 1 :], upper[length - 1 :]
    inv_f = 1.0 / (1.0 - u0 * a1)
    inv_e = 1.0 / (1.0 - le * b2)
    return (
        (l0 * inv_f, -le * a2 * inv_e),
        (-u0 * b1 * inv_f, ue * inv_e),
        ((t0 - u0 * t1) * inv_f, (te - le * t2) * inv_e),
    )


def reduce_block(lower, upper, target):
    length = lower.shape[0]
    il, iu, keep, a_init, b_init = interior(lower, upper)
    it, ia, ib = pcr_levels(il, iu, [target * keep, a_init, b_init])
    n2 = length - 2
    rows = interface_rows(
        lower, upper, target[0:1], target[length - 1 :], it[1:2], it[n2 : n2 + 1],
        ia[1:2], ib[1:2], ia[n2 : n2 + 1], ib[n2 : n2 + 1],
    )
    return it, ia, ib, rows


def store_rows(red_ref, v, rows):
    for q, pair in enumerate(rows):
        for i, value in enumerate(pair):
            red_ref[v, 0, q, i : i + 1, :] = value


def reduced_ends(red_refs, rows_ref, v):
    for k, ref in enumerate(red_refs):
        rows_ref[:, 2 * k : 2 * k + 2, :] = ref[v, 0]
    lower, upper, target = rows_ref[0], rows_ref[1], rows_ref[2]
    length = lower.shape[0]
    stride = 1
    while stride < length:
        back = length - stride
        ll, ul = pltpu.roll(lower, stride, 0), pltpu.roll(upper, stride, 0)
        lr, ur = pltpu.roll(lower, back, 0), pltpu.roll(upper, back, 0)
        inv = 1.0 / (1.0 - lower * ul - upper * lr)
        target = (target - lower * pltpu.roll(target, stride, 0) - upper * pltpu.roll(target, back, 0)) * inv
        lower, upper = -lower * ll * inv, -upper * ur * inv
        stride = stride * 2
    ends = target / (1.0 + lower + upper)
    return ends[0:1], ends[1:2]


def back_substitute(it, ia, ib, first, last):
    length = it.shape[0]
    idx = lax.broadcasted_iota(jnp.int32, it.shape, 0)
    inner = it - ia * first - ib * last
    return jnp.where(idx == 0, first, jnp.where(idx == length - 1, last, inner))


def mixed(mix_ref, values):
    out = []
    for v in range(len(values)):
        summed = values[v]
        for w in range(len(values)):
            summed = summed + mix_ref[v, w : w + 1, :] * values[w]
        out.append(summed)
    return out


def az_coefficients(cell, visc_ref, beta_ref, v):
    coupling = visc_ref[v : v + 1, :] * cell
    scale = -1.0 / (1.0 + 2.0 * coupling)
    tilt = beta_ref[v : v + 1, :]
    lower = coupling * (1.0 + tilt) * scale
    upper = coupling * (1.0 - tilt) * scale
    return lower, upper, scale


def az_local_kernel(fs_ref, src_ref, cell_ref, visc_ref, beta_ref, diff_ref, mix_ref, ot_ref, oa_ref, ob_ref, edge_ref):
    count = fs_ref.shape[0]
    explicit = [src_ref[w, 0] + diff_ref[w : w + 1, :] * (-2.0 * fs_ref[w, 0]) for w in range(count)]
    section_one = mixed(mix_ref, explicit)
    cell = cell_ref[0]
    for v in range(count):
        lower, upper, scale = az_coefficients(cell, visc_ref, beta_ref, v)
        target = section_one[v] * -scale
        length = lower.shape[0]
        il, iu, keep, a_init, b_init = interior(lower, upper)
        it, ia, ib = pcr_levels(il, iu, [target * keep, a_init, b_init])
        ot_ref[v, 0] = it
        oa_ref[v, 0] = ia
        ob_ref[v, 0] = ib
        n2 = length - 2
        for k, value in enumerate(
            (target[0:1], target[length - 1 :], ia[1:2], ib[1:2], ia[n2 : n2 + 1], ib[n2 : n2 + 1])
        ):
            edge_ref[v, 0, k : k + 1, :] = value


def az_plane_kernel(nb_ref, cell_ref, visc_ref, beta_ref, diff_ref, mix_ref, it_in_ref, edge_ref, order_ref, ot_ref, red_ref):
    count = nb_ref.shape[0]
    explicit = [diff_ref[w : w + 1, :] * nb_ref[w, 0] for w in range(count)]
    section_one = mixed(mix_ref, explicit)
    cell = cell_ref[0]
    for v in range(count):
        lower, upper, scale = az_coefficients(cell, visc_ref, beta_ref, v)
        target = section_one[v] * -scale
        length = lower.shape[0]
        il, iu, keep, _, _ = interior(lower, upper)
        (it,) = pcr_levels(il, iu, [target * keep])
        it = it_in_ref[v, 0] + it
        ot_ref[v, 0] = it
        edge = edge_ref[v, 0]
        n2 = length - 2
        rows = interface_rows(
            lower, upper, edge[0:1] + target[0:1], edge[1:2] + target[length - 1 :], it[1:2], it[n2 : n2 + 1],
            edge[2:3], edge[3:4], edge[4:5], edge[5:6],
        )
        store_rows(red_ref, v, rows)


def rad_side(cell, visc, v):
    coupling = visc[v : v + 1, :] * cell
    scale = 1.0 / (1.0 + 2.0 * coupling)
    return -coupling * scale, scale


def local_visc(visc_ref, axis_name, cells):
    place = lax.axis_index(axis_name)
    return visc_ref[:, pl.ds(pl.multiple_of(place * cells, cells), cells)]


def rad_pre_kernel(cell_ref, visc_ref, oa_ref, ob_ref, os_ref, edge_ref, *, axis_name):
    count = oa_ref.shape[0]
    cells = cell_ref.shape[2]
    visc = local_visc(visc_ref, axis_name, cells)
    cell = cell_ref[0]
    for v in range(count):
        side, _ = rad_side(cell, visc, v)
        side = side.T
        os_ref[v, 0] = side
        length = side.shape[0]
        il, iu, _, a_init, b_init = interior(side, side)
        ia, ib = pcr_levels(il, iu, [a_init, b_init])
        oa_ref[v, 0] = ia
        ob_ref[v, 0] = ib
        n2 = length - 2
        for k, value in enumerate((ia[1:2], ib[1:2], ia[n2 : n2 + 1], ib[n2 : n2 + 1])):
            edge_ref[v, 0, k : k + 1, :] = value


def rad_kernel(*refs, axis_name, devices, pieces):
    it_ref, ia_ref, ib_ref = refs[:3]
    red_in = refs[3 : 3 + pieces]
    mix_ref, cell_ref, visc_ref, edge_ref, ra_ref, rb_ref, side_ref, tt_ref, red_ref, rows_ref = refs[3 + pieces :]
    count = it_ref.shape[0]
    cells = it_ref.shape[3]
    place = lax.axis_index(axis_name)
    visc = local_visc(visc_ref, axis_name, cells)
    solved = []
    for w in range(count):
        first, last = reduced_ends(red_in, rows_ref, w)
        solved.append(back_substitute(it_ref[w, 0], ia_ref[w, 0], ib_ref[w, 0], first, last))
    section_three = mixed(mix_ref, solved)
    cell = cell_ref[0]
    for v in range(count):
        _, scale = rad_side(cell, visc, v)
        side = side_ref[v, 0]
        target = (section_three[v] * scale).T
        length = side.shape[0]
        _, _, keep, _, _ = interior(side, side)
        inner = target * keep
        tt_ref[v, 0] = inner
        t1 = jnp.sum(ra_ref[v, 0] / side * inner, axis=0, keepdims=True)
        t2 = jnp.sum(rb_ref[v, 0] / side * inner, axis=0, keepdims=True)
        edge = edge_ref[v, 0]
        (lf, le), (uf, ue), trow = interface_rows(
            side, side, target[0:1], target[length - 1 :], t1, t2,
            edge[0:1], edge[1:2], edge[2:3], edge[3:4],
        )
        lf = jnp.where(place == 0, jnp.zeros_like(lf), lf)
        ue = jnp.where(place == devices - 1, jnp.zeros_like(ue), ue)
        store_rows(red_ref, v, ((lf, le), (uf, ue), trow))


def rad_solve_kernel(tt_ref, side_ref, ot_ref):
    count = tt_ref.shape[0]
    for v in range(count):
        side = side_ref[v, 0]
        il, iu, _, _, _ = interior(side, side)
        (it,) = pcr_levels(il, iu, [tt_ref[v, 0]])
        ot_ref[v, 0] = it


def out_kernel(*refs, pieces):
    it_ref, ia_ref, ib_ref = refs[:3]
    red_in = refs[3 : 3 + pieces]
    mix_ref, out_ref, rows_ref = refs[3 + pieces :]
    count = it_ref.shape[0]
    solved = []
    for w in range(count):
        first, last = reduced_ends(red_in, rows_ref, w)
        solved.append(back_substitute(it_ref[w, 0], ia_ref[w, 0], ib_ref[w, 0], first, last).T)
    for v, value in enumerate(mixed(mix_ref, solved)):
        out_ref[v, 0] = value


def az_sweep(flow_state, nb, source, cell_az, visc_az, beta_az, axial_diff, mix_in, order):
    nv, nz, na, nr = flow_state.shape
    chunk = 128 if nr % 128 == 0 else nr
    grid = (nz, nr // chunk)
    big = pl.BlockSpec((nv, 1, na, chunk), lambda z, c: (0, z, 0, c))
    cell = pl.BlockSpec((1, na, chunk), lambda z, c: (z, 0, c))
    par = pl.BlockSpec((nv, chunk), lambda z, c: (0, c))
    mixs = pl.BlockSpec((nv, nv, chunk), lambda z, c: (0, 0, c))
    edge = pl.BlockSpec((nv, 1, 6, chunk), lambda z, c: (0, z, 0, c))
    red = pl.BlockSpec((nv, 1, 3, 2, chunk), lambda z, c: (0, z, 0, 0, c))
    out = jax.ShapeDtypeStruct(flow_state.shape, flow_state.dtype)
    it, ia, ib, edges = pl.pallas_call(
        az_local_kernel,
        grid=grid,
        in_specs=[big, big, cell, par, par, par, mixs],
        out_specs=[big, big, big, edge],
        out_shape=[out, out, out, jax.ShapeDtypeStruct((nv, nz, 6, nr), flow_state.dtype)],
    )(flow_state, source, cell_az, visc_az, beta_az, axial_diff, mix_in)
    it, red = pl.pallas_call(
        az_plane_kernel,
        grid=grid,
        in_specs=[big, cell, par, par, par, mixs, big, edge, pl.BlockSpec(memory_space=pl.ANY)],
        out_specs=[big, red],
        out_shape=[out, jax.ShapeDtypeStruct((nv, nz, 3, 2, nr), flow_state.dtype)],
        input_output_aliases={6: 0},
    )(nb, cell_az, visc_az, beta_az, axial_diff, mix_in, it, edges, order)
    return it, ia, ib, red


def rad_pre(cell_rad, visc_rad, nv):
    nz, na, nr = cell_rad.shape
    big_t = pl.BlockSpec((nv, 1, nr, na), lambda z: (0, z, 0, 0))
    cell = pl.BlockSpec((1, na, nr), lambda z: (z, 0, 0))
    par = pl.BlockSpec(visc_rad.shape, lambda z: (0, 0))
    edge = pl.BlockSpec((nv, 1, 4, na), lambda z: (0, z, 0, 0))
    out = jax.ShapeDtypeStruct((nv, nz, nr, na), cell_rad.dtype)
    return pl.pallas_call(
        functools.partial(rad_pre_kernel, axis_name="rad"),
        grid=(nz,),
        in_specs=[cell, par],
        out_specs=[big_t, big_t, big_t, edge],
        out_shape=[out, out, out, jax.ShapeDtypeStruct((nv, nz, 4, na), cell_rad.dtype)],
    )(cell_rad, visc_rad)


def rad_sweep(it, ia, ib, red_in, mix_mid, cell_rad, visc_rad, edges, rad_a, rad_b, sides):
    nv, nz, na, nr = it.shape
    big = pl.BlockSpec((nv, 1, na, nr), lambda z: (0, z, 0, 0))
    big_t = pl.BlockSpec((nv, 1, nr, na), lambda z: (0, z, 0, 0))
    red_in_spec = pl.BlockSpec((nv, 1) + red_in[0].shape[2:], lambda z: (0, z, 0, 0, 0))
    mixs = pl.BlockSpec((nv, nv, nr), lambda z: (0, 0, 0))
    cell = pl.BlockSpec((1, na, nr), lambda z: (z, 0, 0))
    par = pl.BlockSpec(visc_rad.shape, lambda z: (0, 0))
    edge = pl.BlockSpec((nv, 1, 4, na), lambda z: (0, z, 0, 0))
    red = pl.BlockSpec((nv, 1, 3, 2, na), lambda z: (0, z, 0, 0, 0))
    out = jax.ShapeDtypeStruct((nv, nz, nr, na), it.dtype)
    pieces = len(red_in)
    kernel = functools.partial(rad_kernel, axis_name="rad", devices=lax.axis_size("rad"), pieces=pieces)
    targets, red_out = pl.pallas_call(
        kernel,
        grid=(nz,),
        in_specs=[big, big, big] + [red_in_spec] * pieces + [mixs, cell, par, edge, big_t, big_t, big_t],
        out_specs=[big_t, red],
        out_shape=[out, jax.ShapeDtypeStruct((nv, nz, 3, 2, na), it.dtype)],
        scratch_shapes=[pltpu.VMEM((3, 2 * pieces, nr), it.dtype)],
    )(it, ia, ib, *red_in, mix_mid, cell_rad, visc_rad, edges, rad_a, rad_b, sides)
    return targets, red_out


def rad_solve(targets, sides):
    nv, nz, nr, na = targets.shape
    big_t = pl.BlockSpec((nv, 1, nr, na), lambda z: (0, z, 0, 0))
    return pl.pallas_call(
        rad_solve_kernel,
        grid=(nz,),
        in_specs=[big_t, big_t],
        out_specs=big_t,
        out_shape=jax.ShapeDtypeStruct(targets.shape, targets.dtype),
    )(targets, sides)


def out_sweep(it, ia, ib, red_in, mix_out):
    nv, nz, nr, na = it.shape
    big_t = pl.BlockSpec((nv, 1, nr, na), lambda z: (0, z, 0, 0))
    big = pl.BlockSpec((nv, 1, na, nr), lambda z: (0, z, 0, 0))
    red_in_spec = pl.BlockSpec((nv, 1) + red_in[0].shape[2:], lambda z: (0, z, 0, 0, 0))
    mixs = pl.BlockSpec((nv, nv, nr), lambda z: (0, 0, 0))
    pieces = len(red_in)
    return pl.pallas_call(
        functools.partial(out_kernel, pieces=pieces),
        grid=(nz,),
        in_specs=[big_t, big_t, big_t] + [red_in_spec] * pieces + [mixs],
        out_specs=big,
        out_shape=jax.ShapeDtypeStruct((nv, nz, na, nr), it.dtype),
        scratch_shapes=[pltpu.VMEM((3, 2 * pieces, na), it.dtype)],
    )(it, ia, ib, *red_in, mix_out)


def gathered(block, axis_name):
    count = lax.axis_size(axis_name)
    received = [block]
    for offset in range(1, count):
        pairs = [((i + offset) % count, i) for i in range(count)]
        received.append(lax.ppermute(block, axis_name, pairs))
    return received


def neighbour_planes(block, axis_name):
    count = lax.axis_size(axis_name)
    if count == 2:
        return lax.ppermute(block, axis_name, [(0, 1), (1, 0)])
    padded = with_halo(block, ((axis_name, 1),), 1, False)
    return padded[:, :-2] + padded[:, 2:]


def mix(matrix, values):
    mixed_rows = []
    for out_var in range(values.shape[0]):
        summed = values[out_var]
        for in_var in range(values.shape[0]):
            summed = summed + matrix[out_var, in_var][None, None, :] * values[in_var]
        mixed_rows.append(summed)
    return jnp.stack(mixed_rows)


def per_device(
    flow_state,
    source,
    cell_az,
    cell_rad,
    visc_az,
    beta_az,
    visc_rad,
    axial_diff,
    mix_in,
    mix_mid,
    mix_out,
):
    rad_cells = flow_state.shape[3]
    nb = neighbour_planes(flow_state, "ax")
    rad_a, rad_b, sides, rad_edges = rad_pre(cell_rad, visc_rad, flow_state.shape[0])
    it, ia, ib, red = az_sweep(flow_state, nb, source, cell_az, visc_az, beta_az, axial_diff, mix_in, rad_edges)
    red = gathered(red, "az")
    targets, red = rad_sweep(it, ia, ib, red, mix_mid, cell_rad, visc_rad, rad_edges, rad_a, rad_b, sides)
    red = gathered(red, "rad")
    it = rad_solve(targets, sides)
    ia, ib = rad_a, rad_b
    return out_sweep(it, ia, ib, red, mix_out)


def solution(mesh):
    in_specs = (
        P(None, "ax", "az", "rad"),
        P(None, "ax", "az", "rad"),
        P("ax", "az", "rad"),
        P("ax", "az", "rad"),
        P(None, "rad"),
        P(None, "rad"),
        P(),
        P(None, "rad"),
        P(None, None, "rad"),
        P(None, None, "rad"),
        P(None, None, "rad"),
    )
    out_specs = P(None, "ax", "az", "rad")
    return jax.shard_map(
        per_device, mesh=mesh, in_specs=in_specs, out_specs=out_specs, check_vma=False
    )
```

```python
import jax
import jax.numpy as jnp
from jax import lax
from jax.experimental import pallas as pl
from jax.experimental.pallas import tpu as pltpu
from jax.sharding import PartitionSpec as P
import functools


def with_halo(block, sides, width, periodic):
    for axis, dim in sides:
        count = lax.axis_size(axis)
        forward = [(i, i + 1) for i in range(count - 1)]
        if periodic:
            forward.append((count - 1, 0))
        backward = [(target, source) for source, target in forward]
        low = lax.ppermute(
            lax.slice_in_dim(block, block.shape[dim] - width, None, axis=dim), axis, forward
        )
        high = lax.ppermute(lax.slice_in_dim(block, 0, width, axis=dim), axis, backward)
        block = jnp.concatenate([low, block, high], axis=dim)
    return block


def shifted(values, offset, axis, periodic):
    if periodic:
        return jnp.roll(values, offset, axis)
    length = values.shape[axis]
    zero_shape = list(values.shape)
    zero_shape[axis] = abs(offset)
    zeros = jnp.zeros(zero_shape, values.dtype)
    if offset > 0:
        kept = lax.slice_in_dim(values, 0, length - offset, axis=axis)
        return jnp.concatenate([zeros, kept], axis=axis)
    kept = lax.slice_in_dim(values, -offset, length, axis=axis)
    return jnp.concatenate([kept, zeros], axis=axis)


def cyclic_reduce(lower, upper, rhs, axis, periodic, steps_below):
    stride = 1
    while stride < steps_below:
        ll, ul = shifted(lower, stride, axis, periodic), shifted(upper, stride, axis, periodic)
        lr, ur = shifted(lower, -stride, axis, periodic), shifted(upper, -stride, axis, periodic)
        inv = 1.0 / (1.0 - lower * ul - upper * lr)
        rhs = [
            (r - lower * shifted(r, stride, axis, periodic) - upper * shifted(r, -stride, axis, periodic)) * inv
            for r in rhs
        ]
        lower, upper = -lower * ll * inv, -upper * ur * inv
        stride = stride * 2
    return lower, upper, rhs


def interior(lower, upper):
    length = lower.shape[0]
    idx = lax.broadcasted_iota(jnp.int32, lower.shape, 0)
    edge = (idx == 0) | (idx == length - 1)
    second = idx == 1
    penult = idx == length - 2
    zero = jnp.zeros_like(lower)
    il = jnp.where(edge | second, zero, lower)
    iu = jnp.where(edge | penult, zero, upper)
    return il, iu, jnp.where(edge, zero, 1.0), jnp.where(second, lower, zero), jnp.where(penult, upper, zero)


def pcr_levels(il, iu, rhs):
    length = il.shape[0]
    stride = 1
    while stride < length - 2:
        back = length - stride
        ll, ul = pltpu.roll(il, stride, 0), pltpu.roll(iu, stride, 0)
        lr, ur = pltpu.roll(il, back, 0), pltpu.roll(iu, back, 0)
        inv = 1.0 / (1.0 - il * ul - iu * lr)
        rhs = [(r - il * pltpu.roll(r, stride, 0) - iu * pltpu.roll(r, back, 0)) * inv for r in rhs]
        flip = -inv
        il, iu = il * ll * flip, iu * ur * flip
        stride = stride * 2
    return rhs


def interface_rows(lower, upper, t0, te, t1, t2, a1, b1, a2, b2):
    length = lower.shape[0]
    l0, u0 = lower[0:1], upper[0:1]
    le, ue = lower[length - 1 :], upper[length - 1 :]
    inv_f = 1.0 / (1.0 - u0 * a1)
    inv_e = 1.0 / (1.0 - le * b2)
    return (
        (l0 * inv_f, -le * a2 * inv_e),
        (-u0 * b1 * inv_f, ue * inv_e),
        ((t0 - u0 * t1) * inv_f, (te - le * t2) * inv_e),
    )


def reduce_block(lower, upper, target):
    length = lower.shape[0]
    il, iu, keep, a_init, b_init = interior(lower, upper)
    it, ia, ib = pcr_levels(il, iu, [target * keep, a_init, b_init])
    n2 = length - 2
    rows = interface_rows(
        lower, upper, target[0:1], target[length - 1 :], it[1:2], it[n2 : n2 + 1],
        ia[1:2], ib[1:2], ia[n2 : n2 + 1], ib[n2 : n2 + 1],
    )
    return it, ia, ib, rows


def store_rows(red_ref, v, rows):
    for q, pair in enumerate(rows):
        for i, value in enumerate(pair):
            red_ref[v, 0, q, i : i + 1, :] = value


def reduced_ends(red_refs, rows_ref, v):
    for k, ref in enumerate(red_refs):
        rows_ref[:, 2 * k : 2 * k + 2, :] = ref[v, 0]
    lower, upper, target = rows_ref[0], rows_ref[1], rows_ref[2]
    length = lower.shape[0]
    stride = 1
    while stride < length:
        back = length - stride
        ll, ul = pltpu.roll(lower, stride, 0), pltpu.roll(upper, stride, 0)
        lr, ur = pltpu.roll(lower, back, 0), pltpu.roll(upper, back, 0)
        inv = 1.0 / (1.0 - lower * ul - upper * lr)
        target = (target - lower * pltpu.roll(target, stride, 0) - upper * pltpu.roll(target, back, 0)) * inv
        lower, upper = -lower * ll * inv, -upper * ur * inv
        stride = stride * 2
    ends = target / (1.0 + lower + upper)
    return ends[0:1], ends[1:2]


def back_substitute(it, ia, ib, first, last, offset=0, length=None):
    length = it.shape[0] if length is None else length
    idx = lax.broadcasted_iota(jnp.int32, it.shape, 0) + offset
    inner = it - ia * first - ib * last
    return jnp.where(idx == 0, first, jnp.where(idx == length - 1, last, inner))


def mixed(mix_ref, values):
    out = []
    for v in range(len(values)):
        summed = values[v]
        for w in range(len(values)):
            summed = summed + mix_ref[v, w : w + 1, :] * values[w]
        out.append(summed)
    return out


def az_coefficients(cell, visc_ref, beta_ref, v):
    coupling = visc_ref[v : v + 1, :] * cell
    scale = -1.0 / (1.0 + 2.0 * coupling)
    tilt = beta_ref[v : v + 1, :]
    lower = coupling * (1.0 + tilt) * scale
    upper = coupling * (1.0 - tilt) * scale
    return lower, upper, scale


def az_local_kernel(fs_ref, src_ref, cell_ref, visc_ref, beta_ref, diff_ref, mix_ref, ot_ref, oa_ref, ob_ref, edge_ref):
    count = fs_ref.shape[0]
    explicit = [src_ref[w, 0] + diff_ref[w : w + 1, :] * (-2.0 * fs_ref[w, 0]) for w in range(count)]
    section_one = mixed(mix_ref, explicit)
    cell = cell_ref[0]
    for v in range(count):
        lower, upper, scale = az_coefficients(cell, visc_ref, beta_ref, v)
        target = section_one[v] * -scale
        length = lower.shape[0]
        il, iu, keep, a_init, b_init = interior(lower, upper)
        it, ia, ib = pcr_levels(il, iu, [target * keep, a_init, b_init])
        ot_ref[v, 0] = it
        oa_ref[v, 0] = ia
        ob_ref[v, 0] = ib
        n2 = length - 2
        for k, value in enumerate(
            (target[0:1], target[length - 1 :], ia[1:2], ib[1:2], ia[n2 : n2 + 1], ib[n2 : n2 + 1])
        ):
            edge_ref[v, 0, k : k + 1, :] = value


def az_plane_kernel(nb_ref, cell_ref, visc_ref, beta_ref, diff_ref, mix_ref, it_in_ref, edge_ref, order_ref, ot_ref, red_ref):
    count = nb_ref.shape[0]
    explicit = [diff_ref[w : w + 1, :] * nb_ref[w, 0] for w in range(count)]
    section_one = mixed(mix_ref, explicit)
    cell = cell_ref[0]
    for v in range(count):
        lower, upper, scale = az_coefficients(cell, visc_ref, beta_ref, v)
        target = section_one[v] * -scale
        length = lower.shape[0]
        il, iu, keep, _, _ = interior(lower, upper)
        (it,) = pcr_levels(il, iu, [target * keep])
        it = it_in_ref[v, 0] + it
        ot_ref[v, 0] = it
        edge = edge_ref[v, 0]
        n2 = length - 2
        rows = interface_rows(
            lower, upper, edge[0:1] + target[0:1], edge[1:2] + target[length - 1 :], it[1:2], it[n2 : n2 + 1],
            edge[2:3], edge[3:4], edge[4:5], edge[5:6],
        )
        store_rows(red_ref, v, rows)


def rad_side(cell, visc, v):
    coupling = visc[v : v + 1, :] * cell
    scale = 1.0 / (1.0 + 2.0 * coupling)
    return -coupling * scale, scale


def local_visc(visc_ref, axis_name, cells):
    place = lax.axis_index(axis_name)
    return visc_ref[:, pl.ds(pl.multiple_of(place * cells, cells), cells)]


def rad_pre_kernel(cell_ref, visc_ref, oa_ref, ob_ref, edge_ref, *, axis_name):
    count = oa_ref.shape[0]
    cells = cell_ref.shape[2]
    visc = local_visc(visc_ref, axis_name, cells)
    cell = cell_ref[0]
    for v in range(count):
        side, _ = rad_side(cell, visc, v)
        side = side.T
        length = side.shape[0]
        il, iu, _, a_init, b_init = interior(side, side)
        ia, ib = pcr_levels(il, iu, [a_init, b_init])
        oa_ref[v, 0] = ia
        ob_ref[v, 0] = ib
        n2 = length - 2
        for k, value in enumerate((ia[1:2], ib[1:2], ia[n2 : n2 + 1], ib[n2 : n2 + 1])):
            edge_ref[v, 0, k : k + 1, :] = value


def rad_kernel(*refs, axis_name, devices, pieces):
    it_ref, ia_ref, ib_ref = refs[:3]
    red_in = refs[3 : 3 + pieces]
    mix_ref, cell_ref, visc_ref, edge_ref, ot_ref, red_ref, rows_ref = refs[3 + pieces :]
    count = it_ref.shape[0]
    cells = it_ref.shape[3]
    place = lax.axis_index(axis_name)
    visc = local_visc(visc_ref, axis_name, cells)
    solved = []
    for w in range(count):
        first, last = reduced_ends(red_in, rows_ref, w)
        solved.append(back_substitute(it_ref[w, 0], ia_ref[w, 0], ib_ref[w, 0], first, last))
    section_three = mixed(mix_ref, solved)
    cell = cell_ref[0]
    for v in range(count):
        side, scale = rad_side(cell, visc, v)
        side = side.T
        target = (section_three[v] * scale).T
        length = side.shape[0]
        il, iu, keep, _, _ = interior(side, side)
        (it,) = pcr_levels(il, iu, [target * keep])
        edge = edge_ref[v, 0]
        n2 = length - 2
        (lf, le), (uf, ue), trow = interface_rows(
            side, side, target[0:1], target[length - 1 :], it[1:2], it[n2 : n2 + 1],
            edge[0:1], edge[1:2], edge[2:3], edge[3:4],
        )
        lf = jnp.where(place == 0, jnp.zeros_like(lf), lf)
        ue = jnp.where(place == devices - 1, jnp.zeros_like(ue), ue)
        store_rows(red_ref, v, ((lf, le), (uf, ue), trow))
        ot_ref[v, 0] = it


def out_kernel(*refs, pieces, length):
    it_ref, ia_ref, ib_ref = refs[:3]
    red_in = refs[3 : 3 + pieces]
    mix_ref, out_ref, rows_ref = refs[3 + pieces :]
    count = it_ref.shape[0]
    offset = pl.program_id(1) * it_ref.shape[2]
    solved = []
    for w in range(count):
        first, last = reduced_ends(red_in, rows_ref, w)
        solved.append(back_substitute(it_ref[w, 0], ia_ref[w, 0], ib_ref[w, 0], first, last, offset, length).T)
    for v, value in enumerate(mixed(mix_ref, solved)):
        out_ref[v, 0] = value


def az_sweep(flow_state, nb, source, cell_az, visc_az, beta_az, axial_diff, mix_in, order):
    nv, nz, na, nr = flow_state.shape
    chunk = 128 if nr % 128 == 0 else nr
    grid = (nz, nr // chunk)
    big = pl.BlockSpec((nv, 1, na, chunk), lambda z, c: (0, z, 0, c))
    cell = pl.BlockSpec((1, na, chunk), lambda z, c: (z, 0, c))
    par = pl.BlockSpec((nv, chunk), lambda z, c: (0, c))
    mixs = pl.BlockSpec((nv, nv, chunk), lambda z, c: (0, 0, c))
    edge = pl.BlockSpec((nv, 1, 6, chunk), lambda z, c: (0, z, 0, c))
    red = pl.BlockSpec((nv, 1, 3, 2, chunk), lambda z, c: (0, z, 0, 0, c))
    out = jax.ShapeDtypeStruct(flow_state.shape, flow_state.dtype)
    it, ia, ib, edges = pl.pallas_call(
        az_local_kernel,
        grid=grid,
        in_specs=[big, big, cell, par, par, par, mixs],
        out_specs=[big, big, big, edge],
        out_shape=[out, out, out, jax.ShapeDtypeStruct((nv, nz, 6, nr), flow_state.dtype)],
    )(flow_state, source, cell_az, visc_az, beta_az, axial_diff, mix_in)
    it, red = pl.pallas_call(
        az_plane_kernel,
        grid=grid,
        in_specs=[big, cell, par, par, par, mixs, big, edge, pl.BlockSpec(memory_space=pl.ANY)],
        out_specs=[big, red],
        out_shape=[out, jax.ShapeDtypeStruct((nv, nz, 3, 2, nr), flow_state.dtype)],
        input_output_aliases={6: 0},
    )(nb, cell_az, visc_az, beta_az, axial_diff, mix_in, it, edges, order)
    return it, ia, ib, red


def rad_pre(cell_rad, visc_rad, nv):
    nz, na, nr = cell_rad.shape
    big_t = pl.BlockSpec((nv, 1, nr, na), lambda z: (0, z, 0, 0))
    cell = pl.BlockSpec((1, na, nr), lambda z: (z, 0, 0))
    par = pl.BlockSpec(visc_rad.shape, lambda z: (0, 0))
    edge = pl.BlockSpec((nv, 1, 4, na), lambda z: (0, z, 0, 0))
    out = jax.ShapeDtypeStruct((nv, nz, nr, na), cell_rad.dtype)
    return pl.pallas_call(
        functools.partial(rad_pre_kernel, axis_name="rad"),
        grid=(nz,),
        in_specs=[cell, par],
        out_specs=[big_t, big_t, edge],
        out_shape=[out, out, jax.ShapeDtypeStruct((nv, nz, 4, na), cell_rad.dtype)],
    )(cell_rad, visc_rad)


def rad_sweep(it, ia, ib, red_in, mix_mid, cell_rad, visc_rad, edges):
    nv, nz, na, nr = it.shape
    big = pl.BlockSpec((nv, 1, na, nr), lambda z: (0, z, 0, 0))
    big_t = pl.BlockSpec((nv, 1, nr, na), lambda z: (0, z, 0, 0))
    red_in_spec = pl.BlockSpec((nv, 1) + red_in[0].shape[2:], lambda z: (0, z, 0, 0, 0))
    mixs = pl.BlockSpec((nv, nv, nr), lambda z: (0, 0, 0))
    cell = pl.BlockSpec((1, na, nr), lambda z: (z, 0, 0))
    par = pl.BlockSpec(visc_rad.shape, lambda z: (0, 0))
    edge = pl.BlockSpec((nv, 1, 4, na), lambda z: (0, z, 0, 0))
    red = pl.BlockSpec((nv, 1, 3, 2, na), lambda z: (0, z, 0, 0, 0))
    out = jax.ShapeDtypeStruct((nv, nz, nr, na), it.dtype)
    pieces = len(red_in)
    kernel = functools.partial(rad_kernel, axis_name="rad", devices=lax.axis_size("rad"), pieces=pieces)
    return pl.pallas_call(
        kernel,
        grid=(nz,),
        in_specs=[big, big, big] + [red_in_spec] * pieces + [mixs, cell, par, edge],
        out_specs=[big_t, red],
        out_shape=[out, jax.ShapeDtypeStruct((nv, nz, 3, 2, na), it.dtype)],
        scratch_shapes=[pltpu.VMEM((3, 2 * pieces, nr), it.dtype)],
    )(it, ia, ib, *red_in, mix_mid, cell_rad, visc_rad, edges)


def out_sweep(it, ia, ib, red_in, mix_out):
    nv, nz, nr, na = it.shape
    chunk = 128 if nr % 128 == 0 else nr
    big_t = pl.BlockSpec((nv, 1, chunk, na), lambda z, c: (0, z, c, 0))
    big = pl.BlockSpec((nv, 1, na, chunk), lambda z, c: (0, z, 0, c))
    red_in_spec = pl.BlockSpec((nv, 1) + red_in[0].shape[2:], lambda z, c: (0, z, 0, 0, 0))
    mixs = pl.BlockSpec((nv, nv, chunk), lambda z, c: (0, 0, c))
    pieces = len(red_in)
    return pl.pallas_call(
        functools.partial(out_kernel, pieces=pieces, length=nr),
        grid=(nz, nr // chunk),
        in_specs=[big_t, big_t, big_t] + [red_in_spec] * pieces + [mixs],
        out_specs=big,
        out_shape=jax.ShapeDtypeStruct((nv, nz, na, nr), it.dtype),
        scratch_shapes=[pltpu.VMEM((3, 2 * pieces, na), it.dtype)],
    )(it, ia, ib, *red_in, mix_out)


def gathered(block, axis_name):
    count = lax.axis_size(axis_name)
    received = [block]
    for offset in range(1, count):
        pairs = [((i + offset) % count, i) for i in range(count)]
        received.append(lax.ppermute(block, axis_name, pairs))
    return received


def neighbour_planes(block, axis_name):
    count = lax.axis_size(axis_name)
    if count == 2:
        return lax.ppermute(block, axis_name, [(0, 1), (1, 0)])
    padded = with_halo(block, ((axis_name, 1),), 1, False)
    return padded[:, :-2] + padded[:, 2:]


def mix(matrix, values):
    mixed_rows = []
    for out_var in range(values.shape[0]):
        summed = values[out_var]
        for in_var in range(values.shape[0]):
            summed = summed + matrix[out_var, in_var][None, None, :] * values[in_var]
        mixed_rows.append(summed)
    return jnp.stack(mixed_rows)


def per_device(
    flow_state,
    source,
    cell_az,
    cell_rad,
    visc_az,
    beta_az,
    visc_rad,
    axial_diff,
    mix_in,
    mix_mid,
    mix_out,
):
    rad_cells = flow_state.shape[3]
    nb = neighbour_planes(flow_state, "ax")
    rad_a, rad_b, rad_edges = rad_pre(cell_rad, visc_rad, flow_state.shape[0])
    it, ia, ib, red = az_sweep(flow_state, nb, source, cell_az, visc_az, beta_az, axial_diff, mix_in, rad_edges)
    red = gathered(red, "az")
    it, red = rad_sweep(it, ia, ib, red, mix_mid, cell_rad, visc_rad, rad_edges)
    ia, ib = rad_a, rad_b
    red = gathered(red, "rad")
    return out_sweep(it, ia, ib, red, mix_out)


def solution(mesh):
    in_specs = (
        P(None, "ax", "az", "rad"),
        P(None, "ax", "az", "rad"),
        P("ax", "az", "rad"),
        P("ax", "az", "rad"),
        P(None, "rad"),
        P(None, "rad"),
        P(),
        P(None, "rad"),
        P(None, None, "rad"),
        P(None, None, "rad"),
        P(None, None, "rad"),
    )
    out_specs = P(None, "ax", "az", "rad")
    return jax.shard_map(
        per_device, mesh=mesh, in_specs=in_specs, out_specs=out_specs, check_vma=False
    )
```

```python
import jax
import jax.numpy as jnp
from jax import lax
from jax.experimental import pallas as pl
from jax.experimental.pallas import tpu as pltpu
from jax.sharding import PartitionSpec as P
import functools


def with_halo(block, sides, width, periodic):
    for axis, dim in sides:
        count = lax.axis_size(axis)
        forward = [(i, i + 1) for i in range(count - 1)]
        if periodic:
            forward.append((count - 1, 0))
        backward = [(target, source) for source, target in forward]
        low = lax.ppermute(
            lax.slice_in_dim(block, block.shape[dim] - width, None, axis=dim), axis, forward
        )
        high = lax.ppermute(lax.slice_in_dim(block, 0, width, axis=dim), axis, backward)
        block = jnp.concatenate([low, block, high], axis=dim)
    return block


def shifted(values, offset, axis, periodic):
    if periodic:
        return jnp.roll(values, offset, axis)
    length = values.shape[axis]
    zero_shape = list(values.shape)
    zero_shape[axis] = abs(offset)
    zeros = jnp.zeros(zero_shape, values.dtype)
    if offset > 0:
        kept = lax.slice_in_dim(values, 0, length - offset, axis=axis)
        return jnp.concatenate([zeros, kept], axis=axis)
    kept = lax.slice_in_dim(values, -offset, length, axis=axis)
    return jnp.concatenate([kept, zeros], axis=axis)


def cyclic_reduce(lower, upper, rhs, axis, periodic, steps_below):
    stride = 1
    while stride < steps_below:
        ll, ul = shifted(lower, stride, axis, periodic), shifted(upper, stride, axis, periodic)
        lr, ur = shifted(lower, -stride, axis, periodic), shifted(upper, -stride, axis, periodic)
        inv = 1.0 / (1.0 - lower * ul - upper * lr)
        rhs = [
            (r - lower * shifted(r, stride, axis, periodic) - upper * shifted(r, -stride, axis, periodic)) * inv
            for r in rhs
        ]
        lower, upper = -lower * ll * inv, -upper * ur * inv
        stride = stride * 2
    return lower, upper, rhs


def interior(lower, upper):
    length = lower.shape[0]
    idx = lax.broadcasted_iota(jnp.int32, lower.shape, 0)
    edge = (idx == 0) | (idx == length - 1)
    second = idx == 1
    penult = idx == length - 2
    zero = jnp.zeros_like(lower)
    il = jnp.where(edge | second, zero, lower)
    iu = jnp.where(edge | penult, zero, upper)
    return il, iu, jnp.where(edge, zero, 1.0), jnp.where(second, lower, zero), jnp.where(penult, upper, zero)


def pcr_levels(il, iu, rhs):
    length = il.shape[0]
    stride = 1
    while stride < length - 2:
        back = length - stride
        ll, ul = pltpu.roll(il, stride, 0), pltpu.roll(iu, stride, 0)
        lr, ur = pltpu.roll(il, back, 0), pltpu.roll(iu, back, 0)
        inv = 1.0 / (1.0 - il * ul - iu * lr)
        rhs = [(r - il * pltpu.roll(r, stride, 0) - iu * pltpu.roll(r, back, 0)) * inv for r in rhs]
        flip = -inv
        il, iu = il * ll * flip, iu * ur * flip
        stride = stride * 2
    return rhs


def interface_rows(lower, upper, t0, te, t1, t2, a1, b1, a2, b2):
    length = lower.shape[0]
    l0, u0 = lower[0:1], upper[0:1]
    le, ue = lower[length - 1 :], upper[length - 1 :]
    inv_f = 1.0 / (1.0 - u0 * a1)
    inv_e = 1.0 / (1.0 - le * b2)
    return (
        (l0 * inv_f, -le * a2 * inv_e),
        (-u0 * b1 * inv_f, ue * inv_e),
        ((t0 - u0 * t1) * inv_f, (te - le * t2) * inv_e),
    )


def reduce_block(lower, upper, target):
    length = lower.shape[0]
    il, iu, keep, a_init, b_init = interior(lower, upper)
    it, ia, ib = pcr_levels(il, iu, [target * keep, a_init, b_init])
    n2 = length - 2
    rows = interface_rows(
        lower, upper, target[0:1], target[length - 1 :], it[1:2], it[n2 : n2 + 1],
        ia[1:2], ib[1:2], ia[n2 : n2 + 1], ib[n2 : n2 + 1],
    )
    return it, ia, ib, rows


def store_rows(red_ref, v, rows):
    for q, pair in enumerate(rows):
        for i, value in enumerate(pair):
            red_ref[v, 0, q, i : i + 1, :] = value


def reduced_ends(red_refs, rows_ref, v):
    for k, ref in enumerate(red_refs):
        rows_ref[:, 2 * k : 2 * k + 2, :] = ref[v, 0]

    lower, upper, target = rows_ref[0], rows_ref[1], rows_ref[2]
    length = lower.shape[0]
    stride = 1
    while stride < length:
        back = length - stride
        ll, ul = pltpu.roll(lower, stride, 0), pltpu.roll(upper, stride, 0)
        lr, ur = pltpu.roll(lower, back, 0), pltpu.roll(upper, back, 0)
        inv = 1.0 / (1.0 - lower * ul - upper * lr)
        target = (target - lower * pltpu.roll(target, stride, 0) - upper * pltpu.roll(target, back, 0)) * inv
        lower, upper = -lower * ll * inv, -upper * ur * inv
        stride = stride * 2
    ends = target / (1.0 + lower + upper)
    return ends[0:1], ends[1:2]


def back_substitute(it, ia, ib, first, last, offset=0, length=None):
    length = it.shape[0] if length is None else length
    idx = lax.broadcasted_iota(jnp.int32, it.shape, 0) + offset
    inner = it - ia * first - ib * last
    return jnp.where(idx == 0, first, jnp.where(idx == length - 1, last, inner))


def mixed(mix_ref, values):
    out = []
    for v in range(len(values)):
        summed = values[v]
        for w in range(len(values)):
            summed = summed + mix_ref[v, w : w + 1, :] * values[w]
        out.append(summed)
    return out


def az_coefficients(cell, visc_ref, beta_ref, v):
    coupling = visc_ref[v : v + 1, :] * cell
    scale = -1.0 / (1.0 + 2.0 * coupling)
    tilt = beta_ref[v : v + 1, :]
    lower = coupling * (1.0 + tilt) * scale
    upper = coupling * (1.0 - tilt) * scale
    return lower, upper, scale


def az_local_kernel(fs_ref, src_ref, cell_ref, visc_ref, beta_ref, diff_ref, mix_ref, ot_ref, oa_ref, ob_ref, edge_ref):
    count = fs_ref.shape[0]
    explicit = [src_ref[w, 0] + diff_ref[w : w + 1, :] * (-2.0 * fs_ref[w, 0]) for w in range(count)]
    section_one = mixed(mix_ref, explicit)
    cell = cell_ref[0]
    for v in range(count):
        lower, upper, scale = az_coefficients(cell, visc_ref, beta_ref, v)
        target = section_one[v] * -scale
        length = lower.shape[0]
        il, iu, keep, a_init, b_init = interior(lower, upper)
        it, ia, ib = pcr_levels(il, iu, [target * keep, a_init, b_init])
        ot_ref[v, 0] = it
        oa_ref[v, 0] = ia
        ob_ref[v, 0] = ib
        n2 = length - 2
        for k, value in enumerate(
            (target[0:1], target[length - 1 :], ia[1:2], ib[1:2], ia[n2 : n2 + 1], ib[n2 : n2 + 1])
        ):
            edge_ref[v, 0, k : k + 1, :] = value


def az_plane_kernel(nb_ref, cell_ref, visc_ref, beta_ref, diff_ref, mix_ref, it_in_ref, edge_ref, order_ref, ot_ref, red_ref):
    count = nb_ref.shape[0]
    explicit = [diff_ref[w : w + 1, :] * nb_ref[w, 0] for w in range(count)]
    section_one = mixed(mix_ref, explicit)
    cell = cell_ref[0]
    for v in range(count):
        lower, upper, scale = az_coefficients(cell, visc_ref, beta_ref, v)
        target = section_one[v] * -scale
        length = lower.shape[0]
        il, iu, keep, _, _ = interior(lower, upper)
        (it,) = pcr_levels(il, iu, [target * keep])
        it = it_in_ref[v, 0] + it
        ot_ref[v, 0] = it
        edge = edge_ref[v, 0]
        n2 = length - 2
        rows = interface_rows(
            lower, upper, edge[0:1] + target[0:1], edge[1:2] + target[length - 1 :], it[1:2], it[n2 : n2 + 1],
            edge[2:3], edge[3:4], edge[4:5], edge[5:6],
        )
        store_rows(red_ref, v, rows)


def rad_side(cell, visc, v):
    coupling = visc[v : v + 1, :] * cell
    scale = 1.0 / (1.0 + 2.0 * coupling)
    return -coupling * scale, scale


def local_visc(visc_ref, axis_name, cells):
    place = lax.axis_index(axis_name)
    return visc_ref[:, pl.ds(pl.multiple_of(place * cells, cells), cells)]


def rad_pre_kernel(cell_ref, visc_ref, oa_ref, ob_ref, edge_ref, *, axis_name):
    count = oa_ref.shape[0]
    cells = cell_ref.shape[2]
    visc = local_visc(visc_ref, axis_name, cells)
    cell = cell_ref[0]
    for v in range(count):
        side, _ = rad_side(cell, visc, v)
        side = side.T
        length = side.shape[0]
        il, iu, _, a_init, b_init = interior(side, side)
        ia, ib = pcr_levels(il, iu, [a_init, b_init])
        oa_ref[v, 0] = ia
        ob_ref[v, 0] = ib
        n2 = length - 2
        for k, value in enumerate((ia[1:2], ib[1:2], ia[n2 : n2 + 1], ib[n2 : n2 + 1])):
            edge_ref[v, 0, k : k + 1, :] = value


def rad_kernel(*refs, axis_name, devices, pieces):
    it_ref, ia_ref, ib_ref = refs[:3]
    red_in = refs[3 : 3 + pieces]
    mix_ref, cell_ref, visc_ref, edge_ref, ot_ref, red_ref, rows_ref, acc_ref = refs[3 + pieces :]
    count = mix_ref.shape[0]
    cells = it_ref.shape[3]
    w = pl.program_id(1)
    first, last = reduced_ends(red_in, rows_ref, w)
    solved = back_substitute(it_ref[0, 0], ia_ref[0, 0], ib_ref[0, 0], first, last)

    @pl.when(w == 0)
    def _():
        acc_ref[...] = jnp.zeros_like(acc_ref)

    for v in range(count):
        acc_ref[v] = acc_ref[v] + mix_ref[v, pl.ds(w, 1), :] * solved
    acc_ref[w] = acc_ref[w] + solved

    @pl.when(w == count - 1)
    def _():
        rad_finish(acc_ref, cell_ref, visc_ref, edge_ref, ot_ref, red_ref, axis_name, devices)


def rad_finish(acc_ref, cell_ref, visc_ref, edge_ref, ot_ref, red_ref, axis_name, devices):
    count = acc_ref.shape[0]
    cells = acc_ref.shape[2]
    place = lax.axis_index(axis_name)
    visc = local_visc(visc_ref, axis_name, cells)
    section_three = [acc_ref[v] for v in range(count)]
    cell = cell_ref[0]
    for v in range(count):
        side, scale = rad_side(cell, visc, v)
        side = side.T
        target = (section_three[v] * scale).T
        length = side.shape[0]
        il, iu, keep, _, _ = interior(side, side)
        (it,) = pcr_levels(il, iu, [target * keep])
        edge = edge_ref[v, 0]
        n2 = length - 2
        (lf, le), (uf, ue), trow = interface_rows(
            side, side, target[0:1], target[length - 1 :], it[1:2], it[n2 : n2 + 1],
            edge[0:1], edge[1:2], edge[2:3], edge[3:4],
        )
        lf = jnp.where(place == 0, jnp.zeros_like(lf), lf)
        ue = jnp.where(place == devices - 1, jnp.zeros_like(ue), ue)
        store_rows(red_ref, v, ((lf, le), (uf, ue), trow))
        ot_ref[v, 0] = it


def out_kernel(*refs, pieces, length):
    it_ref, ia_ref, ib_ref = refs[:3]
    red_in = refs[3 : 3 + pieces]
    mix_ref, out_ref, rows_ref = refs[3 + pieces :]
    count = it_ref.shape[0]
    offset = pl.program_id(1) * it_ref.shape[2]
    solved = []
    for w in range(count):
        first, last = reduced_ends(red_in, rows_ref, w)
        solved.append(back_substitute(it_ref[w, 0], ia_ref[w, 0], ib_ref[w, 0], first, last, offset, length).T)
    for v, value in enumerate(mixed(mix_ref, solved)):
        out_ref[v, 0] = value


def az_sweep(flow_state, nb, source, cell_az, visc_az, beta_az, axial_diff, mix_in, order):
    nv, nz, na, nr = flow_state.shape
    chunk = 128 if nr % 128 == 0 else nr
    grid = (nz, nr // chunk)
    big = pl.BlockSpec((nv, 1, na, chunk), lambda z, c: (0, z, 0, c))
    cell = pl.BlockSpec((1, na, chunk), lambda z, c: (z, 0, c))
    par = pl.BlockSpec((nv, chunk), lambda z, c: (0, c))
    mixs = pl.BlockSpec((nv, nv, chunk), lambda z, c: (0, 0, c))
    edge = pl.BlockSpec((nv, 1, 6, chunk), lambda z, c: (0, z, 0, c))
    red = pl.BlockSpec((nv, 1, 3, 2, chunk), lambda z, c: (0, z, 0, 0, c))
    out = jax.ShapeDtypeStruct(flow_state.shape, flow_state.dtype)
    it, ia, ib, edges = pl.pallas_call(
        az_local_kernel,
        grid=grid,
        in_specs=[big, big, cell, par, par, par, mixs],
        out_specs=[big, big, big, edge],
        out_shape=[out, out, out, jax.ShapeDtypeStruct((nv, nz, 6, nr), flow_state.dtype)],
    )(flow_state, source, cell_az, visc_az, beta_az, axial_diff, mix_in)
    it, red = pl.pallas_call(
        az_plane_kernel,
        grid=grid,
        in_specs=[big, cell, par, par, par, mixs, big, edge, pl.BlockSpec(memory_space=pl.ANY)],
        out_specs=[big, red],
        out_shape=[out, jax.ShapeDtypeStruct((nv, nz, 3, 2, nr), flow_state.dtype)],
        input_output_aliases={6: 0},
    )(nb, cell_az, visc_az, beta_az, axial_diff, mix_in, it, edges, order)
    return it, ia, ib, red


def rad_pre(cell_rad, visc_rad, nv):
    nz, na, nr = cell_rad.shape
    big_t = pl.BlockSpec((nv, 1, nr, na), lambda z: (0, z, 0, 0))
    cell = pl.BlockSpec((1, na, nr), lambda z: (z, 0, 0))
    par = pl.BlockSpec(visc_rad.shape, lambda z: (0, 0))
    edge = pl.BlockSpec((nv, 1, 4, na), lambda z: (0, z, 0, 0))
    out = jax.ShapeDtypeStruct((nv, nz, nr, na), cell_rad.dtype)
    return pl.pallas_call(
        functools.partial(rad_pre_kernel, axis_name="rad"),
        grid=(nz,),
        in_specs=[cell, par],
        out_specs=[big_t, big_t, edge],
        out_shape=[out, out, jax.ShapeDtypeStruct((nv, nz, 4, na), cell_rad.dtype)],
    )(cell_rad, visc_rad)


def rad_sweep(it, ia, ib, red_in, mix_mid, cell_rad, visc_rad, edges):
    nv, nz, na, nr = it.shape
    one = pl.BlockSpec((1, 1, na, nr), lambda z, w: (w, z, 0, 0))
    big_t = pl.BlockSpec((nv, 1, nr, na), lambda z, w: (0, z, 0, 0))
    red_in_spec = pl.BlockSpec((nv, 1) + red_in[0].shape[2:], lambda z, w: (0, z, 0, 0, 0))
    mixs = pl.BlockSpec((nv, nv, nr), lambda z, w: (0, 0, 0))
    cell = pl.BlockSpec((1, na, nr), lambda z, w: (z, 0, 0))
    par = pl.BlockSpec(visc_rad.shape, lambda z, w: (0, 0))
    edge = pl.BlockSpec((nv, 1, 4, na), lambda z, w: (0, z, 0, 0))
    red = pl.BlockSpec((nv, 1, 3, 2, na), lambda z, w: (0, z, 0, 0, 0))
    out = jax.ShapeDtypeStruct((nv, nz, nr, na), it.dtype)
    pieces = len(red_in)
    kernel = functools.partial(rad_kernel, axis_name="rad", devices=lax.axis_size("rad"), pieces=pieces)
    return pl.pallas_call(
        kernel,
        grid=(nz, nv),
        in_specs=[one, one, one] + [red_in_spec] * pieces + [mixs, cell, par, edge],
        out_specs=[big_t, red],
        out_shape=[out, jax.ShapeDtypeStruct((nv, nz, 3, 2, na), it.dtype)],
        scratch_shapes=[pltpu.VMEM((3, 2 * pieces, nr), it.dtype), pltpu.VMEM((nv, na, nr), it.dtype)],
    )(it, ia, ib, *red_in, mix_mid, cell_rad, visc_rad, edges)


def out_sweep(it, ia, ib, red_in, mix_out):
    nv, nz, nr, na = it.shape
    chunk = 128 if nr % 128 == 0 else nr
    big_t = pl.BlockSpec((nv, 1, chunk, na), lambda z, c: (0, z, c, 0))
    big = pl.BlockSpec((nv, 1, na, chunk), lambda z, c: (0, z, 0, c))
    red_in_spec = pl.BlockSpec((nv, 1) + red_in[0].shape[2:], lambda z, c: (0, z, 0, 0, 0))
    mixs = pl.BlockSpec((nv, nv, chunk), lambda z, c: (0, 0, c))
    pieces = len(red_in)
    return pl.pallas_call(
        functools.partial(out_kernel, pieces=pieces, length=nr),
        grid=(nz, nr // chunk),
        in_specs=[big_t, big_t, big_t] + [red_in_spec] * pieces + [mixs],
        out_specs=big,
        out_shape=jax.ShapeDtypeStruct((nv, nz, na, nr), it.dtype),
        scratch_shapes=[pltpu.VMEM((3, 2 * pieces, na), it.dtype)],
    )(it, ia, ib, *red_in, mix_out)


def gathered(block, axis_name):
    count = lax.axis_size(axis_name)
    received = [block]
    for offset in range(1, count):
        pairs = [((i + offset) % count, i) for i in range(count)]
        received.append(lax.ppermute(block, axis_name, pairs))
    return received


def neighbour_planes(block, axis_name):
    count = lax.axis_size(axis_name)
    if count == 2:
        return lax.ppermute(block, axis_name, [(0, 1), (1, 0)])
    padded = with_halo(block, ((axis_name, 1),), 1, False)
    return padded[:, :-2] + padded[:, 2:]


def mix(matrix, values):
    mixed_rows = []
    for out_var in range(values.shape[0]):
        summed = values[out_var]
        for in_var in range(values.shape[0]):
            summed = summed + matrix[out_var, in_var][None, None, :] * values[in_var]
        mixed_rows.append(summed)
    return jnp.stack(mixed_rows)


def per_device(
    flow_state,
    source,
    cell_az,
    cell_rad,
    visc_az,
    beta_az,
    visc_rad,
    axial_diff,
    mix_in,
    mix_mid,
    mix_out,
):
    rad_cells = flow_state.shape[3]
    nb = neighbour_planes(flow_state, "ax")
    rad_a, rad_b, rad_edges = rad_pre(cell_rad, visc_rad, flow_state.shape[0])
    it, ia, ib, red = az_sweep(flow_state, nb, source, cell_az, visc_az, beta_az, axial_diff, mix_in, rad_edges)
    red = gathered(red, "az")
    it, red = rad_sweep(it, ia, ib, red, mix_mid, cell_rad, visc_rad, rad_edges)
    ia, ib = rad_a, rad_b
    red = gathered(red, "rad")
    return out_sweep(it, ia, ib, red, mix_out)


def solution(mesh):
    in_specs = (
        P(None, "ax", "az", "rad"),
        P(None, "ax", "az", "rad"),
        P("ax", "az", "rad"),
        P("ax", "az", "rad"),
        P(None, "rad"),
        P(None, "rad"),
        P(),
        P(None, "rad"),
        P(None, None, "rad"),
        P(None, None, "rad"),
        P(None, None, "rad"),
    )
    out_specs = P(None, "ax", "az", "rad")
    return jax.shard_map(
        per_device, mesh=mesh, in_specs=in_specs, out_specs=out_specs, check_vma=False
    )
```

```python
import jax
import jax.numpy as jnp
from jax import lax
from jax.experimental import pallas as pl
from jax.experimental.pallas import tpu as pltpu
from jax.sharding import PartitionSpec as P
import functools


def with_halo(block, sides, width, periodic):
    for axis, dim in sides:
        count = lax.axis_size(axis)
        forward = [(i, i + 1) for i in range(count - 1)]
        if periodic:
            forward.append((count - 1, 0))
        backward = [(target, source) for source, target in forward]
        low = lax.ppermute(
            lax.slice_in_dim(block, block.shape[dim] - width, None, axis=dim), axis, forward
        )
        high = lax.ppermute(lax.slice_in_dim(block, 0, width, axis=dim), axis, backward)
        block = jnp.concatenate([low, block, high], axis=dim)
    return block


def shifted(values, offset, axis, periodic):
    if periodic:
        return jnp.roll(values, offset, axis)
    length = values.shape[axis]
    zero_shape = list(values.shape)
    zero_shape[axis] = abs(offset)
    zeros = jnp.zeros(zero_shape, values.dtype)
    if offset > 0:
        kept = lax.slice_in_dim(values, 0, length - offset, axis=axis)
        return jnp.concatenate([zeros, kept], axis=axis)
    kept = lax.slice_in_dim(values, -offset, length, axis=axis)
    return jnp.concatenate([kept, zeros], axis=axis)


def cyclic_reduce(lower, upper, rhs, axis, periodic, steps_below):
    stride = 1
    while stride < steps_below:
        ll, ul = shifted(lower, stride, axis, periodic), shifted(upper, stride, axis, periodic)
        lr, ur = shifted(lower, -stride, axis, periodic), shifted(upper, -stride, axis, periodic)
        inv = 1.0 / (1.0 - lower * ul - upper * lr)
        rhs = [
            (r - lower * shifted(r, stride, axis, periodic) - upper * shifted(r, -stride, axis, periodic)) * inv
            for r in rhs
        ]
        lower, upper = -lower * ll * inv, -upper * ur * inv
        stride = stride * 2
    return lower, upper, rhs


def interior(lower, upper):
    length = lower.shape[0]
    idx = lax.broadcasted_iota(jnp.int32, lower.shape, 0)
    edge = (idx == 0) | (idx == length - 1)
    second = idx == 1
    penult = idx == length - 2
    zero = jnp.zeros_like(lower)
    il = jnp.where(edge | second, zero, lower)
    iu = jnp.where(edge | penult, zero, upper)
    return il, iu, jnp.where(edge, zero, 1.0), jnp.where(second, lower, zero), jnp.where(penult, upper, zero)


def pcr_levels(il, iu, rhs):
    length = il.shape[0]
    stride = 1
    while stride < length - 2:
        back = length - stride
        ll, ul = pltpu.roll(il, stride, 0), pltpu.roll(iu, stride, 0)
        lr, ur = pltpu.roll(il, back, 0), pltpu.roll(iu, back, 0)
        inv = 1.0 / (1.0 - il * ul - iu * lr)
        rhs = [(r - il * pltpu.roll(r, stride, 0) - iu * pltpu.roll(r, back, 0)) * inv for r in rhs]
        flip = -inv
        il, iu = il * ll * flip, iu * ur * flip
        stride = stride * 2
    return rhs


def interface_rows(lower, upper, t0, te, t1, t2, a1, b1, a2, b2):
    length = lower.shape[0]
    l0, u0 = lower[0:1], upper[0:1]
    le, ue = lower[length - 1 :], upper[length - 1 :]
    inv_f = 1.0 / (1.0 - u0 * a1)
    inv_e = 1.0 / (1.0 - le * b2)
    return (
        (l0 * inv_f, -le * a2 * inv_e),
        (-u0 * b1 * inv_f, ue * inv_e),
        ((t0 - u0 * t1) * inv_f, (te - le * t2) * inv_e),
    )


def reduce_block(lower, upper, target):
    length = lower.shape[0]
    il, iu, keep, a_init, b_init = interior(lower, upper)
    it, ia, ib = pcr_levels(il, iu, [target * keep, a_init, b_init])
    n2 = length - 2
    rows = interface_rows(
        lower, upper, target[0:1], target[length - 1 :], it[1:2], it[n2 : n2 + 1],
        ia[1:2], ib[1:2], ia[n2 : n2 + 1], ib[n2 : n2 + 1],
    )
    return it, ia, ib, rows


def store_rows(red_ref, v, rows):
    for q, pair in enumerate(rows):
        for i, value in enumerate(pair):
            red_ref[v, 0, q, i : i + 1, :] = value


def reduced_ends(red_refs, rows_ref, v):
    for k, ref in enumerate(red_refs):
        rows_ref[:, 2 * k : 2 * k + 2, :] = ref[v, 0]
    lower, upper, target = rows_ref[0], rows_ref[1], rows_ref[2]
    length = lower.shape[0]
    stride = 1
    while stride < length:
        back = length - stride
        ll, ul = pltpu.roll(lower, stride, 0), pltpu.roll(upper, stride, 0)
        lr, ur = pltpu.roll(lower, back, 0), pltpu.roll(upper, back, 0)
        inv = 1.0 / (1.0 - lower * ul - upper * lr)
        target = (target - lower * pltpu.roll(target, stride, 0) - upper * pltpu.roll(target, back, 0)) * inv
        lower, upper = -lower * ll * inv, -upper * ur * inv
        stride = stride * 2
    ends = target / (1.0 + lower + upper)
    return ends[0:1], ends[1:2]


def back_substitute(it, ia, ib, first, last, offset=0, length=None):
    length = it.shape[0] if length is None else length
    idx = lax.broadcasted_iota(jnp.int32, it.shape, 0) + offset
    inner = it - ia * first - ib * last
    return jnp.where(idx == 0, first, jnp.where(idx == length - 1, last, inner))


def mixed(mix_ref, values):
    out = []
    for v in range(len(values)):
        summed = values[v]
        for w in range(len(values)):
            summed = summed + mix_ref[v, w : w + 1, :] * values[w]
        out.append(summed)
    return out


def az_coefficients(cell, visc_ref, beta_ref, v):
    coupling = visc_ref[v : v + 1, :] * cell
    scale = -1.0 / (1.0 + 2.0 * coupling)
    tilt = beta_ref[v : v + 1, :]
    lower = coupling * (1.0 + tilt) * scale
    upper = coupling * (1.0 - tilt) * scale
    return lower, upper, scale


def az_local_kernel(fs_ref, src_ref, cell_ref, visc_ref, beta_ref, diff_ref, mix_ref, ot_ref, oa_ref, ob_ref, ol_ref, ou_ref, os_ref, edge_ref):
    count = fs_ref.shape[0]
    explicit = [src_ref[w, 0] + diff_ref[w : w + 1, :] * (-2.0 * fs_ref[w, 0]) for w in range(count)]
    section_one = mixed(mix_ref, explicit)
    cell = cell_ref[0]
    for v in range(count):
        lower, upper, scale = az_coefficients(cell, visc_ref, beta_ref, v)
        target = section_one[v] * -scale
        length = lower.shape[0]
        il, iu, keep, a_init, b_init = interior(lower, upper)
        ol_ref[v, 0] = il
        ou_ref[v, 0] = iu
        os_ref[v, 0] = -scale
        it, ia, ib = pcr_levels(il, iu, [target * keep, a_init, b_init])
        ot_ref[v, 0] = it
        oa_ref[v, 0] = ia
        ob_ref[v, 0] = ib
        n2 = length - 2
        for k, value in enumerate(
            (target[0:1], target[length - 1 :], ia[1:2], ib[1:2], ia[n2 : n2 + 1], ib[n2 : n2 + 1],
             lower[0:1], lower[length - 1 :], upper[0:1], upper[length - 1 :])
        ):
            edge_ref[v, 0, k : k + 1, :] = value


def az_plane_kernel(nb_ref, il_ref, iu_ref, sc_ref, diff_ref, mix_ref, it_in_ref, edge_ref, order_ref, ot_ref, red_ref):
    count = nb_ref.shape[0]
    explicit = [diff_ref[w : w + 1, :] * nb_ref[w, 0] for w in range(count)]
    section_one = mixed(mix_ref, explicit)
    for v in range(count):
        il, iu = il_ref[v, 0], iu_ref[v, 0]
        target = section_one[v] * sc_ref[v, 0]
        length = il.shape[0]
        _, _, keep, _, _ = interior(il, iu)
        (it,) = pcr_levels(il, iu, [target * keep])
        it = it_in_ref[v, 0] + it
        ot_ref[v, 0] = it
        edge = edge_ref[v, 0]
        n2 = length - 2
        rows = interface_rows(
            edge[6:8], edge[8:10], edge[0:1] + target[0:1], edge[1:2] + target[length - 1 :], it[1:2], it[n2 : n2 + 1],
            edge[2:3], edge[3:4], edge[4:5], edge[5:6],
        )
        store_rows(red_ref, v, rows)


def rad_side(cell, visc, v):
    coupling = visc[v : v + 1, :] * cell
    scale = 1.0 / (1.0 + 2.0 * coupling)
    return -coupling * scale, scale


def local_visc(visc_ref, axis_name, cells):
    place = lax.axis_index(axis_name)
    return visc_ref[:, pl.ds(pl.multiple_of(place * cells, cells), cells)]


def rad_pre_kernel(cell_ref, visc_ref, oa_ref, ob_ref, edge_ref, *, axis_name):
    count = oa_ref.shape[0]
    cells = cell_ref.shape[2]
    visc = local_visc(visc_ref, axis_name, cells)
    cell = cell_ref[0]
    for v in range(count):
        side, _ = rad_side(cell, visc, v)
        side = side.T
        length = side.shape[0]
        il, iu, _, a_init, b_init = interior(side, side)
        ia, ib = pcr_levels(il, iu, [a_init, b_init])
        oa_ref[v, 0] = ia
        ob_ref[v, 0] = ib
        n2 = length - 2
        for k, value in enumerate((ia[1:2], ib[1:2], ia[n2 : n2 + 1], ib[n2 : n2 + 1])):
            edge_ref[v, 0, k : k + 1, :] = value


def rad_kernel(*refs, axis_name, devices, pieces):
    it_ref, ia_ref, ib_ref = refs[:3]
    red_in = refs[3 : 3 + pieces]
    mix_ref, cell_ref, visc_ref, edge_ref, ot_ref, red_ref, rows_ref = refs[3 + pieces :]
    count = it_ref.shape[0]
    cells = it_ref.shape[3]
    place = lax.axis_index(axis_name)
    visc = local_visc(visc_ref, axis_name, cells)
    solved = []
    for w in range(count):
        first, last = reduced_ends(red_in, rows_ref, w)
        solved.append(back_substitute(it_ref[w, 0], ia_ref[w, 0], ib_ref[w, 0], first, last))
    section_three = mixed(mix_ref, solved)
    cell = cell_ref[0]
    for v in range(count):
        side, scale = rad_side(cell, visc, v)
        side = side.T
        target = (section_three[v] * scale).T
        length = side.shape[0]
        il, iu, keep, _, _ = interior(side, side)
        (it,) = pcr_levels(il, iu, [target * keep])
        edge = edge_ref[v, 0]
        n2 = length - 2
        (lf, le), (uf, ue), trow = interface_rows(
            side, side, target[0:1], target[length - 1 :], it[1:2], it[n2 : n2 + 1],
            edge[0:1], edge[1:2], edge[2:3], edge[3:4],
        )
        lf = jnp.where(place == 0, jnp.zeros_like(lf), lf)
        ue = jnp.where(place == devices - 1, jnp.zeros_like(ue), ue)
        store_rows(red_ref, v, ((lf, le), (uf, ue), trow))
        ot_ref[v, 0] = it


def out_kernel(*refs, pieces, length):
    it_ref, ia_ref, ib_ref = refs[:3]
    red_in = refs[3 : 3 + pieces]
    mix_ref, out_ref, rows_ref = refs[3 + pieces :]
    count = it_ref.shape[0]
    offset = pl.program_id(1) * it_ref.shape[2]
    solved = []
    for w in range(count):
        first, last = reduced_ends(red_in, rows_ref, w)
        solved.append(back_substitute(it_ref[w, 0], ia_ref[w, 0], ib_ref[w, 0], first, last, offset, length).T)
    for v, value in enumerate(mixed(mix_ref, solved)):
        out_ref[v, 0] = value


def az_sweep(flow_state, nb, source, cell_az, visc_az, beta_az, axial_diff, mix_in, order):
    nv, nz, na, nr = flow_state.shape
    chunk = 128 if nr % 128 == 0 else nr
    grid = (nz, nr // chunk)
    big = pl.BlockSpec((nv, 1, na, chunk), lambda z, c: (0, z, 0, c))
    cell = pl.BlockSpec((1, na, chunk), lambda z, c: (z, 0, c))
    par = pl.BlockSpec((nv, chunk), lambda z, c: (0, c))
    mixs = pl.BlockSpec((nv, nv, chunk), lambda z, c: (0, 0, c))
    edge = pl.BlockSpec((nv, 1, 10, chunk), lambda z, c: (0, z, 0, c))
    red = pl.BlockSpec((nv, 1, 3, 2, chunk), lambda z, c: (0, z, 0, 0, c))
    out = jax.ShapeDtypeStruct(flow_state.shape, flow_state.dtype)
    it, ia, ib, il, iu, scale, edges = pl.pallas_call(
        az_local_kernel,
        grid=grid,
        in_specs=[big, big, cell, par, par, par, mixs],
        out_specs=[big] * 6 + [edge],
        out_shape=[out] * 6 + [jax.ShapeDtypeStruct((nv, nz, 10, nr), flow_state.dtype)],
    )(flow_state, source, cell_az, visc_az, beta_az, axial_diff, mix_in)
    it, red = pl.pallas_call(
        az_plane_kernel,
        grid=grid,
        in_specs=[big, big, big, big, par, mixs, big, edge, pl.BlockSpec(memory_space=pl.ANY)],
        out_specs=[big, red],
        out_shape=[out, jax.ShapeDtypeStruct((nv, nz, 3, 2, nr), flow_state.dtype)],
        input_output_aliases={6: 0},
    )(nb, il, iu, scale, axial_diff, mix_in, it, edges, order)
    return it, ia, ib, red


def rad_pre(cell_rad, visc_rad, nv):
    nz, na, nr = cell_rad.shape
    big_t = pl.BlockSpec((nv, 1, nr, na), lambda z: (0, z, 0, 0))
    cell = pl.BlockSpec((1, na, nr), lambda z: (z, 0, 0))
    par = pl.BlockSpec(visc_rad.shape, lambda z: (0, 0))
    edge = pl.BlockSpec((nv, 1, 4, na), lambda z: (0, z, 0, 0))
    out = jax.ShapeDtypeStruct((nv, nz, nr, na), cell_rad.dtype)
    return pl.pallas_call(
        functools.partial(rad_pre_kernel, axis_name="rad"),
        grid=(nz,),
        in_specs=[cell, par],
        out_specs=[big_t, big_t, edge],
        out_shape=[out, out, jax.ShapeDtypeStruct((nv, nz, 4, na), cell_rad.dtype)],
    )(cell_rad, visc_rad)


def rad_sweep(it, ia, ib, red_in, mix_mid, cell_rad, visc_rad, edges):
    nv, nz, na, nr = it.shape
    big = pl.BlockSpec((nv, 1, na, nr), lambda z: (0, z, 0, 0))
    big_t = pl.BlockSpec((nv, 1, nr, na), lambda z: (0, z, 0, 0))
    red_in_spec = pl.BlockSpec((nv, 1) + red_in[0].shape[2:], lambda z: (0, z, 0, 0, 0))
    mixs = pl.BlockSpec((nv, nv, nr), lambda z: (0, 0, 0))
    cell = pl.BlockSpec((1, na, nr), lambda z: (z, 0, 0))
    par = pl.BlockSpec(visc_rad.shape, lambda z: (0, 0))
    edge = pl.BlockSpec((nv, 1, 4, na), lambda z: (0, z, 0, 0))
    red = pl.BlockSpec((nv, 1, 3, 2, na), lambda z: (0, z, 0, 0, 0))
    out = jax.ShapeDtypeStruct((nv, nz, nr, na), it.dtype)
    pieces = len(red_in)
    kernel = functools.partial(rad_kernel, axis_name="rad", devices=lax.axis_size("rad"), pieces=pieces)
    return pl.pallas_call(
        kernel,
        grid=(nz,),
        in_specs=[big, big, big] + [red_in_spec] * pieces + [mixs, cell, par, edge],
        out_specs=[big_t, red],
        out_shape=[out, jax.ShapeDtypeStruct((nv, nz, 3, 2, na), it.dtype)],
        scratch_shapes=[pltpu.VMEM((3, 2 * pieces, nr), it.dtype)],
    )(it, ia, ib, *red_in, mix_mid, cell_rad, visc_rad, edges)


def out_sweep(it, ia, ib, red_in, mix_out):
    nv, nz, nr, na = it.shape
    chunk = 128 if nr % 128 == 0 else nr
    big_t = pl.BlockSpec((nv, 1, chunk, na), lambda z, c: (0, z, c, 0))
    big = pl.BlockSpec((nv, 1, na, chunk), lambda z, c: (0, z, 0, c))
    red_in_spec = pl.BlockSpec((nv, 1) + red_in[0].shape[2:], lambda z, c: (0, z, 0, 0, 0))
    mixs = pl.BlockSpec((nv, nv, chunk), lambda z, c: (0, 0, c))
    pieces = len(red_in)
    return pl.pallas_call(
        functools.partial(out_kernel, pieces=pieces, length=nr),
        grid=(nz, nr // chunk),
        in_specs=[big_t, big_t, big_t] + [red_in_spec] * pieces + [mixs],
        out_specs=big,
        out_shape=jax.ShapeDtypeStruct((nv, nz, na, nr), it.dtype),
        scratch_shapes=[pltpu.VMEM((3, 2 * pieces, na), it.dtype)],
    )(it, ia, ib, *red_in, mix_out)


def gathered(block, axis_name):
    count = lax.axis_size(axis_name)
    received = [block]
    for offset in range(1, count):
        pairs = [((i + offset) % count, i) for i in range(count)]
        received.append(lax.ppermute(block, axis_name, pairs))
    return received


def neighbour_planes(block, axis_name):
    count = lax.axis_size(axis_name)
    if count == 2:
        return lax.ppermute(block, axis_name, [(0, 1), (1, 0)])
    padded = with_halo(block, ((axis_name, 1),), 1, False)
    return padded[:, :-2] + padded[:, 2:]


def mix(matrix, values):
    mixed_rows = []
    for out_var in range(values.shape[0]):
        summed = values[out_var]
        for in_var in range(values.shape[0]):
            summed = summed + matrix[out_var, in_var][None, None, :] * values[in_var]
        mixed_rows.append(summed)
    return jnp.stack(mixed_rows)


def per_device(
    flow_state,
    source,
    cell_az,
    cell_rad,
    visc_az,
    beta_az,
    visc_rad,
    axial_diff,
    mix_in,
    mix_mid,
    mix_out,
):
    rad_cells = flow_state.shape[3]
    nb = neighbour_planes(flow_state, "ax")
    rad_a, rad_b, rad_edges = rad_pre(cell_rad, visc_rad, flow_state.shape[0])
    it, ia, ib, red = az_sweep(flow_state, nb, source, cell_az, visc_az, beta_az, axial_diff, mix_in, rad_edges)
    red = gathered(red, "az")
    it, red = rad_sweep(it, ia, ib, red, mix_mid, cell_rad, visc_rad, rad_edges)
    ia, ib = rad_a, rad_b
    red = gathered(red, "rad")
    return out_sweep(it, ia, ib, red, mix_out)


def solution(mesh):
    in_specs = (
        P(None, "ax", "az", "rad"),
        P(None, "ax", "az", "rad"),
        P("ax", "az", "rad"),
        P("ax", "az", "rad"),
        P(None, "rad"),
        P(None, "rad"),
        P(),
        P(None, "rad"),
        P(None, None, "rad"),
        P(None, None, "rad"),
        P(None, None, "rad"),
    )
    out_specs = P(None, "ax", "az", "rad")
    return jax.shard_map(
        per_device, mesh=mesh, in_specs=in_specs, out_specs=out_specs, check_vma=False
    )
```

```python
import jax
import jax.numpy as jnp
from jax import lax
from jax.experimental import pallas as pl
from jax.experimental.pallas import tpu as pltpu
from jax.sharding import PartitionSpec as P
import functools


def with_halo(block, sides, width, periodic):
    for axis, dim in sides:
        count = lax.axis_size(axis)
        forward = [(i, i + 1) for i in range(count - 1)]
        if periodic:
            forward.append((count - 1, 0))
        backward = [(target, source) for source, target in forward]
        low = lax.ppermute(
            lax.slice_in_dim(block, block.shape[dim] - width, None, axis=dim), axis, forward
        )
        high = lax.ppermute(lax.slice_in_dim(block, 0, width, axis=dim), axis, backward)
        block = jnp.concatenate([low, block, high], axis=dim)
    return block


def shifted(values, offset, axis, periodic):
    if periodic:
        return jnp.roll(values, offset, axis)
    length = values.shape[axis]
    zero_shape = list(values.shape)
    zero_shape[axis] = abs(offset)
    zeros = jnp.zeros(zero_shape, values.dtype)
    if offset > 0:
        kept = lax.slice_in_dim(values, 0, length - offset, axis=axis)
        return jnp.concatenate([zeros, kept], axis=axis)
    kept = lax.slice_in_dim(values, -offset, length, axis=axis)
    return jnp.concatenate([kept, zeros], axis=axis)


def cyclic_reduce(lower, upper, rhs, axis, periodic, steps_below):
    stride = 1
    while stride < steps_below:
        ll, ul = shifted(lower, stride, axis, periodic), shifted(upper, stride, axis, periodic)
        lr, ur = shifted(lower, -stride, axis, periodic), shifted(upper, -stride, axis, periodic)
        inv = 1.0 / (1.0 - lower * ul - upper * lr)
        rhs = [
            (r - lower * shifted(r, stride, axis, periodic) - upper * shifted(r, -stride, axis, periodic)) * inv
            for r in rhs
        ]
        lower, upper = -lower * ll * inv, -upper * ur * inv
        stride = stride * 2
    return lower, upper, rhs


def interior(lower, upper):
    length = lower.shape[0]
    idx = lax.broadcasted_iota(jnp.int32, lower.shape, 0)
    edge = (idx == 0) | (idx == length - 1)
    second = idx == 1
    penult = idx == length - 2
    zero = jnp.zeros_like(lower)
    il = jnp.where(edge | second, zero, lower)
    iu = jnp.where(edge | penult, zero, upper)
    return il, iu, jnp.where(edge, zero, 1.0), jnp.where(second, lower, zero), jnp.where(penult, upper, zero)


def pcr_levels(il, iu, rhs):
    length = il.shape[0]
    stride = 1
    while stride < length - 2:
        back = length - stride
        ll, ul = pltpu.roll(il, stride, 0), pltpu.roll(iu, stride, 0)
        lr, ur = pltpu.roll(il, back, 0), pltpu.roll(iu, back, 0)
        inv = 1.0 / (1.0 - il * ul - iu * lr)
        rhs = [(r - il * pltpu.roll(r, stride, 0) - iu * pltpu.roll(r, back, 0)) * inv for r in rhs]
        flip = -inv
        il, iu = il * ll * flip, iu * ur * flip
        stride = stride * 2
    return rhs


def interface_rows(lower, upper, t0, te, t1, t2, a1, b1, a2, b2):
    length = lower.shape[0]
    l0, u0 = lower[0:1], upper[0:1]
    le, ue = lower[length - 1 :], upper[length - 1 :]
    inv_f = 1.0 / (1.0 - u0 * a1)
    inv_e = 1.0 / (1.0 - le * b2)
    return (
        (l0 * inv_f, -le * a2 * inv_e),
        (-u0 * b1 * inv_f, ue * inv_e),
        ((t0 - u0 * t1) * inv_f, (te - le * t2) * inv_e),
    )


def reduce_block(lower, upper, target):
    length = lower.shape[0]
    il, iu, keep, a_init, b_init = interior(lower, upper)
    it, ia, ib = pcr_levels(il, iu, [target * keep, a_init, b_init])
    n2 = length - 2
    rows = interface_rows(
        lower, upper, target[0:1], target[length - 1 :], it[1:2], it[n2 : n2 + 1],
        ia[1:2], ib[1:2], ia[n2 : n2 + 1], ib[n2 : n2 + 1],
    )
    return it, ia, ib, rows


def store_rows(red_ref, v, rows):
    for q, pair in enumerate(rows):
        for i, value in enumerate(pair):
            red_ref[v, 0, q, i : i + 1, :] = value


def reduced_ends(red_refs, rows_ref, v):
    for k, ref in enumerate(red_refs):
        rows_ref[:, 2 * k : 2 * k + 2, :] = ref[v, 0]
    lower, upper, target = rows_ref[0], rows_ref[1], rows_ref[2]
    length = lower.shape[0]
    stride = 1
    while stride < length:
        back = length - stride
        ll, ul = pltpu.roll(lower, stride, 0), pltpu.roll(upper, stride, 0)
        lr, ur = pltpu.roll(lower, back, 0), pltpu.roll(upper, back, 0)
        inv = 1.0 / (1.0 - lower * ul - upper * lr)
        target = (target - lower * pltpu.roll(target, stride, 0) - upper * pltpu.roll(target, back, 0)) * inv
        lower, upper = -lower * ll * inv, -upper * ur * inv
        stride = stride * 2
    ends = target / (1.0 + lower + upper)
    return ends[0:1], ends[1:2]


def back_substitute(it, ia, ib, first, last, offset=0, length=None):
    length = it.shape[0] if length is None else length
    idx = lax.broadcasted_iota(jnp.int32, it.shape, 0) + offset
    inner = it - ia * first - ib * last
    return jnp.where(idx == 0, first, jnp.where(idx == length - 1, last, inner))


def mixed(mix_ref, values):
    out = []
    for v in range(len(values)):
        summed = values[v]
        for w in range(len(values)):
            summed = summed + mix_ref[v, w : w + 1, :] * values[w]
        out.append(summed)
    return out


def az_coefficients(cell, visc_ref, beta_ref, v):
    coupling = visc_ref[v : v + 1, :] * cell
    scale = -1.0 / (1.0 + 2.0 * coupling)
    tilt = beta_ref[v : v + 1, :]
    lower = coupling * (1.0 + tilt) * scale
    upper = coupling * (1.0 - tilt) * scale
    return lower, upper, scale


def az_local_kernel(fs_ref, src_ref, cell_ref, visc_ref, beta_ref, diff_ref, mix_ref, ot_ref, oa_ref, ob_ref, ol_ref, ou_ref, os_ref, edge_ref):
    count = fs_ref.shape[0]
    explicit = [src_ref[w, 0] + diff_ref[w : w + 1, :] * (-2.0 * fs_ref[w, 0]) for w in range(count)]
    section_one = mixed(mix_ref, explicit)
    cell = cell_ref[0]
    for v in range(count):
        lower, upper, scale = az_coefficients(cell, visc_ref, beta_ref, v)
        target = section_one[v] * -scale
        length = lower.shape[0]
        il, iu, keep, a_init, b_init = interior(lower, upper)
        ol_ref[v, 0] = il
        ou_ref[v, 0] = iu
        os_ref[v, 0] = -scale
        it, ia, ib = pcr_levels(il, iu, [target * keep, a_init, b_init])
        ot_ref[v, 0] = it
        oa_ref[v, 0] = ia
        ob_ref[v, 0] = ib
        n2 = length - 2
        for k, value in enumerate(
            (target[0:1], target[length - 1 :], ia[1:2], ib[1:2], ia[n2 : n2 + 1], ib[n2 : n2 + 1],
             lower[0:1], lower[length - 1 :], upper[0:1], upper[length - 1 :])
        ):
            edge_ref[v, 0, k : k + 1, :] = value


def az_plane_kernel(nb_ref, il_ref, iu_ref, sc_ref, diff_ref, mix_ref, it_in_ref, edge_ref, order_ref, ot_ref, red_ref):
    count = nb_ref.shape[0]
    explicit = [diff_ref[w : w + 1, :] * nb_ref[w, 0] for w in range(count)]
    section_one = mixed(mix_ref, explicit)
    for v in range(count):
        il, iu = il_ref[v, 0], iu_ref[v, 0]
        target = section_one[v] * sc_ref[v, 0]
        length = il.shape[0]
        _, _, keep, _, _ = interior(il, iu)
        (it,) = pcr_levels(il, iu, [target * keep])
        it = it_in_ref[v, 0] + it
        ot_ref[v, 0] = it
        edge = edge_ref[v, 0]
        n2 = length - 2
        rows = interface_rows(
            edge[6:8], edge[8:10], edge[0:1] + target[0:1], edge[1:2] + target[length - 1 :], it[1:2], it[n2 : n2 + 1],
            edge[2:3], edge[3:4], edge[4:5], edge[5:6],
        )
        store_rows(red_ref, v, rows)


def rad_side(cell, visc, v):
    coupling = visc[v : v + 1, :] * cell
    scale = 1.0 / (1.0 + 2.0 * coupling)
    return -coupling * scale, scale


def local_visc(visc_ref, axis_name, cells):
    place = lax.axis_index(axis_name)
    return visc_ref[:, pl.ds(pl.multiple_of(place * cells, cells), cells)]


def rad_pre_kernel(cell_ref, visc_ref, oa_ref, ob_ref, edge_ref, *, axis_name):
    count = oa_ref.shape[0]
    cells = cell_ref.shape[2]
    visc = local_visc(visc_ref, axis_name, cells)
    cell = cell_ref[0]
    for v in range(count):
        side, _ = rad_side(cell, visc, v)
        side = side.T
        length = side.shape[0]
        il, iu, _, a_init, b_init = interior(side, side)
        ia, ib = pcr_levels(il, iu, [a_init, b_init])
        oa_ref[v, 0] = ia
        ob_ref[v, 0] = ib
        n2 = length - 2
        for k, value in enumerate((ia[1:2], ib[1:2], ia[n2 : n2 + 1], ib[n2 : n2 + 1])):
            edge_ref[v, 0, k : k + 1, :] = value


def rad_kernel(*refs, axis_name, devices, pieces):
    it_ref, ia_ref, ib_ref = refs[:3]
    red_in = refs[3 : 3 + pieces]
    mix_ref, cell_ref, visc_ref, edge_ref, ot_ref, red_ref, rows_ref, s3_ref = refs[3 + pieces :]
    count = it_ref.shape[0]
    half = it_ref.shape[2]
    step = pl.program_id(1)
    solved = []
    for w in range(count):
        first, last = reduced_ends(red_in, rows_ref, w)
        solved.append(
            back_substitute(it_ref[w, 0], ia_ref[w, 0], ib_ref[w, 0], first, last, step * half, s3_ref.shape[1])
        )
    for v, value in enumerate(mixed(mix_ref, solved)):
        s3_ref[v, pl.ds(pl.multiple_of(step * half, half), half), :] = value

    @pl.when(step == pl.num_programs(1) - 1)
    def _():
        rad_finish(s3_ref, cell_ref, visc_ref, edge_ref, ot_ref, red_ref, axis_name, devices)


def rad_finish(s3_ref, cell_ref, visc_ref, edge_ref, ot_ref, red_ref, axis_name, devices):
    count = s3_ref.shape[0]
    cells = s3_ref.shape[2]
    place = lax.axis_index(axis_name)
    visc = local_visc(visc_ref, axis_name, cells)
    section_three = [s3_ref[v] for v in range(count)]
    cell = cell_ref[0]
    for v in range(count):
        side, scale = rad_side(cell, visc, v)
        side = side.T
        target = (section_three[v] * scale).T
        length = side.shape[0]
        il, iu, keep, _, _ = interior(side, side)
        (it,) = pcr_levels(il, iu, [target * keep])
        edge = edge_ref[v, 0]
        n2 = length - 2
        (lf, le), (uf, ue), trow = interface_rows(
            side, side, target[0:1], target[length - 1 :], it[1:2], it[n2 : n2 + 1],
            edge[0:1], edge[1:2], edge[2:3], edge[3:4],
        )
        lf = jnp.where(place == 0, jnp.zeros_like(lf), lf)
        ue = jnp.where(place == devices - 1, jnp.zeros_like(ue), ue)
        store_rows(red_ref, v, ((lf, le), (uf, ue), trow))
        ot_ref[v, 0] = it


def out_kernel(*refs, pieces, length):
    it_ref, ia_ref, ib_ref = refs[:3]
    red_in = refs[3 : 3 + pieces]
    mix_ref, out_ref, rows_ref = refs[3 + pieces :]
    count = it_ref.shape[0]
    offset = pl.program_id(1) * it_ref.shape[2]
    solved = []
    for w in range(count):
        first, last = reduced_ends(red_in, rows_ref, w)
        solved.append(back_substitute(it_ref[w, 0], ia_ref[w, 0], ib_ref[w, 0], first, last, offset, length).T)
    for v, value in enumerate(mixed(mix_ref, solved)):
        out_ref[v, 0] = value


def az_sweep(flow_state, nb, source, cell_az, visc_az, beta_az, axial_diff, mix_in, order):
    nv, nz, na, nr = flow_state.shape
    chunk = 128 if nr % 128 == 0 else nr
    grid = (nz, nr // chunk)
    big = pl.BlockSpec((nv, 1, na, chunk), lambda z, c: (0, z, 0, c))
    cell = pl.BlockSpec((1, na, chunk), lambda z, c: (z, 0, c))
    par = pl.BlockSpec((nv, chunk), lambda z, c: (0, c))
    mixs = pl.BlockSpec((nv, nv, chunk), lambda z, c: (0, 0, c))
    edge = pl.BlockSpec((nv, 1, 10, chunk), lambda z, c: (0, z, 0, c))
    red = pl.BlockSpec((nv, 1, 3, 2, chunk), lambda z, c: (0, z, 0, 0, c))
    out = jax.ShapeDtypeStruct(flow_state.shape, flow_state.dtype)
    it, ia, ib, il, iu, scale, edges = pl.pallas_call(
        az_local_kernel,
        grid=grid,
        in_specs=[big, big, cell, par, par, par, mixs],
        out_specs=[big] * 6 + [edge],
        out_shape=[out] * 6 + [jax.ShapeDtypeStruct((nv, nz, 10, nr), flow_state.dtype)],
    )(flow_state, source, cell_az, visc_az, beta_az, axial_diff, mix_in)
    it, red = pl.pallas_call(
        az_plane_kernel,
        grid=grid,
        in_specs=[big, big, big, big, par, mixs, big, edge, pl.BlockSpec(memory_space=pl.ANY)],
        out_specs=[big, red],
        out_shape=[out, jax.ShapeDtypeStruct((nv, nz, 3, 2, nr), flow_state.dtype)],
        input_output_aliases={6: 0},
    )(nb, il, iu, scale, axial_diff, mix_in, it, edges, order)
    return it, ia, ib, red


def rad_pre(cell_rad, visc_rad, nv):
    nz, na, nr = cell_rad.shape
    big_t = pl.BlockSpec((nv, 1, nr, na), lambda z: (0, z, 0, 0))
    cell = pl.BlockSpec((1, na, nr), lambda z: (z, 0, 0))
    par = pl.BlockSpec(visc_rad.shape, lambda z: (0, 0))
    edge = pl.BlockSpec((nv, 1, 4, na), lambda z: (0, z, 0, 0))
    out = jax.ShapeDtypeStruct((nv, nz, nr, na), cell_rad.dtype)
    return pl.pallas_call(
        functools.partial(rad_pre_kernel, axis_name="rad"),
        grid=(nz,),
        in_specs=[cell, par],
        out_specs=[big_t, big_t, edge],
        out_shape=[out, out, jax.ShapeDtypeStruct((nv, nz, 4, na), cell_rad.dtype)],
    )(cell_rad, visc_rad)


def rad_sweep(it, ia, ib, red_in, mix_mid, cell_rad, visc_rad, edges):
    nv, nz, na, nr = it.shape
    halves = 2 if na % 16 == 0 else 1
    big = pl.BlockSpec((nv, 1, na // halves, nr), lambda z, c: (0, z, c, 0))
    big_t = pl.BlockSpec((nv, 1, nr, na), lambda z, c: (0, z, 0, 0))
    red_in_spec = pl.BlockSpec((nv, 1) + red_in[0].shape[2:], lambda z, c: (0, z, 0, 0, 0))
    mixs = pl.BlockSpec((nv, nv, nr), lambda z, c: (0, 0, 0))
    cell = pl.BlockSpec((1, na, nr), lambda z, c: (z, 0, 0))
    par = pl.BlockSpec(visc_rad.shape, lambda z, c: (0, 0))
    edge = pl.BlockSpec((nv, 1, 4, na), lambda z, c: (0, z, 0, 0))
    red = pl.BlockSpec((nv, 1, 3, 2, na), lambda z, c: (0, z, 0, 0, 0))
    out = jax.ShapeDtypeStruct((nv, nz, nr, na), it.dtype)
    pieces = len(red_in)
    kernel = functools.partial(rad_kernel, axis_name="rad", devices=lax.axis_size("rad"), pieces=pieces)
    return pl.pallas_call(
        kernel,
        grid=(nz, halves),
        in_specs=[big, big, big] + [red_in_spec] * pieces + [mixs, cell, par, edge],
        out_specs=[big_t, red],
        out_shape=[out, jax.ShapeDtypeStruct((nv, nz, 3, 2, na), it.dtype)],
        scratch_shapes=[pltpu.VMEM((3, 2 * pieces, nr), it.dtype), pltpu.VMEM((nv, na, nr), it.dtype)],
    )(it, ia, ib, *red_in, mix_mid, cell_rad, visc_rad, edges)


def out_sweep(it, ia, ib, red_in, mix_out):
    nv, nz, nr, na = it.shape
    chunk = 128 if nr % 128 == 0 else nr
    big_t = pl.BlockSpec((nv, 1, chunk, na), lambda z, c: (0, z, c, 0))
    big = pl.BlockSpec((nv, 1, na, chunk), lambda z, c: (0, z, 0, c))
    red_in_spec = pl.BlockSpec((nv, 1) + red_in[0].shape[2:], lambda z, c: (0, z, 0, 0, 0))
    mixs = pl.BlockSpec((nv, nv, chunk), lambda z, c: (0, 0, c))
    pieces = len(red_in)
    return pl.pallas_call(
        functools.partial(out_kernel, pieces=pieces, length=nr),
        grid=(nz, nr // chunk),
        in_specs=[big_t, big_t, big_t] + [red_in_spec] * pieces + [mixs],
        out_specs=big,
        out_shape=jax.ShapeDtypeStruct((nv, nz, na, nr), it.dtype),
        scratch_shapes=[pltpu.VMEM((3, 2 * pieces, na), it.dtype)],
    )(it, ia, ib, *red_in, mix_out)


def gathered(block, axis_name):
    count = lax.axis_size(axis_name)
    received = [block]
    for offset in range(1, count):
        pairs = [((i + offset) % count, i) for i in range(count)]
        received.append(lax.ppermute(block, axis_name, pairs))
    return received


def neighbour_planes(block, axis_name):
    count = lax.axis_size(axis_name)
    if count == 2:
        return lax.ppermute(block, axis_name, [(0, 1), (1, 0)])
    padded = with_halo(block, ((axis_name, 1),), 1, False)
    return padded[:, :-2] + padded[:, 2:]


def mix(matrix, values):
    mixed_rows = []
    for out_var in range(values.shape[0]):
        summed = values[out_var]
        for in_var in range(values.shape[0]):
            summed = summed + matrix[out_var, in_var][None, None, :] * values[in_var]
        mixed_rows.append(summed)
    return jnp.stack(mixed_rows)


def per_device(
    flow_state,
    source,
    cell_az,
    cell_rad,
    visc_az,
    beta_az,
    visc_rad,
    axial_diff,
    mix_in,
    mix_mid,
    mix_out,
):
    rad_cells = flow_state.shape[3]
    nb = neighbour_planes(flow_state, "ax")
    rad_a, rad_b, rad_edges = rad_pre(cell_rad, visc_rad, flow_state.shape[0])
    it, ia, ib, red = az_sweep(flow_state, nb, source, cell_az, visc_az, beta_az, axial_diff, mix_in, rad_edges)
    red = gathered(red, "az")
    it, red = rad_sweep(it, ia, ib, red, mix_mid, cell_rad, visc_rad, rad_edges)
    ia, ib = rad_a, rad_b
    red = gathered(red, "rad")
    return out_sweep(it, ia, ib, red, mix_out)


def solution(mesh):
    in_specs = (
        P(None, "ax", "az", "rad"),
        P(None, "ax", "az", "rad"),
        P("ax", "az", "rad"),
        P("ax", "az", "rad"),
        P(None, "rad"),
        P(None, "rad"),
        P(),
        P(None, "rad"),
        P(None, None, "rad"),
        P(None, None, "rad"),
        P(None, None, "rad"),
    )
    out_specs = P(None, "ax", "az", "rad")
    return jax.shard_map(
        per_device, mesh=mesh, in_specs=in_specs, out_specs=out_specs, check_vma=False
    )
```

```python
import jax
import jax.numpy as jnp
from jax import lax
from jax.experimental import pallas as pl
from jax.experimental.pallas import tpu as pltpu
from jax.sharding import PartitionSpec as P
import functools


def with_halo(block, sides, width, periodic):
    for axis, dim in sides:
        count = lax.axis_size(axis)
        forward = [(i, i + 1) for i in range(count - 1)]
        if periodic:
            forward.append((count - 1, 0))
        backward = [(target, source) for source, target in forward]
        low = lax.ppermute(
            lax.slice_in_dim(block, block.shape[dim] - width, None, axis=dim), axis, forward
        )
        high = lax.ppermute(lax.slice_in_dim(block, 0, width, axis=dim), axis, backward)
        block = jnp.concatenate([low, block, high], axis=dim)
    return block


def shifted(values, offset, axis, periodic):
    if periodic:
        return jnp.roll(values, offset, axis)
    length = values.shape[axis]
    zero_shape = list(values.shape)
    zero_shape[axis] = abs(offset)
    zeros = jnp.zeros(zero_shape, values.dtype)
    if offset > 0:
        kept = lax.slice_in_dim(values, 0, length - offset, axis=axis)
        return jnp.concatenate([zeros, kept], axis=axis)
    kept = lax.slice_in_dim(values, -offset, length, axis=axis)
    return jnp.concatenate([kept, zeros], axis=axis)


def cyclic_reduce(lower, upper, rhs, axis, periodic, steps_below):
    stride = 1
    while stride < steps_below:
        ll, ul = shifted(lower, stride, axis, periodic), shifted(upper, stride, axis, periodic)
        lr, ur = shifted(lower, -stride, axis, periodic), shifted(upper, -stride, axis, periodic)
        inv = 1.0 / (1.0 - lower * ul - upper * lr)
        rhs = [
            (r - lower * shifted(r, stride, axis, periodic) - upper * shifted(r, -stride, axis, periodic)) * inv
            for r in rhs
        ]
        lower, upper = -lower * ll * inv, -upper * ur * inv
        stride = stride * 2
    return lower, upper, rhs


def interior(lower, upper):
    length = lower.shape[0]
    idx = lax.broadcasted_iota(jnp.int32, lower.shape, 0)
    edge = (idx == 0) | (idx == length - 1)
    second = idx == 1
    penult = idx == length - 2
    zero = jnp.zeros_like(lower)
    il = jnp.where(edge | second, zero, lower)
    iu = jnp.where(edge | penult, zero, upper)
    return il, iu, jnp.where(edge, zero, 1.0), jnp.where(second, lower, zero), jnp.where(penult, upper, zero)


def pcr_levels(il, iu, rhs):
    length = il.shape[0]
    stride = 1
    while stride < length - 2:
        back = length - stride
        ll, ul = pltpu.roll(il, stride, 0), pltpu.roll(iu, stride, 0)
        lr, ur = pltpu.roll(il, back, 0), pltpu.roll(iu, back, 0)
        inv = 1.0 / (1.0 - il * ul - iu * lr)
        rhs = [(r - il * pltpu.roll(r, stride, 0) - iu * pltpu.roll(r, back, 0)) * inv for r in rhs]
        flip = -inv
        il, iu = il * ll * flip, iu * ur * flip
        stride = stride * 2
    return rhs


def interface_rows(lower, upper, t0, te, t1, t2, a1, b1, a2, b2):
    length = lower.shape[0]
    l0, u0 = lower[0:1], upper[0:1]
    le, ue = lower[length - 1 :], upper[length - 1 :]
    inv_f = 1.0 / (1.0 - u0 * a1)
    inv_e = 1.0 / (1.0 - le * b2)
    return (
        (l0 * inv_f, -le * a2 * inv_e),
        (-u0 * b1 * inv_f, ue * inv_e),
        ((t0 - u0 * t1) * inv_f, (te - le * t2) * inv_e),
    )


def reduce_block(lower, upper, target):
    length = lower.shape[0]
    il, iu, keep, a_init, b_init = interior(lower, upper)
    it, ia, ib = pcr_levels(il, iu, [target * keep, a_init, b_init])
    n2 = length - 2
    rows = interface_rows(
        lower, upper, target[0:1], target[length - 1 :], it[1:2], it[n2 : n2 + 1],
        ia[1:2], ib[1:2], ia[n2 : n2 + 1], ib[n2 : n2 + 1],
    )
    return it, ia, ib, rows


def store_rows(red_ref, v, rows):
    for q, pair in enumerate(rows):
        for i, value in enumerate(pair):
            red_ref[v, 0, q, i : i + 1, :] = value


def reduced_ends(red_refs, rows_ref, v):
    for k, ref in enumerate(red_refs):
        rows_ref[:, 2 * k : 2 * k + 2, :] = ref[v, 0]
    lower, upper, target = rows_ref[0], rows_ref[1], rows_ref[2]
    length = lower.shape[0]
    stride = 1
    while stride < length:
        back = length - stride
        ll, ul = pltpu.roll(lower, stride, 0), pltpu.roll(upper, stride, 0)
        lr, ur = pltpu.roll(lower, back, 0), pltpu.roll(upper, back, 0)
        inv = 1.0 / (1.0 - lower * ul - upper * lr)
        target = (target - lower * pltpu.roll(target, stride, 0) - upper * pltpu.roll(target, back, 0)) * inv
        lower, upper = -lower * ll * inv, -upper * ur * inv
        stride = stride * 2
    ends = target / (1.0 + lower + upper)
    return ends[0:1], ends[1:2]


def back_substitute(it, ia, ib, first, last, offset=0, length=None):
    length = it.shape[0] if length is None else length
    idx = lax.broadcasted_iota(jnp.int32, it.shape, 0) + offset
    inner = it - ia * first - ib * last
    return jnp.where(idx == 0, first, jnp.where(idx == length - 1, last, inner))


def mixed(mix_ref, values):
    out = []
    for v in range(len(values)):
        summed = values[v]
        for w in range(len(values)):
            summed = summed + mix_ref[v, w : w + 1, :] * values[w]
        out.append(summed)
    return out


def az_coefficients(cell, visc_ref, beta_ref, v):
    coupling = visc_ref[v : v + 1, :] * cell
    scale = -1.0 / (1.0 + 2.0 * coupling)
    tilt = beta_ref[v : v + 1, :]
    lower = coupling * (1.0 + tilt) * scale
    upper = coupling * (1.0 - tilt) * scale
    return lower, upper, scale


def az_local_kernel(fs_ref, src_ref, cell_ref, visc_ref, beta_ref, diff_ref, mix_ref, ot_ref, oa_ref, ob_ref, ol_ref, ou_ref, os_ref, edge_ref):
    count = fs_ref.shape[0]
    explicit = [src_ref[w, 0] + diff_ref[w : w + 1, :] * (-2.0 * fs_ref[w, 0]) for w in range(count)]
    section_one = mixed(mix_ref, explicit)
    cell = cell_ref[0]
    for v in range(count):
        lower, upper, scale = az_coefficients(cell, visc_ref, beta_ref, v)
        target = section_one[v] * -scale
        length = lower.shape[0]
        il, iu, keep, a_init, b_init = interior(lower, upper)
        ol_ref[v, 0] = il
        ou_ref[v, 0] = iu
        os_ref[v, 0] = -scale
        it, ia, ib = pcr_levels(il, iu, [target * keep, a_init, b_init])
        ot_ref[v, 0] = it
        oa_ref[v, 0] = ia
        ob_ref[v, 0] = ib
        n2 = length - 2
        for k, value in enumerate(
            (target[0:1], target[length - 1 :], ia[1:2], ib[1:2], ia[n2 : n2 + 1], ib[n2 : n2 + 1],
             lower[0:1], lower[length - 1 :], upper[0:1], upper[length - 1 :])
        ):
            edge_ref[v, 0, k : k + 1, :] = value


def az_plane_kernel(nb_ref, il_ref, iu_ref, sc_ref, diff_ref, mix_ref, it_in_ref, edge_ref, order_ref, ot_ref, red_ref):
    count = nb_ref.shape[0]
    explicit = [diff_ref[w : w + 1, :] * nb_ref[w, 0] for w in range(count)]
    section_one = mixed(mix_ref, explicit)
    for v in range(count):
        il, iu = il_ref[v, 0], iu_ref[v, 0]
        target = section_one[v] * sc_ref[v, 0]
        length = il.shape[0]
        _, _, keep, _, _ = interior(il, iu)
        (it,) = pcr_levels(il, iu, [target * keep])
        it = it_in_ref[v, 0] + it
        ot_ref[v, 0] = it
        edge = edge_ref[v, 0]
        n2 = length - 2
        rows = interface_rows(
            edge[6:8], edge[8:10], edge[0:1] + target[0:1], edge[1:2] + target[length - 1 :], it[1:2], it[n2 : n2 + 1],
            edge[2:3], edge[3:4], edge[4:5], edge[5:6],
        )
        store_rows(red_ref, v, rows)


def rad_side(cell, visc, v):
    coupling = visc[v : v + 1, :] * cell
    scale = 1.0 / (1.0 + 2.0 * coupling)
    return -coupling * scale, scale


def local_visc(visc_ref, axis_name, cells):
    place = lax.axis_index(axis_name)
    return visc_ref[:, pl.ds(pl.multiple_of(place * cells, cells), cells)]


def rad_pre_kernel(cell_ref, visc_ref, oa_ref, ob_ref, edge_ref, *, axis_name):
    count = oa_ref.shape[0]
    cells = cell_ref.shape[2]
    visc = local_visc(visc_ref, axis_name, cells)
    cell = cell_ref[0]
    for v in range(count):
        side, _ = rad_side(cell, visc, v)
        side = side.T
        length = side.shape[0]
        il, iu, _, a_init, b_init = interior(side, side)
        ia, ib = pcr_levels(il, iu, [a_init, b_init])
        oa_ref[v, 0] = ia
        ob_ref[v, 0] = ib
        n2 = length - 2
        for k, value in enumerate((ia[1:2], ib[1:2], ia[n2 : n2 + 1], ib[n2 : n2 + 1])):
            edge_ref[v, 0, k : k + 1, :] = value


def rad_kernel(*refs, axis_name, devices, pieces):
    it_ref, ia_ref, ib_ref = refs[:3]
    red_in = refs[3 : 3 + pieces]
    mix_ref, cell_ref, visc_ref, edge_ref, ot_ref, red_ref, rows_ref, s3_ref = refs[3 + pieces :]
    count = it_ref.shape[0]
    half = it_ref.shape[2]
    step = pl.program_id(1)
    solved = []
    for w in range(count):
        first, last = reduced_ends(red_in, rows_ref, w)
        solved.append(
            back_substitute(it_ref[w, 0], ia_ref[w, 0], ib_ref[w, 0], first, last, step * half, s3_ref.shape[1])
        )
    for v, value in enumerate(mixed(mix_ref, solved)):
        s3_ref[v, pl.ds(pl.multiple_of(step * half, half), half), :] = value

    @pl.when(step == pl.num_programs(1) - 1)
    def _():
        rad_finish(s3_ref, cell_ref, visc_ref, edge_ref, ot_ref, red_ref, axis_name, devices)


def rad_finish(s3_ref, cell_ref, visc_ref, edge_ref, ot_ref, red_ref, axis_name, devices):
    count = s3_ref.shape[0]
    cells = s3_ref.shape[2]
    place = lax.axis_index(axis_name)
    visc = local_visc(visc_ref, axis_name, cells)
    section_three = [s3_ref[v] for v in range(count)]
    cell = cell_ref[0]
    for v in range(count):
        side, scale = rad_side(cell, visc, v)
        side = side.T
        target = (section_three[v] * scale).T
        length = side.shape[0]
        il, iu, keep, _, _ = interior(side, side)
        (it,) = pcr_levels(il, iu, [target * keep])
        edge = edge_ref[v, 0]
        n2 = length - 2
        (lf, le), (uf, ue), trow = interface_rows(
            side, side, target[0:1], target[length - 1 :], it[1:2], it[n2 : n2 + 1],
            edge[0:1], edge[1:2], edge[2:3], edge[3:4],
        )
        lf = jnp.where(place == 0, jnp.zeros_like(lf), lf)
        ue = jnp.where(place == devices - 1, jnp.zeros_like(ue), ue)
        store_rows(red_ref, v, ((lf, le), (uf, ue), trow))
        ot_ref[v, 0] = it


def out_kernel(*refs, pieces, length):
    it_ref, ia_ref, ib_ref = refs[:3]
    red_in = refs[3 : 3 + pieces]
    mix_ref, out_ref, rows_ref = refs[3 + pieces :]
    count = it_ref.shape[0]
    offset = pl.program_id(1) * it_ref.shape[2]
    solved = []
    for w in range(count):
        first, last = reduced_ends(red_in, rows_ref, w)
        solved.append(back_substitute(it_ref[w, 0], ia_ref[w, 0], ib_ref[w, 0], first, last, offset, length).T)
    for v, value in enumerate(mixed(mix_ref, solved)):
        out_ref[v, 0] = value


def az_sweep(flow_state, nb, source, cell_az, visc_az, beta_az, axial_diff, mix_in, order):
    nv, nz, na, nr = flow_state.shape
    chunk = 128 if nr % 128 == 0 else nr
    grid = (nz, nr // chunk)
    big = pl.BlockSpec((nv, 1, na, chunk), lambda z, c: (0, z, 0, c))
    cell = pl.BlockSpec((1, na, chunk), lambda z, c: (z, 0, c))
    par = pl.BlockSpec((nv, chunk), lambda z, c: (0, c))
    mixs = pl.BlockSpec((nv, nv, chunk), lambda z, c: (0, 0, c))
    edge = pl.BlockSpec((nv, 1, 10, chunk), lambda z, c: (0, z, 0, c))
    red = pl.BlockSpec((nv, 1, 3, 2, chunk), lambda z, c: (0, z, 0, 0, c))
    out = jax.ShapeDtypeStruct(flow_state.shape, flow_state.dtype)
    it, ia, ib, il, iu, scale, edges = pl.pallas_call(
        az_local_kernel,
        grid=grid,
        in_specs=[big, big, cell, par, par, par, mixs],
        out_specs=[big] * 6 + [edge],
        out_shape=[out] * 6 + [jax.ShapeDtypeStruct((nv, nz, 10, nr), flow_state.dtype)],
    )(flow_state, source, cell_az, visc_az, beta_az, axial_diff, mix_in)
    it, red = pl.pallas_call(
        az_plane_kernel,
        grid=grid,
        in_specs=[big, big, big, big, par, mixs, big, edge, pl.BlockSpec(memory_space=pl.ANY)],
        out_specs=[big, red],
        out_shape=[out, jax.ShapeDtypeStruct((nv, nz, 3, 2, nr), flow_state.dtype)],
        input_output_aliases={6: 0},
    )(nb, il, iu, scale, axial_diff, mix_in, it, edges, order)
    return it, ia, ib, red


def rad_pre(cell_rad, visc_rad, nv):
    nz, na, nr = cell_rad.shape
    big_t = pl.BlockSpec((nv, 1, nr, na), lambda z: (0, z, 0, 0))
    cell = pl.BlockSpec((1, na, nr), lambda z: (z, 0, 0))
    par = pl.BlockSpec(visc_rad.shape, lambda z: (0, 0))
    edge = pl.BlockSpec((nv, 1, 4, na), lambda z: (0, z, 0, 0))
    out = jax.ShapeDtypeStruct((nv, nz, nr, na), cell_rad.dtype)
    return pl.pallas_call(
        functools.partial(rad_pre_kernel, axis_name="rad"),
        grid=(nz,),
        in_specs=[cell, par],
        out_specs=[big_t, big_t, edge],
        out_shape=[out, out, jax.ShapeDtypeStruct((nv, nz, 4, na), cell_rad.dtype)],
    )(cell_rad, visc_rad)


def rad_sweep(it, ia, ib, red_in, mix_mid, cell_rad, visc_rad, edges):
    nv, nz, na, nr = it.shape
    halves = 4 if na % 32 == 0 else 1
    big = pl.BlockSpec((nv, 1, na // halves, nr), lambda z, c: (0, z, c, 0))
    big_t = pl.BlockSpec((nv, 1, nr, na), lambda z, c: (0, z, 0, 0))
    red_in_spec = pl.BlockSpec((nv, 1) + red_in[0].shape[2:], lambda z, c: (0, z, 0, 0, 0))
    mixs = pl.BlockSpec((nv, nv, nr), lambda z, c: (0, 0, 0))
    cell = pl.BlockSpec((1, na, nr), lambda z, c: (z, 0, 0))
    par = pl.BlockSpec(visc_rad.shape, lambda z, c: (0, 0))
    edge = pl.BlockSpec((nv, 1, 4, na), lambda z, c: (0, z, 0, 0))
    red = pl.BlockSpec((nv, 1, 3, 2, na), lambda z, c: (0, z, 0, 0, 0))
    out = jax.ShapeDtypeStruct((nv, nz, nr, na), it.dtype)
    pieces = len(red_in)
    kernel = functools.partial(rad_kernel, axis_name="rad", devices=lax.axis_size("rad"), pieces=pieces)
    return pl.pallas_call(
        kernel,
        grid=(nz, halves),
        in_specs=[big, big, big] + [red_in_spec] * pieces + [mixs, cell, par, edge],
        out_specs=[big_t, red],
        out_shape=[out, jax.ShapeDtypeStruct((nv, nz, 3, 2, na), it.dtype)],
        scratch_shapes=[pltpu.VMEM((3, 2 * pieces, nr), it.dtype), pltpu.VMEM((nv, na, nr), it.dtype)],
    )(it, ia, ib, *red_in, mix_mid, cell_rad, visc_rad, edges)


def out_sweep(it, ia, ib, red_in, mix_out):
    nv, nz, nr, na = it.shape
    chunk = 128 if nr % 128 == 0 else nr
    big_t = pl.BlockSpec((nv, 1, chunk, na), lambda z, c: (0, z, c, 0))
    big = pl.BlockSpec((nv, 1, na, chunk), lambda z, c: (0, z, 0, c))
    red_in_spec = pl.BlockSpec((nv, 1) + red_in[0].shape[2:], lambda z, c: (0, z, 0, 0, 0))
    mixs = pl.BlockSpec((nv, nv, chunk), lambda z, c: (0, 0, c))
    pieces = len(red_in)
    return pl.pallas_call(
        functools.partial(out_kernel, pieces=pieces, length=nr),
        grid=(nz, nr // chunk),
        in_specs=[big_t, big_t, big_t] + [red_in_spec] * pieces + [mixs],
        out_specs=big,
        out_shape=jax.ShapeDtypeStruct((nv, nz, na, nr), it.dtype),
        scratch_shapes=[pltpu.VMEM((3, 2 * pieces, na), it.dtype)],
    )(it, ia, ib, *red_in, mix_out)


def gathered(block, axis_name):
    count = lax.axis_size(axis_name)
    received = [block]
    for offset in range(1, count):
        pairs = [((i + offset) % count, i) for i in range(count)]
        received.append(lax.ppermute(block, axis_name, pairs))
    return received


def neighbour_planes(block, axis_name):
    count = lax.axis_size(axis_name)
    if count == 2:
        return lax.ppermute(block, axis_name, [(0, 1), (1, 0)])
    padded = with_halo(block, ((axis_name, 1),), 1, False)
    return padded[:, :-2] + padded[:, 2:]


def mix(matrix, values):
    mixed_rows = []
    for out_var in range(values.shape[0]):
        summed = values[out_var]
        for in_var in range(values.shape[0]):
            summed = summed + matrix[out_var, in_var][None, None, :] * values[in_var]
        mixed_rows.append(summed)
    return jnp.stack(mixed_rows)


def per_device(
    flow_state,
    source,
    cell_az,
    cell_rad,
    visc_az,
    beta_az,
    visc_rad,
    axial_diff,
    mix_in,
    mix_mid,
    mix_out,
):
    rad_cells = flow_state.shape[3]
    nb = neighbour_planes(flow_state, "ax")
    rad_a, rad_b, rad_edges = rad_pre(cell_rad, visc_rad, flow_state.shape[0])
    it, ia, ib, red = az_sweep(flow_state, nb, source, cell_az, visc_az, beta_az, axial_diff, mix_in, rad_edges)
    red = gathered(red, "az")
    it, red = rad_sweep(it, ia, ib, red, mix_mid, cell_rad, visc_rad, rad_edges)
    ia, ib = rad_a, rad_b
    red = gathered(red, "rad")
    return out_sweep(it, ia, ib, red, mix_out)


def solution(mesh):
    in_specs = (
        P(None, "ax", "az", "rad"),
        P(None, "ax", "az", "rad"),
        P("ax", "az", "rad"),
        P("ax", "az", "rad"),
        P(None, "rad"),
        P(None, "rad"),
        P(),
        P(None, "rad"),
        P(None, None, "rad"),
        P(None, None, "rad"),
        P(None, None, "rad"),
    )
    out_specs = P(None, "ax", "az", "rad")
    return jax.shard_map(
        per_device, mesh=mesh, in_specs=in_specs, out_specs=out_specs, check_vma=False
    )
```

```python
import jax
import jax.numpy as jnp
from jax import lax
from jax.experimental import pallas as pl
from jax.experimental.pallas import tpu as pltpu
from jax.sharding import PartitionSpec as P
import functools


def with_halo(block, sides, width, periodic):
    for axis, dim in sides:
        count = lax.axis_size(axis)
        forward = [(i, i + 1) for i in range(count - 1)]
        if periodic:
            forward.append((count - 1, 0))
        backward = [(target, source) for source, target in forward]
        low = lax.ppermute(
            lax.slice_in_dim(block, block.shape[dim] - width, None, axis=dim), axis, forward
        )
        high = lax.ppermute(lax.slice_in_dim(block, 0, width, axis=dim), axis, backward)
        block = jnp.concatenate([low, block, high], axis=dim)
    return block


def shifted(values, offset, axis, periodic):
    if periodic:
        return jnp.roll(values, offset, axis)
    length = values.shape[axis]
    zero_shape = list(values.shape)
    zero_shape[axis] = abs(offset)
    zeros = jnp.zeros(zero_shape, values.dtype)
    if offset > 0:
        kept = lax.slice_in_dim(values, 0, length - offset, axis=axis)
        return jnp.concatenate([zeros, kept], axis=axis)
    kept = lax.slice_in_dim(values, -offset, length, axis=axis)
    return jnp.concatenate([kept, zeros], axis=axis)


def cyclic_reduce(lower, upper, rhs, axis, periodic, steps_below):
    stride = 1
    while stride < steps_below:
        ll, ul = shifted(lower, stride, axis, periodic), shifted(upper, stride, axis, periodic)
        lr, ur = shifted(lower, -stride, axis, periodic), shifted(upper, -stride, axis, periodic)
        inv = 1.0 / (1.0 - lower * ul - upper * lr)
        rhs = [
            (r - lower * shifted(r, stride, axis, periodic) - upper * shifted(r, -stride, axis, periodic)) * inv
            for r in rhs
        ]
        lower, upper = -lower * ll * inv, -upper * ur * inv
        stride = stride * 2
    return lower, upper, rhs


def interior(lower, upper):
    length = lower.shape[0]
    idx = lax.broadcasted_iota(jnp.int32, lower.shape, 0)
    edge = (idx == 0) | (idx == length - 1)
    second = idx == 1
    penult = idx == length - 2
    zero = jnp.zeros_like(lower)
    il = jnp.where(edge | second, zero, lower)
    iu = jnp.where(edge | penult, zero, upper)
    return il, iu, jnp.where(edge, zero, 1.0), jnp.where(second, lower, zero), jnp.where(penult, upper, zero)


def pcr_levels(il, iu, rhs):
    length = il.shape[0]
    stride = 1
    while stride < length - 2:
        back = length - stride
        ll, ul = pltpu.roll(il, stride, 0), pltpu.roll(iu, stride, 0)
        lr, ur = pltpu.roll(il, back, 0), pltpu.roll(iu, back, 0)
        inv = 1.0 / (1.0 - il * ul - iu * lr)
        rhs = [(r - il * pltpu.roll(r, stride, 0) - iu * pltpu.roll(r, back, 0)) * inv for r in rhs]
        flip = -inv
        il, iu = il * ll * flip, iu * ur * flip
        stride = stride * 2
    return rhs


def interface_rows(lower, upper, t0, te, t1, t2, a1, b1, a2, b2):
    length = lower.shape[0]
    l0, u0 = lower[0:1], upper[0:1]
    le, ue = lower[length - 1 :], upper[length - 1 :]
    inv_f = 1.0 / (1.0 - u0 * a1)
    inv_e = 1.0 / (1.0 - le * b2)
    return (
        (l0 * inv_f, -le * a2 * inv_e),
        (-u0 * b1 * inv_f, ue * inv_e),
        ((t0 - u0 * t1) * inv_f, (te - le * t2) * inv_e),
    )


def reduce_block(lower, upper, target):
    length = lower.shape[0]
    il, iu, keep, a_init, b_init = interior(lower, upper)
    it, ia, ib = pcr_levels(il, iu, [target * keep, a_init, b_init])
    n2 = length - 2
    rows = interface_rows(
        lower, upper, target[0:1], target[length - 1 :], it[1:2], it[n2 : n2 + 1],
        ia[1:2], ib[1:2], ia[n2 : n2 + 1], ib[n2 : n2 + 1],
    )
    return it, ia, ib, rows


def store_rows(red_ref, v, rows):
    for q, pair in enumerate(rows):
        for i, value in enumerate(pair):
            red_ref[v, 0, q, i : i + 1, :] = value


def reduced_ends(red_refs, rows_ref, v):
    for k, ref in enumerate(red_refs):
        rows_ref[:, 2 * k : 2 * k + 2, :] = ref[v, 0]
    lower, upper, target = rows_ref[0], rows_ref[1], rows_ref[2]
    length = lower.shape[0]
    stride = 1
    while stride < length:
        back = length - stride
        ll, ul = pltpu.roll(lower, stride, 0), pltpu.roll(upper, stride, 0)
        lr, ur = pltpu.roll(lower, back, 0), pltpu.roll(upper, back, 0)
        inv = 1.0 / (1.0 - lower * ul - upper * lr)
        target = (target - lower * pltpu.roll(target, stride, 0) - upper * pltpu.roll(target, back, 0)) * inv
        lower, upper = -lower * ll * inv, -upper * ur * inv
        stride = stride * 2
    ends = target / (1.0 + lower + upper)
    return ends[0:1], ends[1:2]


def cached_ends(red_refs, rows_ref, ends_ref, w):
    @pl.when(pl.program_id(1) == 0)
    def _():
        first, last = reduced_ends(red_refs, rows_ref, w)
        ends_ref[w, 0:1, :] = first
        ends_ref[w, 1:2, :] = last

    return ends_ref[w, 0:1, :], ends_ref[w, 1:2, :]


def back_substitute(it, ia, ib, first, last, offset=0, length=None):
    length = it.shape[0] if length is None else length
    idx = lax.broadcasted_iota(jnp.int32, it.shape, 0) + offset
    inner = it - ia * first - ib * last
    return jnp.where(idx == 0, first, jnp.where(idx == length - 1, last, inner))


def mixed(mix_ref, values):
    out = []
    for v in range(len(values)):
        summed = values[v]
        for w in range(len(values)):
            summed = summed + mix_ref[v, w : w + 1, :] * values[w]
        out.append(summed)
    return out


def az_coefficients(cell, visc_ref, beta_ref, v):
    coupling = visc_ref[v : v + 1, :] * cell
    scale = -1.0 / (1.0 + 2.0 * coupling)
    tilt = beta_ref[v : v + 1, :]
    lower = coupling * (1.0 + tilt) * scale
    upper = coupling * (1.0 - tilt) * scale
    return lower, upper, scale


def az_local_kernel(fs_ref, src_ref, cell_ref, visc_ref, beta_ref, diff_ref, mix_ref, ot_ref, oa_ref, ob_ref, ol_ref, ou_ref, os_ref, edge_ref):
    count = fs_ref.shape[0]
    explicit = [src_ref[w, 0] + diff_ref[w : w + 1, :] * (-2.0 * fs_ref[w, 0]) for w in range(count)]
    section_one = mixed(mix_ref, explicit)
    cell = cell_ref[0]
    for v in range(count):
        lower, upper, scale = az_coefficients(cell, visc_ref, beta_ref, v)
        target = section_one[v] * -scale
        length = lower.shape[0]
        il, iu, keep, a_init, b_init = interior(lower, upper)
        ol_ref[v, 0] = il
        ou_ref[v, 0] = iu
        os_ref[v, 0] = -scale
        it, ia, ib = pcr_levels(il, iu, [target * keep, a_init, b_init])
        ot_ref[v, 0] = it
        oa_ref[v, 0] = ia
        ob_ref[v, 0] = ib
        n2 = length - 2
        for k, value in enumerate(
            (target[0:1], target[length - 1 :], ia[1:2], ib[1:2], ia[n2 : n2 + 1], ib[n2 : n2 + 1],
             lower[0:1], lower[length - 1 :], upper[0:1], upper[length - 1 :])
        ):
            edge_ref[v, 0, k : k + 1, :] = value


def az_plane_kernel(nb_ref, il_ref, iu_ref, sc_ref, diff_ref, mix_ref, it_in_ref, edge_ref, order_ref, ot_ref, red_ref):
    count = nb_ref.shape[0]
    explicit = [diff_ref[w : w + 1, :] * nb_ref[w, 0] for w in range(count)]
    section_one = mixed(mix_ref, explicit)
    for v in range(count):
        il, iu = il_ref[v, 0], iu_ref[v, 0]
        target = section_one[v] * sc_ref[v, 0]
        length = il.shape[0]
        _, _, keep, _, _ = interior(il, iu)
        (it,) = pcr_levels(il, iu, [target * keep])
        it = it_in_ref[v, 0] + it
        ot_ref[v, 0] = it
        edge = edge_ref[v, 0]
        n2 = length - 2
        rows = interface_rows(
            edge[6:8], edge[8:10], edge[0:1] + target[0:1], edge[1:2] + target[length - 1 :], it[1:2], it[n2 : n2 + 1],
            edge[2:3], edge[3:4], edge[4:5], edge[5:6],
        )
        store_rows(red_ref, v, rows)


def rad_side(cell, visc, v):
    coupling = visc[v : v + 1, :] * cell
    scale = 1.0 / (1.0 + 2.0 * coupling)
    return -coupling * scale, scale


def local_visc(visc_ref, axis_name, cells):
    place = lax.axis_index(axis_name)
    return visc_ref[:, pl.ds(pl.multiple_of(place * cells, cells), cells)]


def rad_pre_kernel(cell_ref, visc_ref, oa_ref, ob_ref, edge_ref, *, axis_name):
    count = oa_ref.shape[0]
    cells = cell_ref.shape[2]
    visc = local_visc(visc_ref, axis_name, cells)
    cell = cell_ref[0]
    for v in range(count):
        side, _ = rad_side(cell, visc, v)
        side = side.T
        length = side.shape[0]
        il, iu, _, a_init, b_init = interior(side, side)
        ia, ib = pcr_levels(il, iu, [a_init, b_init])
        oa_ref[v, 0] = ia
        ob_ref[v, 0] = ib
        n2 = length - 2
        for k, value in enumerate((ia[1:2], ib[1:2], ia[n2 : n2 + 1], ib[n2 : n2 + 1])):
            edge_ref[v, 0, k : k + 1, :] = value


def rad_kernel(*refs, axis_name, devices, pieces):
    it_ref, ia_ref, ib_ref = refs[:3]
    red_in = refs[3 : 3 + pieces]
    mix_ref, cell_ref, visc_ref, edge_ref, ot_ref, red_ref, rows_ref, s3_ref, ends_ref = refs[3 + pieces :]
    count = it_ref.shape[0]
    half = it_ref.shape[2]
    step = pl.program_id(1)
    solved = []
    for w in range(count):
        first, last = cached_ends(red_in, rows_ref, ends_ref, w)
        solved.append(
            back_substitute(it_ref[w, 0], ia_ref[w, 0], ib_ref[w, 0], first, last, step * half, s3_ref.shape[1])
        )
    for v, value in enumerate(mixed(mix_ref, solved)):
        s3_ref[v, pl.ds(pl.multiple_of(step * half, half), half), :] = value

    @pl.when(step == pl.num_programs(1) - 1)
    def _():
        rad_finish(s3_ref, cell_ref, visc_ref, edge_ref, ot_ref, red_ref, axis_name, devices)


def rad_finish(s3_ref, cell_ref, visc_ref, edge_ref, ot_ref, red_ref, axis_name, devices):
    count = s3_ref.shape[0]
    cells = s3_ref.shape[2]
    place = lax.axis_index(axis_name)
    visc = local_visc(visc_ref, axis_name, cells)
    section_three = [s3_ref[v] for v in range(count)]
    cell = cell_ref[0]
    for v in range(count):
        side, scale = rad_side(cell, visc, v)
        side = side.T
        target = (section_three[v] * scale).T
        length = side.shape[0]
        il, iu, keep, _, _ = interior(side, side)
        (it,) = pcr_levels(il, iu, [target * keep])
        edge = edge_ref[v, 0]
        n2 = length - 2
        (lf, le), (uf, ue), trow = interface_rows(
            side, side, target[0:1], target[length - 1 :], it[1:2], it[n2 : n2 + 1],
            edge[0:1], edge[1:2], edge[2:3], edge[3:4],
        )
        lf = jnp.where(place == 0, jnp.zeros_like(lf), lf)
        ue = jnp.where(place == devices - 1, jnp.zeros_like(ue), ue)
        store_rows(red_ref, v, ((lf, le), (uf, ue), trow))
        ot_ref[v, 0] = it


def out_kernel(*refs, pieces, length):
    it_ref, ia_ref, ib_ref = refs[:3]
    red_in = refs[3 : 3 + pieces]
    mix_ref, out_ref, rows_ref, ends_ref = refs[3 + pieces :]
    count = it_ref.shape[0]
    offset = pl.program_id(1) * it_ref.shape[2]
    solved = []
    for w in range(count):
        first, last = cached_ends(red_in, rows_ref, ends_ref, w)
        solved.append(back_substitute(it_ref[w, 0], ia_ref[w, 0], ib_ref[w, 0], first, last, offset, length).T)
    for v, value in enumerate(mixed(mix_ref, solved)):
        out_ref[v, 0] = value


def az_sweep(flow_state, nb, source, cell_az, visc_az, beta_az, axial_diff, mix_in, order):
    nv, nz, na, nr = flow_state.shape
    chunk = 128 if nr % 128 == 0 else nr
    grid = (nz, nr // chunk)
    big = pl.BlockSpec((nv, 1, na, chunk), lambda z, c: (0, z, 0, c))
    cell = pl.BlockSpec((1, na, chunk), lambda z, c: (z, 0, c))
    par = pl.BlockSpec((nv, chunk), lambda z, c: (0, c))
    mixs = pl.BlockSpec((nv, nv, chunk), lambda z, c: (0, 0, c))
    edge = pl.BlockSpec((nv, 1, 10, chunk), lambda z, c: (0, z, 0, c))
    red = pl.BlockSpec((nv, 1, 3, 2, chunk), lambda z, c: (0, z, 0, 0, c))
    out = jax.ShapeDtypeStruct(flow_state.shape, flow_state.dtype)
    it, ia, ib, il, iu, scale, edges = pl.pallas_call(
        az_local_kernel,
        grid=grid,
        in_specs=[big, big, cell, par, par, par, mixs],
        out_specs=[big] * 6 + [edge],
        out_shape=[out] * 6 + [jax.ShapeDtypeStruct((nv, nz, 10, nr), flow_state.dtype)],
    )(flow_state, source, cell_az, visc_az, beta_az, axial_diff, mix_in)
    it, red = pl.pallas_call(
        az_plane_kernel,
        grid=grid,
        in_specs=[big, big, big, big, par, mixs, big, edge, pl.BlockSpec(memory_space=pl.ANY)],
        out_specs=[big, red],
        out_shape=[out, jax.ShapeDtypeStruct((nv, nz, 3, 2, nr), flow_state.dtype)],
        input_output_aliases={6: 0},
    )(nb, il, iu, scale, axial_diff, mix_in, it, edges, order)
    return it, ia, ib, red


def rad_pre(cell_rad, visc_rad, nv):
    nz, na, nr = cell_rad.shape
    big_t = pl.BlockSpec((nv, 1, nr, na), lambda z: (0, z, 0, 0))
    cell = pl.BlockSpec((1, na, nr), lambda z: (z, 0, 0))
    par = pl.BlockSpec(visc_rad.shape, lambda z: (0, 0))
    edge = pl.BlockSpec((nv, 1, 4, na), lambda z: (0, z, 0, 0))
    out = jax.ShapeDtypeStruct((nv, nz, nr, na), cell_rad.dtype)
    return pl.pallas_call(
        functools.partial(rad_pre_kernel, axis_name="rad"),
        grid=(nz,),
        in_specs=[cell, par],
        out_specs=[big_t, big_t, edge],
        out_shape=[out, out, jax.ShapeDtypeStruct((nv, nz, 4, na), cell_rad.dtype)],
    )(cell_rad, visc_rad)


def rad_sweep(it, ia, ib, red_in, mix_mid, cell_rad, visc_rad, edges):
    nv, nz, na, nr = it.shape
    halves = 2 if na % 16 == 0 else 1
    big = pl.BlockSpec((nv, 1, na // halves, nr), lambda z, c: (0, z, c, 0))
    big_t = pl.BlockSpec((nv, 1, nr, na), lambda z, c: (0, z, 0, 0))
    red_in_spec = pl.BlockSpec((nv, 1) + red_in[0].shape[2:], lambda z, c: (0, z, 0, 0, 0))
    mixs = pl.BlockSpec((nv, nv, nr), lambda z, c: (0, 0, 0))
    cell = pl.BlockSpec((1, na, nr), lambda z, c: (z, 0, 0))
    par = pl.BlockSpec(visc_rad.shape, lambda z, c: (0, 0))
    edge = pl.BlockSpec((nv, 1, 4, na), lambda z, c: (0, z, 0, 0))
    red = pl.BlockSpec((nv, 1, 3, 2, na), lambda z, c: (0, z, 0, 0, 0))
    out = jax.ShapeDtypeStruct((nv, nz, nr, na), it.dtype)
    pieces = len(red_in)
    kernel = functools.partial(rad_kernel, axis_name="rad", devices=lax.axis_size("rad"), pieces=pieces)
    return pl.pallas_call(
        kernel,
        grid=(nz, halves),
        in_specs=[big, big, big] + [red_in_spec] * pieces + [mixs, cell, par, edge],
        out_specs=[big_t, red],
        out_shape=[out, jax.ShapeDtypeStruct((nv, nz, 3, 2, na), it.dtype)],
        scratch_shapes=[
            pltpu.VMEM((3, 2 * pieces, nr), it.dtype), pltpu.VMEM((nv, na, nr), it.dtype), pltpu.VMEM((nv, 2, nr), it.dtype)
        ],
    )(it, ia, ib, *red_in, mix_mid, cell_rad, visc_rad, edges)


def out_sweep(it, ia, ib, red_in, mix_out):
    nv, nz, nr, na = it.shape
    chunk = 128 if nr % 128 == 0 else nr
    big_t = pl.BlockSpec((nv, 1, chunk, na), lambda z, c: (0, z, c, 0))
    big = pl.BlockSpec((nv, 1, na, chunk), lambda z, c: (0, z, 0, c))
    red_in_spec = pl.BlockSpec((nv, 1) + red_in[0].shape[2:], lambda z, c: (0, z, 0, 0, 0))
    mixs = pl.BlockSpec((nv, nv, chunk), lambda z, c: (0, 0, c))
    pieces = len(red_in)
    return pl.pallas_call(
        functools.partial(out_kernel, pieces=pieces, length=nr),
        grid=(nz, nr // chunk),
        in_specs=[big_t, big_t, big_t] + [red_in_spec] * pieces + [mixs],
        out_specs=big,
        out_shape=jax.ShapeDtypeStruct((nv, nz, na, nr), it.dtype),
        scratch_shapes=[pltpu.VMEM((3, 2 * pieces, na), it.dtype), pltpu.VMEM((nv, 2, na), it.dtype)],
    )(it, ia, ib, *red_in, mix_out)


def gathered(block, axis_name):
    count = lax.axis_size(axis_name)
    received = [block]
    for offset in range(1, count):
        pairs = [((i + offset) % count, i) for i in range(count)]
        received.append(lax.ppermute(block, axis_name, pairs))
    return received


def neighbour_planes(block, axis_name):
    count = lax.axis_size(axis_name)
    if count == 2:
        return lax.ppermute(block, axis_name, [(0, 1), (1, 0)])
    padded = with_halo(block, ((axis_name, 1),), 1, False)
    return padded[:, :-2] + padded[:, 2:]


def mix(matrix, values):
    mixed_rows = []
    for out_var in range(values.shape[0]):
        summed = values[out_var]
        for in_var in range(values.shape[0]):
            summed = summed + matrix[out_var, in_var][None, None, :] * values[in_var]
        mixed_rows.append(summed)
    return jnp.stack(mixed_rows)


def per_device(
    flow_state,
    source,
    cell_az,
    cell_rad,
    visc_az,
    beta_az,
    visc_rad,
    axial_diff,
    mix_in,
    mix_mid,
    mix_out,
):
    rad_cells = flow_state.shape[3]
    nb = neighbour_planes(flow_state, "ax")
    rad_a, rad_b, rad_edges = rad_pre(cell_rad, visc_rad, flow_state.shape[0])
    it, ia, ib, red = az_sweep(flow_state, nb, source, cell_az, visc_az, beta_az, axial_diff, mix_in, rad_edges)
    red = gathered(red, "az")
    it, red = rad_sweep(it, ia, ib, red, mix_mid, cell_rad, visc_rad, rad_edges)
    ia, ib = rad_a, rad_b
    red = gathered(red, "rad")
    return out_sweep(it, ia, ib, red, mix_out)


def solution(mesh):
    in_specs = (
        P(None, "ax", "az", "rad"),
        P(None, "ax", "az", "rad"),
        P("ax", "az", "rad"),
        P("ax", "az", "rad"),
        P(None, "rad"),
        P(None, "rad"),
        P(),
        P(None, "rad"),
        P(None, None, "rad"),
        P(None, None, "rad"),
        P(None, None, "rad"),
    )
    out_specs = P(None, "ax", "az", "rad")
    return jax.shard_map(
        per_device, mesh=mesh, in_specs=in_specs, out_specs=out_specs, check_vma=False
    )
```

```python
import jax
import jax.numpy as jnp
from jax import lax
from jax.experimental import pallas as pl
from jax.experimental.pallas import tpu as pltpu
from jax.sharding import PartitionSpec as P
import functools


def with_halo(block, sides, width, periodic):
    for axis, dim in sides:
        count = lax.axis_size(axis)
        forward = [(i, i + 1) for i in range(count - 1)]
        if periodic:
            forward.append((count - 1, 0))
        backward = [(target, source) for source, target in forward]
        low = lax.ppermute(
            lax.slice_in_dim(block, block.shape[dim] - width, None, axis=dim), axis, forward
        )
        high = lax.ppermute(lax.slice_in_dim(block, 0, width, axis=dim), axis, backward)
        block = jnp.concatenate([low, block, high], axis=dim)
    return block


def shifted(values, offset, axis, periodic):
    if periodic:
        return jnp.roll(values, offset, axis)
    length = values.shape[axis]
    zero_shape = list(values.shape)
    zero_shape[axis] = abs(offset)
    zeros = jnp.zeros(zero_shape, values.dtype)
    if offset > 0:
        kept = lax.slice_in_dim(values, 0, length - offset, axis=axis)
        return jnp.concatenate([zeros, kept], axis=axis)
    kept = lax.slice_in_dim(values, -offset, length, axis=axis)
    return jnp.concatenate([kept, zeros], axis=axis)


def cyclic_reduce(lower, upper, rhs, axis, periodic, steps_below):
    stride = 1
    while stride < steps_below:
        ll, ul = shifted(lower, stride, axis, periodic), shifted(upper, stride, axis, periodic)
        lr, ur = shifted(lower, -stride, axis, periodic), shifted(upper, -stride, axis, periodic)
        inv = 1.0 / (1.0 - lower * ul - upper * lr)
        rhs = [
            (r - lower * shifted(r, stride, axis, periodic) - upper * shifted(r, -stride, axis, periodic)) * inv
            for r in rhs
        ]
        lower, upper = -lower * ll * inv, -upper * ur * inv
        stride = stride * 2
    return lower, upper, rhs


def interior(lower, upper):
    length = lower.shape[0]
    idx = lax.broadcasted_iota(jnp.int32, lower.shape, 0)
    edge = (idx == 0) | (idx == length - 1)
    second = idx == 1
    penult = idx == length - 2
    zero = jnp.zeros_like(lower)
    il = jnp.where(edge | second, zero, lower)
    iu = jnp.where(edge | penult, zero, upper)
    return il, iu, jnp.where(edge, zero, 1.0), jnp.where(second, lower, zero), jnp.where(penult, upper, zero)


def pcr_levels(il, iu, rhs):
    length = il.shape[0]
    stride = 1
    while stride < length - 2:
        back = length - stride
        ll, ul = pltpu.roll(il, stride, 0), pltpu.roll(iu, stride, 0)
        lr, ur = pltpu.roll(il, back, 0), pltpu.roll(iu, back, 0)
        inv = 1.0 / (1.0 - il * ul - iu * lr)
        rhs = [(r - il * pltpu.roll(r, stride, 0) - iu * pltpu.roll(r, back, 0)) * inv for r in rhs]
        flip = -inv
        il, iu = il * ll * flip, iu * ur * flip
        stride = stride * 2
    return rhs


def interface_rows(lower, upper, t0, te, t1, t2, a1, b1, a2, b2):
    length = lower.shape[0]
    l0, u0 = lower[0:1], upper[0:1]
    le, ue = lower[length - 1 :], upper[length - 1 :]
    inv_f = 1.0 / (1.0 - u0 * a1)
    inv_e = 1.0 / (1.0 - le * b2)
    return (
        (l0 * inv_f, -le * a2 * inv_e),
        (-u0 * b1 * inv_f, ue * inv_e),
        ((t0 - u0 * t1) * inv_f, (te - le * t2) * inv_e),
    )


def reduce_block(lower, upper, target):
    length = lower.shape[0]
    il, iu, keep, a_init, b_init = interior(lower, upper)
    it, ia, ib = pcr_levels(il, iu, [target * keep, a_init, b_init])
    n2 = length - 2
    rows = interface_rows(
        lower, upper, target[0:1], target[length - 1 :], it[1:2], it[n2 : n2 + 1],
        ia[1:2], ib[1:2], ia[n2 : n2 + 1], ib[n2 : n2 + 1],
    )
    return it, ia, ib, rows


def store_rows(red_ref, v, rows):
    for q, pair in enumerate(rows):
        for i, value in enumerate(pair):
            red_ref[v, 0, q, i : i + 1, :] = value


def reduced_ends(red_refs, rows_ref, v):
    for k, ref in enumerate(red_refs):
        rows_ref[:, 2 * k : 2 * k + 2, :] = ref[v, 0]
    lower, upper, target = rows_ref[0], rows_ref[1], rows_ref[2]
    length = lower.shape[0]
    stride = 1
    while stride < length:
        back = length - stride
        ll, ul = pltpu.roll(lower, stride, 0), pltpu.roll(upper, stride, 0)
        lr, ur = pltpu.roll(lower, back, 0), pltpu.roll(upper, back, 0)
        inv = 1.0 / (1.0 - lower * ul - upper * lr)
        target = (target - lower * pltpu.roll(target, stride, 0) - upper * pltpu.roll(target, back, 0)) * inv
        lower, upper = -lower * ll * inv, -upper * ur * inv
        stride = stride * 2
    ends = target / (1.0 + lower + upper)
    return ends[0:1], ends[1:2]


def back_substitute(it, ia, ib, first, last, offset=0, length=None):
    length = it.shape[0] if length is None else length
    idx = lax.broadcasted_iota(jnp.int32, it.shape, 0) + offset
    inner = it - ia * first - ib * last
    return jnp.where(idx == 0, first, jnp.where(idx == length - 1, last, inner))


def mixed(mix_ref, values):
    out = []
    for v in range(len(values)):
        summed = values[v]
        for w in range(len(values)):
            summed = summed + mix_ref[v, w : w + 1, :] * values[w]
        out.append(summed)
    return out


def az_coefficients(cell, visc_ref, beta_ref, v):
    coupling = visc_ref[v : v + 1, :] * cell
    scale = -1.0 / (1.0 + 2.0 * coupling)
    tilt = beta_ref[v : v + 1, :]
    lower = coupling * (1.0 + tilt) * scale
    upper = coupling * (1.0 - tilt) * scale
    return lower, upper, scale


def az_local_kernel(fs_ref, src_ref, cell_ref, visc_ref, beta_ref, diff_ref, mix_ref, ot_ref, oa_ref, ob_ref, ol_ref, ou_ref, os_ref, edge_ref):
    count = fs_ref.shape[0]
    explicit = [src_ref[w, 0] + diff_ref[w : w + 1, :] * (-2.0 * fs_ref[w, 0]) for w in range(count)]
    section_one = mixed(mix_ref, explicit)
    cell = cell_ref[0]
    for v in range(count):
        lower, upper, scale = az_coefficients(cell, visc_ref, beta_ref, v)
        target = section_one[v] * -scale
        length = lower.shape[0]
        il, iu, keep, a_init, b_init = interior(lower, upper)
        ol_ref[v, 0] = il
        ou_ref[v, 0] = iu
        os_ref[v, 0] = -scale
        it, ia, ib = pcr_levels(il, iu, [target * keep, a_init, b_init])
        ot_ref[v, 0] = it
        oa_ref[v, 0] = ia
        ob_ref[v, 0] = ib
        n2 = length - 2
        for k, value in enumerate(
            (target[0:1], target[length - 1 :], ia[1:2], ib[1:2], ia[n2 : n2 + 1], ib[n2 : n2 + 1],
             lower[0:1], lower[length - 1 :], upper[0:1], upper[length - 1 :])
        ):
            edge_ref[v, 0, k : k + 1, :] = value


def az_plane_kernel(nb_ref, il_ref, iu_ref, sc_ref, diff_ref, mix_ref, it_in_ref, edge_ref, order_ref, ot_ref, red_ref):
    count = nb_ref.shape[0]
    explicit = [diff_ref[w : w + 1, :] * nb_ref[w, 0] for w in range(count)]
    section_one = mixed(mix_ref, explicit)
    for v in range(count):
        il, iu = il_ref[v, 0], iu_ref[v, 0]
        target = section_one[v] * sc_ref[v, 0]
        length = il.shape[0]
        _, _, keep, _, _ = interior(il, iu)
        (it,) = pcr_levels(il, iu, [target * keep])
        it = it_in_ref[v, 0] + it
        ot_ref[v, 0] = it
        edge = edge_ref[v, 0]
        n2 = length - 2
        rows = interface_rows(
            edge[6:8], edge[8:10], edge[0:1] + target[0:1], edge[1:2] + target[length - 1 :], it[1:2], it[n2 : n2 + 1],
            edge[2:3], edge[3:4], edge[4:5], edge[5:6],
        )
        store_rows(red_ref, v, rows)


def rad_side(cell, visc, v):
    coupling = visc[v : v + 1, :] * cell
    scale = 1.0 / (1.0 + 2.0 * coupling)
    return -coupling * scale, scale


def local_visc(visc_ref, axis_name, cells):
    place = lax.axis_index(axis_name)
    return visc_ref[:, pl.ds(pl.multiple_of(place * cells, cells), cells)]


def rad_pre_kernel(cell_ref, visc_ref, oa_ref, ob_ref, edge_ref, *, axis_name):
    count = oa_ref.shape[0]
    cells = cell_ref.shape[2]
    visc = local_visc(visc_ref, axis_name, cells)
    cell = cell_ref[0]
    for v in range(count):
        side, _ = rad_side(cell, visc, v)
        side = side.T
        length = side.shape[0]
        il, iu, _, a_init, b_init = interior(side, side)
        ia, ib = pcr_levels(il, iu, [a_init, b_init])
        oa_ref[v, 0] = ia
        ob_ref[v, 0] = ib
        n2 = length - 2
        for k, value in enumerate((ia[1:2], ib[1:2], ia[n2 : n2 + 1], ib[n2 : n2 + 1])):
            edge_ref[v, 0, k : k + 1, :] = value


def rad_kernel(*refs, axis_name, devices, pieces):
    it_ref, ia_ref, ib_ref = refs[:3]
    red_in = refs[3 : 3 + pieces]
    mix_ref, cell_ref, visc_ref, edge_ref, ot_ref, red_ref, rows_ref, s3_ref = refs[3 + pieces :]
    count = it_ref.shape[0]
    half = it_ref.shape[2]
    step = pl.program_id(1)
    solved = []
    for w in range(count):
        first, last = reduced_ends(red_in, rows_ref, w)
        solved.append(
            back_substitute(it_ref[w, 0], ia_ref[w, 0], ib_ref[w, 0], first, last, step * half, s3_ref.shape[1])
        )
    for v, value in enumerate(mixed(mix_ref, solved)):
        s3_ref[v, pl.ds(pl.multiple_of(step * half, half), half), :] = value

    @pl.when(step == pl.num_programs(1) - 1)
    def _():
        rad_finish(s3_ref, cell_ref, visc_ref, edge_ref, ot_ref, red_ref, axis_name, devices)


def rad_finish(s3_ref, cell_ref, visc_ref, edge_ref, ot_ref, red_ref, axis_name, devices):
    count = s3_ref.shape[0]
    cells = s3_ref.shape[2]
    place = lax.axis_index(axis_name)
    visc = local_visc(visc_ref, axis_name, cells)
    section_three = [s3_ref[v] for v in range(count)]
    cell = cell_ref[0]
    for v in range(count):
        side, scale = rad_side(cell, visc, v)
        side = side.T
        target = (section_three[v] * scale).T
        length = side.shape[0]
        il, iu, keep, _, _ = interior(side, side)
        (it,) = pcr_levels(il, iu, [target * keep])
        edge = edge_ref[v, 0]
        n2 = length - 2
        (lf, le), (uf, ue), trow = interface_rows(
            side, side, target[0:1], target[length - 1 :], it[1:2], it[n2 : n2 + 1],
            edge[0:1], edge[1:2], edge[2:3], edge[3:4],
        )
        lf = jnp.where(place == 0, jnp.zeros_like(lf), lf)
        ue = jnp.where(place == devices - 1, jnp.zeros_like(ue), ue)
        store_rows(red_ref, v, ((lf, le), (uf, ue), trow))
        ot_ref[v, 0] = it


def out_kernel(*refs, pieces, length):
    it_ref, ia_ref, ib_ref = refs[:3]
    red_in = refs[3 : 3 + pieces]
    mix_ref, out_ref, rows_ref = refs[3 + pieces :]
    count = it_ref.shape[0]
    offset = pl.program_id(1) * it_ref.shape[2]
    solved = []
    for w in range(count):
        first, last = reduced_ends(red_in, rows_ref, w)
        solved.append(back_substitute(it_ref[w, 0], ia_ref[w, 0], ib_ref[w, 0], first, last, offset, length).T)
    for v, value in enumerate(mixed(mix_ref, solved)):
        out_ref[v, 0] = value


def az_sweep(flow_state, nb, source, cell_az, visc_az, beta_az, axial_diff, mix_in, order):
    nv, nz, na, nr = flow_state.shape
    chunk = nr
    grid = (nz, nr // chunk)
    big = pl.BlockSpec((nv, 1, na, chunk), lambda z, c: (0, z, 0, c))
    cell = pl.BlockSpec((1, na, chunk), lambda z, c: (z, 0, c))
    par = pl.BlockSpec((nv, chunk), lambda z, c: (0, c))
    mixs = pl.BlockSpec((nv, nv, chunk), lambda z, c: (0, 0, c))
    edge = pl.BlockSpec((nv, 1, 10, chunk), lambda z, c: (0, z, 0, c))
    red = pl.BlockSpec((nv, 1, 3, 2, chunk), lambda z, c: (0, z, 0, 0, c))
    out = jax.ShapeDtypeStruct(flow_state.shape, flow_state.dtype)
    it, ia, ib, il, iu, scale, edges = pl.pallas_call(
        az_local_kernel,
        grid=grid,
        in_specs=[big, big, cell, par, par, par, mixs],
        out_specs=[big] * 6 + [edge],
        out_shape=[out] * 6 + [jax.ShapeDtypeStruct((nv, nz, 10, nr), flow_state.dtype)],
    )(flow_state, source, cell_az, visc_az, beta_az, axial_diff, mix_in)
    it, red = pl.pallas_call(
        az_plane_kernel,
        grid=grid,
        in_specs=[big, big, big, big, par, mixs, big, edge, pl.BlockSpec(memory_space=pl.ANY)],
        out_specs=[big, red],
        out_shape=[out, jax.ShapeDtypeStruct((nv, nz, 3, 2, nr), flow_state.dtype)],
        input_output_aliases={6: 0},
    )(nb, il, iu, scale, axial_diff, mix_in, it, edges, order)
    return it, ia, ib, red


def rad_pre(cell_rad, visc_rad, nv):
    nz, na, nr = cell_rad.shape
    big_t = pl.BlockSpec((nv, 1, nr, na), lambda z: (0, z, 0, 0))
    cell = pl.BlockSpec((1, na, nr), lambda z: (z, 0, 0))
    par = pl.BlockSpec(visc_rad.shape, lambda z: (0, 0))
    edge = pl.BlockSpec((nv, 1, 4, na), lambda z: (0, z, 0, 0))
    out = jax.ShapeDtypeStruct((nv, nz, nr, na), cell_rad.dtype)
    return pl.pallas_call(
        functools.partial(rad_pre_kernel, axis_name="rad"),
        grid=(nz,),
        in_specs=[cell, par],
        out_specs=[big_t, big_t, edge],
        out_shape=[out, out, jax.ShapeDtypeStruct((nv, nz, 4, na), cell_rad.dtype)],
    )(cell_rad, visc_rad)


def rad_sweep(it, ia, ib, red_in, mix_mid, cell_rad, visc_rad, edges):
    nv, nz, na, nr = it.shape
    halves = 2 if na % 16 == 0 else 1
    big = pl.BlockSpec((nv, 1, na // halves, nr), lambda z, c: (0, z, c, 0))
    big_t = pl.BlockSpec((nv, 1, nr, na), lambda z, c: (0, z, 0, 0))
    red_in_spec = pl.BlockSpec((nv, 1) + red_in[0].shape[2:], lambda z, c: (0, z, 0, 0, 0))
    mixs = pl.BlockSpec((nv, nv, nr), lambda z, c: (0, 0, 0))
    cell = pl.BlockSpec((1, na, nr), lambda z, c: (z, 0, 0))
    par = pl.BlockSpec(visc_rad.shape, lambda z, c: (0, 0))
    edge = pl.BlockSpec((nv, 1, 4, na), lambda z, c: (0, z, 0, 0))
    red = pl.BlockSpec((nv, 1, 3, 2, na), lambda z, c: (0, z, 0, 0, 0))
    out = jax.ShapeDtypeStruct((nv, nz, nr, na), it.dtype)
    pieces = len(red_in)
    kernel = functools.partial(rad_kernel, axis_name="rad", devices=lax.axis_size("rad"), pieces=pieces)
    return pl.pallas_call(
        kernel,
        grid=(nz, halves),
        in_specs=[big, big, big] + [red_in_spec] * pieces + [mixs, cell, par, edge],
        out_specs=[big_t, red],
        out_shape=[out, jax.ShapeDtypeStruct((nv, nz, 3, 2, na), it.dtype)],
        scratch_shapes=[pltpu.VMEM((3, 2 * pieces, nr), it.dtype), pltpu.VMEM((nv, na, nr), it.dtype)],
    )(it, ia, ib, *red_in, mix_mid, cell_rad, visc_rad, edges)


def out_sweep(it, ia, ib, red_in, mix_out):
    nv, nz, nr, na = it.shape
    chunk = 128 if nr % 128 == 0 else nr
    big_t = pl.BlockSpec((nv, 1, chunk, na), lambda z, c: (0, z, c, 0))
    big = pl.BlockSpec((nv, 1, na, chunk), lambda z, c: (0, z, 0, c))
    red_in_spec = pl.BlockSpec((nv, 1) + red_in[0].shape[2:], lambda z, c: (0, z, 0, 0, 0))
    mixs = pl.BlockSpec((nv, nv, chunk), lambda z, c: (0, 0, c))
    pieces = len(red_in)
    return pl.pallas_call(
        functools.partial(out_kernel, pieces=pieces, length=nr),
        grid=(nz, nr // chunk),
        in_specs=[big_t, big_t, big_t] + [red_in_spec] * pieces + [mixs],
        out_specs=big,
        out_shape=jax.ShapeDtypeStruct((nv, nz, na, nr), it.dtype),
        scratch_shapes=[pltpu.VMEM((3, 2 * pieces, na), it.dtype)],
    )(it, ia, ib, *red_in, mix_out)


def gathered(block, axis_name):
    count = lax.axis_size(axis_name)
    received = [block]
    for offset in range(1, count):
        pairs = [((i + offset) % count, i) for i in range(count)]
        received.append(lax.ppermute(block, axis_name, pairs))
    return received


def neighbour_planes(block, axis_name):
    count = lax.axis_size(axis_name)
    if count == 2:
        return lax.ppermute(block, axis_name, [(0, 1), (1, 0)])
    padded = with_halo(block, ((axis_name, 1),), 1, False)
    return padded[:, :-2] + padded[:, 2:]


def mix(matrix, values):
    mixed_rows = []
    for out_var in range(values.shape[0]):
        summed = values[out_var]
        for in_var in range(values.shape[0]):
            summed = summed + matrix[out_var, in_var][None, None, :] * values[in_var]
        mixed_rows.append(summed)
    return jnp.stack(mixed_rows)


def per_device(
    flow_state,
    source,
    cell_az,
    cell_rad,
    visc_az,
    beta_az,
    visc_rad,
    axial_diff,
    mix_in,
    mix_mid,
    mix_out,
):
    rad_cells = flow_state.shape[3]
    nb = neighbour_planes(flow_state, "ax")
    rad_a, rad_b, rad_edges = rad_pre(cell_rad, visc_rad, flow_state.shape[0])
    it, ia, ib, red = az_sweep(flow_state, nb, source, cell_az, visc_az, beta_az, axial_diff, mix_in, rad_edges)
    red = gathered(red, "az")
    it, red = rad_sweep(it, ia, ib, red, mix_mid, cell_rad, visc_rad, rad_edges)
    ia, ib = rad_a, rad_b
    red = gathered(red, "rad")
    return out_sweep(it, ia, ib, red, mix_out)


def solution(mesh):
    in_specs = (
        P(None, "ax", "az", "rad"),
        P(None, "ax", "az", "rad"),
        P("ax", "az", "rad"),
        P("ax", "az", "rad"),
        P(None, "rad"),
        P(None, "rad"),
        P(),
        P(None, "rad"),
        P(None, None, "rad"),
        P(None, None, "rad"),
        P(None, None, "rad"),
    )
    out_specs = P(None, "ax", "az", "rad")
    return jax.shard_map(
        per_device, mesh=mesh, in_specs=in_specs, out_specs=out_specs, check_vma=False
    )
```
